128 devices in a mesh: tm: 8 (over z_lo, x), row: 16 (over z_hi, y, core).
Axes of the slice: x: 4, y: 4, z: 4 (z_hi: 2, z_lo: 2; z = z_hi * 2 + z_lo), core: 2. Of those that a mesh axis runs over, the one named last changes fastest.
Arguments:
- video_clip: bfloat16 [128, 128, 64, 128], P('tm', 'row'), may hold values from -6 to 6
- spatial_one: bfloat16 [3, 3, 144, 64], replicated, may hold values from -0.25 to 0.25
- temporal_one: bfloat16 [3, 64, 144], replicated, may hold values from -0.3125 to 0.3125
- down_weight: bfloat16 [3, 3, 128, 64], replicated, may hold values from -0.25 to 0.25
- spatial_two: bfloat16 [3, 3, 288, 128], replicated, may hold values from -0.1875 to 0.1875
- temporal_two: bfloat16 [3, 128, 288], replicated, may hold values from -0.21875 to 0.21875
Outputs:
- encoded: bfloat16 [128, 64, 64, 128], P('tm', 'row')
The draws below stay inside these ranges and needn't reach their ends.
All inputs are finite; a program needn't handle non-finite values.
Results may differ from the reference program's by a relative error of at most 0.0061.
Values may be sent and summed in bfloat16 or wider, within the bound.
No kernel may reach another device: no remote copies, remote signals or barrier semaphores. Data moves between devices by JAX's collectives and lax.ppermute only.
A program may use at most 64 MiB of HBM per device.

```python
import jax
import jax.numpy as jnp
from jax import lax

C1 = 64
M1 = 144
C2 = 128
M2 = 288
WIDTH = 128
FRAMES = 128
HEIGHT = 128


def levels(own_key, shape, split, low, largest):
    def one(position, parts):
        steps = jax.random.uniform(jax.random.fold_in(jax.random.fold_in(own_key, 6), position), (parts,), jnp.float32, low / len(split), largest / len(split))
        return jnp.repeat(jnp.exp(steps), shape[position] // parts).reshape((-1,) + (1,) * (len(shape) - position - 1))

    loudness = one(*split[0])
    for cut in split[1:]:
        loudness = loudness * one(*cut)
    return loudness


def scatter_about(own_key, dims, scale, most, split=(), held_as=jnp.bfloat16):
    drawn = jax.random.normal(own_key, dims, jnp.float32) * scale
    if len(split) > 0:
        drawn = levels(own_key, dims, split, -0.22, 0.18) * drawn
    return jnp.clip(drawn, min=-most, max=most).astype(held_as)


def setup_inputs(seed: int = 0) -> dict:
    arg_keys = jax.random.split(jax.random.key(seed), 7)
    return {
        "video_clip": scatter_about(arg_keys[0], (FRAMES, HEIGHT, C1, WIDTH), 1.0, 6.0, ((0, 8), (1, 16))),
        "spatial_one": scatter_about(arg_keys[1], (3, 3, M1, C1), (9 * C1) ** -0.5, 0.25),
        "temporal_one": scatter_about(arg_keys[2], (3, C1, M1), (3 * M1) ** -0.5, 0.3125),
        "down_weight": scatter_about(arg_keys[3], (3, 3, C2, C1), (9 * C1) ** -0.5, 0.25),
        "spatial_two": scatter_about(arg_keys[4], (3, 3, M2, C2), (9 * C2) ** -0.5, 0.1875),
        "temporal_two": scatter_about(arg_keys[5], (3, C2, M2), (3 * M2) ** -0.5, 0.21875),
    }


def spatial(source, kernel, layout, margin, strides):
    return lax.conv_general_dilated(source, kernel, strides, ((margin, margin), (1, 1)), dimension_numbers=(layout, "HWOI", layout), preferred_element_type=jnp.float32)


def temporal(source, kernel, layout, margin):
    return lax.conv_general_dilated(source, kernel[:, None], (1, 1), ((margin, margin), (0, 0)), dimension_numbers=(layout, "HWOI", layout), preferred_element_type=jnp.float32)


def reference(video_clip, spatial_one, temporal_one, down_weight, spatial_two, temporal_two):
    middle_one = jax.nn.relu(spatial(video_clip, spatial_one, "NHCW", 1, (1, 1))).astype(jnp.bfloat16)
    section_one = jax.nn.relu(video_clip.astype(jnp.float32) + temporal(middle_one, temporal_one, "HWCN", 1)).astype(jnp.bfloat16)
    reduced = lax.conv_general_dilated(section_one, down_weight, (2, 2), ((1, 1), (1, 1)), dimension_numbers=("NHCW", "HWOI", "NHWC"), preferred_element_type=jnp.float32)
    reduced = jax.nn.relu(reduced).astype(jnp.bfloat16)
    middle_two = jax.nn.relu(spatial(reduced, spatial_two, "NHWC", 1, (1, 1))).astype(jnp.bfloat16)
    encoded = jax.nn.relu(reduced.astype(jnp.float32) + temporal(middle_two, temporal_two, "HWNC", 1)).astype(jnp.bfloat16)
    return encoded
```

```python
import jax
import jax.numpy as jnp
from jax import lax
from jax.sharding import PartitionSpec as P


def from_offset(block, dt, dr):
    nt, nr = lax.axis_size("tm"), lax.axis_size("row")
    pairs = []
    for t in range(nt):
        for r in range(nr):
            if 0 <= t + dt < nt and 0 <= r + dr < nr:
                pairs.append(((t + dt) * nr + r + dr, t * nr + r))
    return lax.ppermute(block, ("tm", "row"), pairs)


def with_halo(block, top, bottom):
    frames, rows = block.shape[0], block.shape[1]
    frame_part = {-1: slice(frames - 1, frames), 0: slice(None), 1: slice(0, 1)}
    row_part = {-1: slice(rows - top, rows), 0: slice(None), 1: slice(0, bottom)}
    slabs = []
    for dt in (-1, 0, 1):
        pieces = []
        for dr in (-1, 0, 1):
            if dt == 0 and dr == 0:
                pieces.append(block)
            else:
                pieces.append(from_offset(block[frame_part[dt]][:, row_part[dr]], dt, dr))
        slabs.append(jnp.concatenate(pieces, axis=1))
    return jnp.concatenate(slabs, axis=0)


def spatial(source, kernel, layout):
    return lax.conv_general_dilated(
        source,
        kernel,
        (1, 1),
        ((0, 0), (1, 1)),
        dimension_numbers=(layout, "HWOI", layout),
        preferred_element_type=jnp.float32,
    )


def temporal(source, kernel, layout):
    return lax.conv_general_dilated(
        source,
        kernel[:, None],
        (1, 1),
        ((0, 0), (0, 0)),
        dimension_numbers=(layout, "HWOI", layout),
        preferred_element_type=jnp.float32,
    )


def residual_block(padded, top, spatial_kernel, temporal_kernel, space_layout, time_layout):
    framed = jax.nn.relu(spatial(padded, spatial_kernel, space_layout)).astype(jnp.bfloat16)
    inner = padded[1:-1, 1:-1]
    summed = inner.astype(jnp.float32) + temporal(framed, temporal_kernel, time_layout)
    return jax.nn.relu(summed).astype(jnp.bfloat16)


def on_device(video_clip, spatial_one, temporal_one, down_weight, spatial_two, temporal_two):
    padded = with_halo(video_clip, 2, 1)
    section_one = residual_block(padded, 2, spatial_one, temporal_one, "NHCW", "HWCN")
    first_device = lax.axis_index("row") == 0
    keep = jnp.logical_or(jnp.arange(section_one.shape[1]) > 0, jnp.logical_not(first_device))
    section_one = jnp.where(keep[None, :, None, None], section_one, jnp.zeros_like(section_one))
    reduced = lax.conv_general_dilated(
        section_one,
        down_weight,
        (2, 2),
        ((0, 0), (1, 1)),
        dimension_numbers=("NHCW", "HWOI", "NHWC"),
        preferred_element_type=jnp.float32,
    )
    reduced = jax.nn.relu(reduced).astype(jnp.bfloat16)
    padded_two = with_halo(reduced, 1, 1)
    return residual_block(padded_two, 1, spatial_two, temporal_two, "NHWC", "HWNC")


def solution(mesh):
    placed = (P("tm", "row", None, None), P(), P(), P(), P(), P())
    return jax.shard_map(
        on_device, mesh=mesh, in_specs=placed, out_specs=P("tm", "row", None, None), check_vma=False
    )
```

```python
import jax
import jax.numpy as jnp
from jax import lax
from jax.sharding import PartitionSpec as P


def from_neighbour(block, axis, by):
    n = lax.axis_size(axis)
    pairs = [(i + by, i) for i in range(n) if 0 <= i + by < n]
    return lax.ppermute(block, axis, pairs)


def spatial(source, kernel, layout):
    return lax.conv_general_dilated(
        source,
        kernel,
        (1, 1),
        ((0, 0), (1, 1)),
        dimension_numbers=(layout, "HWOI", layout),
        preferred_element_type=jnp.float32,
    )


def temporal(source, kernel, layout):
    return lax.conv_general_dilated(
        source,
        kernel[:, None],
        (1, 1),
        ((0, 0), (0, 0)),
        dimension_numbers=(layout, "HWOI", layout),
        preferred_element_type=jnp.float32,
    )


def residual_block(rowed, spatial_kernel, temporal_kernel, space_layout, time_layout):
    middle = jax.nn.relu(spatial(rowed, spatial_kernel, space_layout)).astype(jnp.bfloat16)
    frames = middle.shape[0]
    before = from_neighbour(middle[frames - 1 :], "tm", -1)
    after = from_neighbour(middle[:1], "tm", 1)
    inner = temporal(middle, temporal_kernel, time_layout)
    first = temporal(jnp.concatenate([before, middle[:2]], axis=0), temporal_kernel, time_layout)
    last = temporal(jnp.concatenate([middle[frames - 2 :], after], axis=0), temporal_kernel, time_layout)
    mixed = jnp.concatenate([first, inner, last], axis=0)
    summed = rowed[:, 1:-1].astype(jnp.float32) + mixed
    return jax.nn.relu(summed).astype(jnp.bfloat16)


def with_rows(block, top, bottom):
    rows = block.shape[1]
    above = from_neighbour(block[:, rows - top :], "row", -1)
    below = from_neighbour(block[:, :bottom], "row", 1)
    return jnp.concatenate([above, block, below], axis=1)


def on_device(video_clip, spatial_one, temporal_one, down_weight, spatial_two, temporal_two):
    section_one = residual_block(with_rows(video_clip, 2, 1), spatial_one, temporal_one, "NHCW", "HWCN")
    first_device = lax.axis_index("row") == 0
    keep = jnp.logical_or(jnp.arange(section_one.shape[1]) > 0, jnp.logical_not(first_device))
    section_one = jnp.where(keep[None, :, None, None], section_one, jnp.zeros_like(section_one))
    reduced = lax.conv_general_dilated(
        section_one,
        down_weight,
        (2, 2),
        ((0, 0), (1, 1)),
        dimension_numbers=("NHCW", "HWOI", "NHWC"),
        preferred_element_type=jnp.float32,
    )
    reduced = jax.nn.relu(reduced).astype(jnp.bfloat16)
    return residual_block(with_rows(reduced, 1, 1), spatial_two, temporal_two, "NHWC", "HWNC")


def solution(mesh):
    placed = (P("tm", "row", None, None), P(), P(), P(), P(), P())
    return jax.shard_map(
        on_device, mesh=mesh, in_specs=placed, out_specs=P("tm", "row", None, None), check_vma=False
    )
```

```python
import functools

import jax
import jax.numpy as jnp
from jax import lax
from jax.experimental import pallas as pl
from jax.experimental.pallas import tpu as pltpu
from jax.sharding import PartitionSpec as P


def padded_2(block, sides, width):
    for axis, dim in sides:
        count = lax.axis_size(axis)
        forward = [(i, i + 1) for i in range(count - 1)]
        backward = [(target, source) for source, target in forward]
        low = lax.ppermute(
            lax.slice_in_dim(block, block.shape[dim] - width, None, axis=dim), axis, forward
        )
        high = lax.ppermute(lax.slice_in_dim(block, 0, width, axis=dim), axis, backward)
        block = jnp.concatenate([low, block, high], axis=dim)
    return block


def from_behind(array, axis, by):
    devices = lax.axis_size(axis)
    pairs = [(i, i + by) for i in range(devices) if 0 <= i + by < devices]
    return lax.ppermute(array, axis, pairs)


def spatial(source, kernel, layout):
    return lax.conv_general_dilated(
        source,
        kernel,
        (1, 1),
        ((0, 0), (1, 1)),
        dimension_numbers=(layout, "HWOI", layout),
        preferred_element_type=jnp.float32,
    )


def temporal(source, kernel, layout):
    return lax.conv_general_dilated(
        source,
        kernel[:, None],
        (1, 1),
        ((0, 0), (0, 0)),
        dimension_numbers=(layout, "HWOI", layout),
        preferred_element_type=jnp.float32,
    )


def residual_block(source, spatial_kernel, temporal_kernel, space_layout, time_layout):
    padded = padded_2(source, (("tm", 0), ("row", 1)), 1)
    framed = jax.nn.relu(spatial(padded, spatial_kernel, space_layout)).astype(jnp.bfloat16)
    summed = source.astype(jnp.float32) + temporal(framed, temporal_kernel, time_layout)
    return jax.nn.relu(summed).astype(jnp.bfloat16)


def _lane_shift(x, by):
    width = x.shape[-1]
    rolled = pltpu.roll(x, (-by) % width, x.ndim - 1)
    lane = lax.broadcasted_iota(jnp.int32, x.shape, x.ndim - 1)
    inside = jnp.logical_and(lane + by >= 0, lane + by < width)
    return jnp.where(inside, rolled, jnp.zeros_like(rolled))


def _block_one_kernel(xp_ref, w9_ref, t3_ref, out_ref, mid_ref):
    frames_p, rows_p = xp_ref.shape[0], xp_ref.shape[1]
    rows = rows_p - 2
    frames = frames_p - 2

    def middle(f, carry):
        slab = xp_ref[f].astype(jnp.float32)
        shifted = [_lane_shift(slab, b - 1).astype(jnp.bfloat16) for b in range(3)]
        parts = []
        for a in range(3):
            for b in range(3):
                parts.append(jnp.concatenate([shifted[b][h + a] for h in range(rows)], axis=1))
        stacked = jnp.concatenate(parts, axis=0)
        m = jnp.dot(w9_ref[...], stacked, preferred_element_type=jnp.float32)
        m = jnp.maximum(m, 0.0).astype(jnp.bfloat16)
        width = out_ref.shape[-1]
        for h in range(rows):
            mid_ref[f, h] = m[:, h * width : (h + 1) * width]
        return carry

    lax.fori_loop(0, frames_p, middle, 0)

    def section(t, carry):
        width = out_ref.shape[-1]
        parts = []
        for k in range(3):
            parts.append(jnp.concatenate([mid_ref[t + k, h] for h in range(rows)], axis=1))
        stacked = jnp.concatenate(parts, axis=0)
        s = jnp.dot(t3_ref[...], stacked, preferred_element_type=jnp.float32)
        for h in range(rows):
            v = s[:, h * width : (h + 1) * width] + xp_ref[t + 1, h + 1].astype(jnp.float32)
            out_ref[t, h] = jnp.maximum(v, 0.0).astype(out_ref.dtype)
        return carry

    lax.fori_loop(0, frames, section, 0)


def block_one(padded, spatial_kernel, temporal_kernel):
    frames_p, rows_p, channels, width = padded.shape
    mids = spatial_kernel.shape[2]
    w9 = jnp.transpose(spatial_kernel, (2, 0, 1, 3)).reshape(mids, 9 * channels)
    t3 = jnp.transpose(temporal_kernel, (1, 0, 2)).reshape(channels, 3 * mids)
    vmem = pltpu.MemorySpace.VMEM if hasattr(pltpu, "MemorySpace") else pltpu.VMEM
    return pl.pallas_call(
        _block_one_kernel,
        out_shape=jax.ShapeDtypeStruct((frames_p - 2, rows_p - 2, channels, width), padded.dtype),
        in_specs=[pl.BlockSpec(memory_space=vmem)] * 3,
        out_specs=pl.BlockSpec(memory_space=vmem),
        scratch_shapes=[pltpu.VMEM((frames_p, rows_p - 2, mids, width), jnp.bfloat16)],
        compiler_params=pltpu.CompilerParams(vmem_limit_bytes=48 * 1024 * 1024),
    )(padded, w9, t3)


def on_device(video_clip, spatial_one, temporal_one, down_weight, spatial_two, temporal_two):
    padded = padded_2(video_clip, (("tm", 0), ("row", 1)), 1)
    section_one = block_one(padded, spatial_one, temporal_one)
    upper_row = from_behind(section_one[:, -1:], "row", 1)
    joined = jnp.concatenate([upper_row, section_one], axis=1)
    reduced = lax.conv_general_dilated(
        joined,
        down_weight,
        (2, 2),
        ((0, 0), (1, 1)),
        dimension_numbers=("NHCW", "HWOI", "NHWC"),
        preferred_element_type=jnp.float32,
    )
    reduced = jax.nn.relu(reduced).astype(jnp.bfloat16)
    return residual_block(reduced, spatial_two, temporal_two, "NHWC", "HWNC")


def solution(mesh):
    placed = (P("tm", "row", None, None), P(), P(), P(), P(), P())
    return jax.shard_map(
        on_device, mesh=mesh, in_specs=placed, out_specs=P("tm", "row", None, None), check_vma=False
    )
```

```python
import functools

import jax
import jax.numpy as jnp
from jax import lax
from jax.experimental import pallas as pl
from jax.experimental.pallas import tpu as pltpu
from jax.sharding import PartitionSpec as P


def padded_2(block, sides, width):
    for axis, dim in sides:
        count = lax.axis_size(axis)
        forward = [(i, i + 1) for i in range(count - 1)]
        backward = [(target, source) for source, target in forward]
        low = lax.ppermute(
            lax.slice_in_dim(block, block.shape[dim] - width, None, axis=dim), axis, forward
        )
        high = lax.ppermute(lax.slice_in_dim(block, 0, width, axis=dim), axis, backward)
        block = jnp.concatenate([low, block, high], axis=dim)
    return block


def from_behind(array, axis, by):
    devices = lax.axis_size(axis)
    pairs = [(i, i + by) for i in range(devices) if 0 <= i + by < devices]
    return lax.ppermute(array, axis, pairs)


def spatial(source, kernel, layout):
    return lax.conv_general_dilated(
        source,
        kernel,
        (1, 1),
        ((0, 0), (1, 1)),
        dimension_numbers=(layout, "HWOI", layout),
        preferred_element_type=jnp.float32,
    )


def temporal(source, kernel, layout):
    return lax.conv_general_dilated(
        source,
        kernel[:, None],
        (1, 1),
        ((0, 0), (0, 0)),
        dimension_numbers=(layout, "HWOI", layout),
        preferred_element_type=jnp.float32,
    )


def residual_block(source, spatial_kernel, temporal_kernel, space_layout, time_layout):
    padded = padded_2(source, (("tm", 0), ("row", 1)), 1)
    framed = jax.nn.relu(spatial(padded, spatial_kernel, space_layout)).astype(jnp.bfloat16)
    summed = source.astype(jnp.float32) + temporal(framed, temporal_kernel, time_layout)
    return jax.nn.relu(summed).astype(jnp.bfloat16)


def _lane_shift(x, by):
    width = x.shape[-1]
    rolled = pltpu.roll(x, (-by) % width, x.ndim - 1)
    lane = lax.broadcasted_iota(jnp.int32, x.shape, x.ndim - 1)
    inside = jnp.logical_and(lane + by >= 0, lane + by < width)
    return jnp.where(inside, rolled, jnp.zeros_like(rolled))


def _block_one_kernel(xp_ref, w9_ref, t3_ref, out_ref, mid_ref):
    frames_p, rows_p = xp_ref.shape[0], xp_ref.shape[1]
    rows = rows_p - 2
    frames = frames_p - 2

    def middle(f, carry):
        slab = xp_ref[f].astype(jnp.float32)
        shifted = [_lane_shift(slab, b - 1).astype(jnp.bfloat16) for b in range(3)]
        parts = []
        for a in range(3):
            for b in range(3):
                parts.append(jnp.concatenate([shifted[b][h + a] for h in range(rows)], axis=1))
        stacked = jnp.concatenate(parts, axis=0)
        m = jnp.dot(w9_ref[...], stacked, preferred_element_type=jnp.float32)
        m = jnp.maximum(m, 0.0).astype(jnp.bfloat16)
        width = out_ref.shape[-1]
        for h in range(rows):
            mid_ref[f, h] = m[:, h * width : (h + 1) * width]
        return carry

    lax.fori_loop(0, frames_p, middle, 0)

    def section(t, carry):
        width = out_ref.shape[-1]
        parts = []
        for k in range(3):
            parts.append(jnp.concatenate([mid_ref[t + k, h] for h in range(rows)], axis=1))
        stacked = jnp.concatenate(parts, axis=0)
        s = jnp.dot(t3_ref[...], stacked, preferred_element_type=jnp.float32)
        for h in range(rows):
            v = s[:, h * width : (h + 1) * width] + xp_ref[t + 1, h + 1].astype(jnp.float32)
            out_ref[t, h] = jnp.maximum(v, 0.0).astype(out_ref.dtype)
        return carry

    lax.fori_loop(0, frames, section, 0)


def block_one(padded, spatial_kernel, temporal_kernel):
    frames_p, rows_p, channels, width = padded.shape
    mids = spatial_kernel.shape[2]
    w9 = jnp.transpose(spatial_kernel, (2, 0, 1, 3)).reshape(mids, 9 * channels)
    t3 = jnp.transpose(temporal_kernel, (1, 0, 2)).reshape(channels, 3 * mids)
    vmem = pltpu.MemorySpace.VMEM if hasattr(pltpu, "MemorySpace") else pltpu.VMEM
    return pl.pallas_call(
        _block_one_kernel,
        out_shape=jax.ShapeDtypeStruct((frames_p - 2, rows_p - 2, channels, width), padded.dtype),
        in_specs=[pl.BlockSpec(memory_space=vmem)] * 3,
        out_specs=pl.BlockSpec(memory_space=vmem),
        scratch_shapes=[pltpu.VMEM((frames_p, rows_p - 2, mids, width), jnp.bfloat16)],
        compiler_params=pltpu.CompilerParams(vmem_limit_bytes=48 * 1024 * 1024),
    )(padded, w9, t3)


def _sublane_shift(x, by, axis):
    size = x.shape[axis]
    rolled = pltpu.roll(x, (-by) % size, axis)
    index = lax.broadcasted_iota(jnp.int32, x.shape, axis)
    inside = jnp.logical_and(index + by >= 0, index + by < size)
    return jnp.where(inside, rolled, jnp.zeros_like(rolled))


def _block_two_kernel(xp_ref, w9_ref, t3_ref, out_ref, mid_ref):
    frames_p, rows_p, width, channels = xp_ref.shape
    rows = rows_p - 2
    frames = frames_p - 2

    def middle(f, carry):
        slab = xp_ref[f].astype(jnp.float32)
        shifted = [_sublane_shift(slab, b - 1, 1).astype(jnp.bfloat16) for b in range(3)]
        stacked = jnp.concatenate(
            [
                jnp.concatenate([shifted[b][i + a] for a in range(3) for b in range(3)], axis=1)
                for i in range(rows)
            ],
            axis=0,
        )
        m = jnp.dot(stacked, w9_ref[...], preferred_element_type=jnp.float32)
        mid_ref[f] = jnp.maximum(m, 0.0).astype(jnp.bfloat16)
        return carry

    lax.fori_loop(0, frames_p, middle, 0)

    def section(t, carry):
        s = jnp.dot(mid_ref[t], t3_ref[0], preferred_element_type=jnp.float32)
        s = s + jnp.dot(mid_ref[t + 1], t3_ref[1], preferred_element_type=jnp.float32)
        s = s + jnp.dot(mid_ref[t + 2], t3_ref[2], preferred_element_type=jnp.float32)
        for i in range(rows):
            v = s[i * width : (i + 1) * width] + xp_ref[t + 1, i + 1].astype(jnp.float32)
            out_ref[t, i] = jnp.maximum(v, 0.0).astype(out_ref.dtype)
        return carry

    lax.fori_loop(0, frames, section, 0)


def block_two(padded, spatial_kernel, temporal_kernel):
    frames_p, rows_p, width, channels = padded.shape
    mids = spatial_kernel.shape[2]
    w9 = jnp.transpose(spatial_kernel, (0, 1, 3, 2)).reshape(9 * channels, mids)
    t3 = jnp.transpose(temporal_kernel, (0, 2, 1))
    vmem = pltpu.MemorySpace.VMEM if hasattr(pltpu, "MemorySpace") else pltpu.VMEM
    return pl.pallas_call(
        _block_two_kernel,
        out_shape=jax.ShapeDtypeStruct((frames_p - 2, rows_p - 2, width, channels), padded.dtype),
        in_specs=[pl.BlockSpec(memory_space=vmem)] * 3,
        out_specs=pl.BlockSpec(memory_space=vmem),
        scratch_shapes=[pltpu.VMEM((frames_p, (rows_p - 2) * width, mids), jnp.bfloat16)],
        compiler_params=pltpu.CompilerParams(vmem_limit_bytes=48 * 1024 * 1024),
    )(padded, w9, t3)


def on_device(video_clip, spatial_one, temporal_one, down_weight, spatial_two, temporal_two):
    padded = padded_2(video_clip, (("tm", 0), ("row", 1)), 1)
    section_one = block_one(padded, spatial_one, temporal_one)
    upper_row = from_behind(section_one[:, -1:], "row", 1)
    joined = jnp.concatenate([upper_row, section_one], axis=1)
    reduced = lax.conv_general_dilated(
        joined,
        down_weight,
        (2, 2),
        ((0, 0), (1, 1)),
        dimension_numbers=("NHCW", "HWOI", "NHWC"),
        preferred_element_type=jnp.float32,
    )
    reduced = jax.nn.relu(reduced).astype(jnp.bfloat16)
    padded_two = padded_2(reduced, (("tm", 0), ("row", 1)), 1)
    return block_two(padded_two, spatial_two, temporal_two)


def solution(mesh):
    placed = (P("tm", "row", None, None), P(), P(), P(), P(), P())
    return jax.shard_map(
        on_device, mesh=mesh, in_specs=placed, out_specs=P("tm", "row", None, None), check_vma=False
    )
```

```python
import functools

import jax
import jax.numpy as jnp
from jax import lax
from jax.experimental import pallas as pl
from jax.experimental.pallas import tpu as pltpu
from jax.sharding import PartitionSpec as P


def padded_2(block, sides, width):
    for axis, dim in sides:
        count = lax.axis_size(axis)
        forward = [(i, i + 1) for i in range(count - 1)]
        backward = [(target, source) for source, target in forward]
        low = lax.ppermute(
            lax.slice_in_dim(block, block.shape[dim] - width, None, axis=dim), axis, forward
        )
        high = lax.ppermute(lax.slice_in_dim(block, 0, width, axis=dim), axis, backward)
        block = jnp.concatenate([low, block, high], axis=dim)
    return block


def from_behind(array, axis, by):
    devices = lax.axis_size(axis)
    pairs = [(i, i + by) for i in range(devices) if 0 <= i + by < devices]
    return lax.ppermute(array, axis, pairs)


def spatial(source, kernel, layout):
    return lax.conv_general_dilated(
        source,
        kernel,
        (1, 1),
        ((0, 0), (1, 1)),
        dimension_numbers=(layout, "HWOI", layout),
        preferred_element_type=jnp.float32,
    )


def temporal(source, kernel, layout):
    return lax.conv_general_dilated(
        source,
        kernel[:, None],
        (1, 1),
        ((0, 0), (0, 0)),
        dimension_numbers=(layout, "HWOI", layout),
        preferred_element_type=jnp.float32,
    )


def residual_block(source, spatial_kernel, temporal_kernel, space_layout, time_layout):
    padded = padded_2(source, (("tm", 0), ("row", 1)), 1)
    framed = jax.nn.relu(spatial(padded, spatial_kernel, space_layout)).astype(jnp.bfloat16)
    summed = source.astype(jnp.float32) + temporal(framed, temporal_kernel, time_layout)
    return jax.nn.relu(summed).astype(jnp.bfloat16)


def _lane_shift(x, by):
    width = x.shape[-1]
    rolled = pltpu.roll(x, (-by) % width, x.ndim - 1)
    lane = lax.broadcasted_iota(jnp.int32, x.shape, x.ndim - 1)
    inside = jnp.logical_and(lane + by >= 0, lane + by < width)
    return jnp.where(inside, rolled, jnp.zeros_like(rolled))


def _block_one_kernel(keep_ref, xp_ref, w9_ref, t3_ref, wd_ref, out_ref, mid_ref):
    frames_p, rows_p, channels, width = xp_ref.shape
    rows = rows_p - 2
    frames = frames_p - 2
    reduced_rows = (rows - 1) // 2

    def middle(f, carry):
        slab = xp_ref[f].astype(jnp.float32)
        shifted = [_lane_shift(slab, b - 1).astype(jnp.bfloat16) for b in range(3)]
        parts = []
        for a in range(3):
            for b in range(3):
                parts.append(jnp.concatenate([shifted[b][h + a] for h in range(rows)], axis=1))
        stacked = jnp.concatenate(parts, axis=0)
        m = jnp.dot(w9_ref[...], stacked, preferred_element_type=jnp.float32)
        m = jnp.maximum(m, 0.0).astype(jnp.bfloat16)
        for h in range(rows):
            mid_ref[f, h] = m[:, h * width : (h + 1) * width]
        return carry

    lax.fori_loop(0, frames_p, middle, 0)

    lane = lax.broadcasted_iota(jnp.int32, (width // 2, width), 1)
    column = lax.broadcasted_iota(jnp.int32, (width // 2, width), 0)
    pick = (lane == 2 * column).astype(jnp.bfloat16)
    keep_first = keep_ref[0].astype(jnp.float32)

    def section(t, carry):
        parts = []
        for k in range(3):
            parts.append(jnp.concatenate([mid_ref[t + k, h] for h in range(rows)], axis=1))
        stacked = jnp.concatenate(parts, axis=0)
        s = jnp.dot(t3_ref[...], stacked, preferred_element_type=jnp.float32)
        sec = []
        for h in range(rows):
            v = s[:, h * width : (h + 1) * width] + xp_ref[t + 1, h + 1].astype(jnp.float32)
            v = jnp.maximum(v, 0.0)
            if h == 0:
                v = v * keep_first
            sec.append(v.astype(jnp.bfloat16).astype(jnp.float32))
        shifted = [[_lane_shift(r, b - 1).astype(jnp.bfloat16) for b in range(3)] for r in sec]
        parts = []
        for a in range(3):
            for b in range(3):
                parts.append(
                    jnp.concatenate([shifted[2 * i + a][b] for i in range(reduced_rows)], axis=1)
                )
        stacked = jnp.concatenate(parts, axis=0)
        full = jnp.dot(wd_ref[...], stacked, preferred_element_type=jnp.float32)
        full = jnp.maximum(full, 0.0).astype(jnp.bfloat16)
        for i in range(reduced_rows):
            r = lax.dot_general(
                pick,
                full[:, i * width : (i + 1) * width],
                (((1,), (1,)), ((), ())),
                preferred_element_type=jnp.float32,
            )
            out_ref[t, i] = r.astype(out_ref.dtype)
        return carry

    lax.fori_loop(0, frames, section, 0)


def block_one(padded, keep_first, spatial_kernel, temporal_kernel, down_kernel):
    frames_p, rows_p, channels, width = padded.shape
    mids = spatial_kernel.shape[2]
    outs = down_kernel.shape[2]
    w9 = jnp.transpose(spatial_kernel, (2, 0, 1, 3)).reshape(mids, 9 * channels)
    t3 = jnp.transpose(temporal_kernel, (1, 0, 2)).reshape(channels, 3 * mids)
    wd = jnp.transpose(down_kernel, (2, 0, 1, 3)).reshape(outs, 9 * channels)
    vmem = pltpu.MemorySpace.VMEM if hasattr(pltpu, "MemorySpace") else pltpu.VMEM
    smem = pltpu.MemorySpace.SMEM if hasattr(pltpu, "MemorySpace") else pltpu.SMEM
    reduced_rows = (rows_p - 3) // 2
    return pl.pallas_call(
        _block_one_kernel,
        out_shape=jax.ShapeDtypeStruct((frames_p - 2, reduced_rows, width // 2, outs), padded.dtype),
        in_specs=[pl.BlockSpec(memory_space=smem)] + [pl.BlockSpec(memory_space=vmem)] * 4,
        out_specs=pl.BlockSpec(memory_space=vmem),
        scratch_shapes=[pltpu.VMEM((frames_p, rows_p - 2, mids, width), jnp.bfloat16)],
        compiler_params=pltpu.CompilerParams(vmem_limit_bytes=48 * 1024 * 1024),
    )(keep_first, padded, w9, t3, wd)


def with_halo_one(block):
    frames, rows = block.shape[0], block.shape[1]
    before = from_behind(block[frames - 1 :], "tm", 1)
    after = from_behind(block[:1], "tm", -1)
    block = jnp.concatenate([before, block, after], axis=0)
    above = from_behind(block[:, rows - 2 :], "row", 1)
    below = from_behind(block[:, :1], "row", -1)
    return jnp.concatenate([above, block, below], axis=1)


def _sublane_shift(x, by, axis):
    size = x.shape[axis]
    rolled = pltpu.roll(x, (-by) % size, axis)
    index = lax.broadcasted_iota(jnp.int32, x.shape, axis)
    inside = jnp.logical_and(index + by >= 0, index + by < size)
    return jnp.where(inside, rolled, jnp.zeros_like(rolled))


def _block_two_kernel(xp_ref, w9_ref, t3_ref, out_ref, mid_ref):
    frames_p, rows_p, width, channels = xp_ref.shape
    rows = rows_p - 2
    frames = frames_p - 2

    def middle(f, carry):
        slab = xp_ref[f].astype(jnp.float32)
        shifted = [_sublane_shift(slab, b - 1, 1).astype(jnp.bfloat16) for b in range(3)]
        stacked = jnp.concatenate(
            [
                jnp.concatenate([shifted[b][i + a] for a in range(3) for b in range(3)], axis=1)
                for i in range(rows)
            ],
            axis=0,
        )
        m = jnp.dot(stacked, w9_ref[...], preferred_element_type=jnp.float32)
        mid_ref[f] = jnp.maximum(m, 0.0).astype(jnp.bfloat16)
        return carry

    lax.fori_loop(0, frames_p, middle, 0)

    def section(t, carry):
        s = jnp.dot(mid_ref[t], t3_ref[0], preferred_element_type=jnp.float32)
        s = s + jnp.dot(mid_ref[t + 1], t3_ref[1], preferred_element_type=jnp.float32)
        s = s + jnp.dot(mid_ref[t + 2], t3_ref[2], preferred_element_type=jnp.float32)
        for i in range(rows):
            v = s[i * width : (i + 1) * width] + xp_ref[t + 1, i + 1].astype(jnp.float32)
            out_ref[t, i] = jnp.maximum(v, 0.0).astype(out_ref.dtype)
        return carry

    lax.fori_loop(0, frames, section, 0)


def block_two(padded, spatial_kernel, temporal_kernel):
    frames_p, rows_p, width, channels = padded.shape
    mids = spatial_kernel.shape[2]
    w9 = jnp.transpose(spatial_kernel, (0, 1, 3, 2)).reshape(9 * channels, mids)
    t3 = jnp.transpose(temporal_kernel, (0, 2, 1))
    vmem = pltpu.MemorySpace.VMEM if hasattr(pltpu, "MemorySpace") else pltpu.VMEM
    return pl.pallas_call(
        _block_two_kernel,
        out_shape=jax.ShapeDtypeStruct((frames_p - 2, rows_p - 2, width, channels), padded.dtype),
        in_specs=[pl.BlockSpec(memory_space=vmem)] * 3,
        out_specs=pl.BlockSpec(memory_space=vmem),
        scratch_shapes=[pltpu.VMEM((frames_p, (rows_p - 2) * width, mids), jnp.bfloat16)],
        compiler_params=pltpu.CompilerParams(vmem_limit_bytes=48 * 1024 * 1024),
    )(padded, w9, t3)


def on_device(video_clip, spatial_one, temporal_one, down_weight, spatial_two, temporal_two):
    padded = with_halo_one(video_clip)
    keep_first = (lax.axis_index("row") > 0).astype(jnp.int32).reshape(1)
    reduced = block_one(padded, keep_first, spatial_one, temporal_one, down_weight)
    padded_two = padded_2(reduced, (("tm", 0), ("row", 1)), 1)
    return block_two(padded_two, spatial_two, temporal_two)


def solution(mesh):
    placed = (P("tm", "row", None, None), P(), P(), P(), P(), P())
    return jax.shard_map(
        on_device, mesh=mesh, in_specs=placed, out_specs=P("tm", "row", None, None), check_vma=False
    )
```

```python
import functools

import jax
import jax.numpy as jnp
from jax import lax
from jax.experimental import pallas as pl
from jax.experimental.pallas import tpu as pltpu
from jax.sharding import PartitionSpec as P


def padded_2(block, sides, width):
    for axis, dim in sides:
        count = lax.axis_size(axis)
        forward = [(i, i + 1) for i in range(count - 1)]
        backward = [(target, source) for source, target in forward]
        low = lax.ppermute(
            lax.slice_in_dim(block, block.shape[dim] - width, None, axis=dim), axis, forward
        )
        high = lax.ppermute(lax.slice_in_dim(block, 0, width, axis=dim), axis, backward)
        block = jnp.concatenate([low, block, high], axis=dim)
    return block


def from_behind(array, axis, by):
    devices = lax.axis_size(axis)
    pairs = [(i, i + by) for i in range(devices) if 0 <= i + by < devices]
    return lax.ppermute(array, axis, pairs)


def spatial(source, kernel, layout):
    return lax.conv_general_dilated(
        source,
        kernel,
        (1, 1),
        ((0, 0), (1, 1)),
        dimension_numbers=(layout, "HWOI", layout),
        preferred_element_type=jnp.float32,
    )


def temporal(source, kernel, layout):
    return lax.conv_general_dilated(
        source,
        kernel[:, None],
        (1, 1),
        ((0, 0), (0, 0)),
        dimension_numbers=(layout, "HWOI", layout),
        preferred_element_type=jnp.float32,
    )


def residual_block(source, spatial_kernel, temporal_kernel, space_layout, time_layout):
    padded = padded_2(source, (("tm", 0), ("row", 1)), 1)
    framed = jax.nn.relu(spatial(padded, spatial_kernel, space_layout)).astype(jnp.bfloat16)
    summed = source.astype(jnp.float32) + temporal(framed, temporal_kernel, time_layout)
    return jax.nn.relu(summed).astype(jnp.bfloat16)


def _lane_shift(x, by):
    width = x.shape[-1]
    rolled = pltpu.roll(x, (-by) % width, x.ndim - 1)
    lane = lax.broadcasted_iota(jnp.int32, x.shape, x.ndim - 1)
    inside = jnp.logical_and(lane + by >= 0, lane + by < width)
    return jnp.where(inside, rolled, jnp.zeros_like(rolled))


def _block_one_kernel(keep_ref, xp_ref, w9_ref, t3_ref, wd_ref, out_ref, mid_ref):
    frames_p, rows_p, channels, width = xp_ref.shape
    rows = rows_p - 2
    frames = frames_p - 2
    reduced_rows = (rows - 1) // 2

    def middle(f, carry):
        slab = xp_ref[f].astype(jnp.float32)
        shifted = [_lane_shift(slab, b - 1).astype(jnp.bfloat16) for b in range(3)]
        parts = []
        for a in range(3):
            for b in range(3):
                parts.append(jnp.concatenate([shifted[b][h + a] for h in range(rows)], axis=1))
        stacked = jnp.concatenate(parts, axis=0)
        m = jnp.dot(w9_ref[...], stacked, preferred_element_type=jnp.float32)
        m = jnp.maximum(m, 0.0).astype(jnp.bfloat16)
        for h in range(rows):
            mid_ref[f, h] = m[:, h * width : (h + 1) * width]
        return carry

    lax.fori_loop(0, frames_p, middle, 0)

    lane = lax.broadcasted_iota(jnp.int32, (width // 2, width), 1)
    column = lax.broadcasted_iota(jnp.int32, (width // 2, width), 0)
    pick = (lane == 2 * column).astype(jnp.bfloat16)
    keep_first = keep_ref[0].astype(jnp.float32)

    def section(t, carry):
        parts = []
        for k in range(3):
            parts.append(jnp.concatenate([mid_ref[t + k, h] for h in range(rows)], axis=1))
        stacked = jnp.concatenate(parts, axis=0)
        s = jnp.dot(t3_ref[...], stacked, preferred_element_type=jnp.float32)
        sec = []
        for h in range(rows):
            v = s[:, h * width : (h + 1) * width] + xp_ref[t + 1, h + 1].astype(jnp.float32)
            v = jnp.maximum(v, 0.0)
            if h == 0:
                v = v * keep_first
            sec.append(v.astype(jnp.bfloat16).astype(jnp.float32))
        shifted = [[_lane_shift(r, b - 1).astype(jnp.bfloat16) for b in range(3)] for r in sec]
        parts = []
        for a in range(3):
            for b in range(3):
                parts.append(
                    jnp.concatenate([shifted[2 * i + a][b] for i in range(reduced_rows)], axis=1)
                )
        stacked = jnp.concatenate(parts, axis=0)
        full = jnp.dot(wd_ref[...], stacked, preferred_element_type=jnp.float32)
        full = jnp.maximum(full, 0.0).astype(jnp.bfloat16)
        for i in range(reduced_rows):
            r = lax.dot_general(
                pick,
                full[:, i * width : (i + 1) * width],
                (((1,), (1,)), ((), ())),
                preferred_element_type=jnp.float32,
            )
            out_ref[t, i] = r.astype(out_ref.dtype)
        return carry

    lax.fori_loop(0, frames, section, 0)


def block_one(padded, keep_first, spatial_kernel, temporal_kernel, down_kernel):
    frames_p, rows_p, channels, width = padded.shape
    mids = spatial_kernel.shape[2]
    outs = down_kernel.shape[2]
    w9 = jnp.transpose(spatial_kernel, (2, 0, 1, 3)).reshape(mids, 9 * channels)
    t3 = jnp.transpose(temporal_kernel, (1, 0, 2)).reshape(channels, 3 * mids)
    wd = jnp.transpose(down_kernel, (2, 0, 1, 3)).reshape(outs, 9 * channels)
    vmem = pltpu.MemorySpace.VMEM if hasattr(pltpu, "MemorySpace") else pltpu.VMEM
    smem = pltpu.MemorySpace.SMEM if hasattr(pltpu, "MemorySpace") else pltpu.SMEM
    reduced_rows = (rows_p - 3) // 2
    return pl.pallas_call(
        _block_one_kernel,
        out_shape=jax.ShapeDtypeStruct((frames_p - 2, reduced_rows, width // 2, outs), padded.dtype),
        in_specs=[pl.BlockSpec(memory_space=smem)] + [pl.BlockSpec(memory_space=vmem)] * 4,
        out_specs=pl.BlockSpec(memory_space=vmem),
        scratch_shapes=[pltpu.VMEM((frames_p, rows_p - 2, mids, width), jnp.bfloat16)],
        compiler_params=pltpu.CompilerParams(vmem_limit_bytes=48 * 1024 * 1024),
    )(keep_first, padded, w9, t3, wd)


def with_halo_one(block):
    frames, rows = block.shape[0], block.shape[1]
    before = from_behind(block[frames - 1 :], "tm", 1)
    after = from_behind(block[:1], "tm", -1)
    block = jnp.concatenate([before, block, after], axis=0)
    above = from_behind(block[:, rows - 2 :], "row", 1)
    below = from_behind(block[:, :1], "row", -1)
    return jnp.concatenate([above, block, below], axis=1)


def _sublane_shift(x, by, axis):
    size = x.shape[axis]
    rolled = pltpu.roll(x, (-by) % size, axis)
    index = lax.broadcasted_iota(jnp.int32, x.shape, axis)
    inside = jnp.logical_and(index + by >= 0, index + by < size)
    return jnp.where(inside, rolled, jnp.zeros_like(rolled))


def _middle_two(xp_ref, f, w9_ref):
    rows = xp_ref.shape[1] - 2
    slab = xp_ref[f].astype(jnp.float32)
    shifted = [_sublane_shift(slab, b - 1, 1).astype(jnp.bfloat16) for b in range(3)]
    stacked = jnp.concatenate(
        [
            jnp.concatenate([shifted[b][i + a] for a in range(3) for b in range(3)], axis=1)
            for i in range(rows)
        ],
        axis=0,
    )
    m = jnp.dot(stacked, w9_ref[...], preferred_element_type=jnp.float32)
    return jnp.maximum(m, 0.0).astype(jnp.bfloat16)


def _edges_two_kernel(xp_ref, w9_ref, edge_ref):
    frames = xp_ref.shape[0]
    edge_ref[0] = _middle_two(xp_ref, 0, w9_ref)
    edge_ref[1] = _middle_two(xp_ref, frames - 1, w9_ref)


def _finish(s, xp_ref, t, out_ref, slot):
    rows, width = xp_ref.shape[1] - 2, xp_ref.shape[2]
    for i in range(rows):
        v = s[i * width : (i + 1) * width] + xp_ref[t, i + 1].astype(jnp.float32)
        out_ref[slot, i] = jnp.maximum(v, 0.0).astype(out_ref.dtype)


def _inner_two_kernel(xp_ref, w9_ref, t3_ref, out_ref, side_ref, mid_ref):
    frames = xp_ref.shape[0]

    def middle(f, carry):
        mid_ref[f] = _middle_two(xp_ref, f, w9_ref)
        return carry

    lax.fori_loop(0, frames, middle, 0)
    side_ref[0] = mid_ref[1]
    side_ref[1] = mid_ref[frames - 2]

    def section(t, carry):
        s = jnp.dot(mid_ref[t - 1], t3_ref[0], preferred_element_type=jnp.float32)
        s = s + jnp.dot(mid_ref[t], t3_ref[1], preferred_element_type=jnp.float32)
        s = s + jnp.dot(mid_ref[t + 1], t3_ref[2], preferred_element_type=jnp.float32)
        _finish(s, xp_ref, t, out_ref, t - 1)
        return carry

    lax.fori_loop(1, frames - 1, section, 0)


def _outer_two_kernel(xp_ref, t3_ref, before_ref, after_ref, edge_ref, side_ref, out_ref):
    frames = xp_ref.shape[0]
    s = jnp.dot(before_ref[0], t3_ref[0], preferred_element_type=jnp.float32)
    s = s + jnp.dot(edge_ref[0], t3_ref[1], preferred_element_type=jnp.float32)
    s = s + jnp.dot(side_ref[0], t3_ref[2], preferred_element_type=jnp.float32)
    _finish(s, xp_ref, 0, out_ref, 0)
    s = jnp.dot(side_ref[1], t3_ref[0], preferred_element_type=jnp.float32)
    s = s + jnp.dot(edge_ref[1], t3_ref[1], preferred_element_type=jnp.float32)
    s = s + jnp.dot(after_ref[0], t3_ref[2], preferred_element_type=jnp.float32)
    _finish(s, xp_ref, frames - 1, out_ref, 1)


def block_two(rowed, spatial_kernel, temporal_kernel):
    frames, rows_p, width, channels = rowed.shape
    rows = rows_p - 2
    mids = spatial_kernel.shape[2]
    w9 = jnp.transpose(spatial_kernel, (0, 1, 3, 2)).reshape(9 * channels, mids)
    t3 = jnp.transpose(temporal_kernel, (0, 2, 1))
    vmem = pltpu.MemorySpace.VMEM if hasattr(pltpu, "MemorySpace") else pltpu.VMEM
    params = pltpu.CompilerParams(vmem_limit_bytes=48 * 1024 * 1024)
    spec = pl.BlockSpec(memory_space=vmem)
    plane = (rows * width, mids)
    edges = pl.pallas_call(
        _edges_two_kernel,
        out_shape=jax.ShapeDtypeStruct((2,) + plane, rowed.dtype),
        in_specs=[spec] * 2,
        out_specs=spec,
        compiler_params=params,
        cost_estimate=pl.CostEstimate(
            flops=2 * 2 * rows * width * 9 * channels * mids, bytes_accessed=2 * rowed.size, transcendentals=0
        ),
    )(rowed, w9)
    before = from_behind(edges[1:], "tm", 1)
    after = from_behind(edges[:1], "tm", -1)
    inner, side = pl.pallas_call(
        _inner_two_kernel,
        out_shape=(
            jax.ShapeDtypeStruct((frames - 2, rows, width, channels), rowed.dtype),
            jax.ShapeDtypeStruct((2,) + plane, rowed.dtype),
        ),
        in_specs=[spec] * 3,
        out_specs=(spec, spec),
        scratch_shapes=[pltpu.VMEM((frames,) + plane, jnp.bfloat16)],
        compiler_params=params,
        cost_estimate=pl.CostEstimate(
            flops=2 * frames * rows * width * (9 * channels * mids + 3 * mids * channels),
            bytes_accessed=4 * rowed.size,
            transcendentals=0,
        ),
    )(rowed, w9, t3)
    outer = pl.pallas_call(
        _outer_two_kernel,
        out_shape=jax.ShapeDtypeStruct((2, rows, width, channels), rowed.dtype),
        in_specs=[spec] * 6,
        out_specs=spec,
        compiler_params=params,
    )(rowed, t3, before, after, edges, side)
    return jnp.concatenate([outer[:1], inner, outer[1:]], axis=0)


def on_device(video_clip, spatial_one, temporal_one, down_weight, spatial_two, temporal_two):
    padded = with_halo_one(video_clip)
    keep_first = (lax.axis_index("row") > 0).astype(jnp.int32).reshape(1)
    reduced = block_one(padded, keep_first, spatial_one, temporal_one, down_weight)
    rows = reduced.shape[1]
    above = from_behind(reduced[:, rows - 1 :], "row", 1)
    below = from_behind(reduced[:, :1], "row", -1)
    return block_two(jnp.concatenate([above, reduced, below], axis=1), spatial_two, temporal_two)


def solution(mesh):
    placed = (P("tm", "row", None, None), P(), P(), P(), P(), P())
    return jax.shard_map(
        on_device, mesh=mesh, in_specs=placed, out_specs=P("tm", "row", None, None), check_vma=False
    )
```

```python
import functools

import jax
import jax.numpy as jnp
from jax import lax
from jax.experimental import pallas as pl
from jax.experimental.pallas import tpu as pltpu
from jax.sharding import PartitionSpec as P


def padded_2(block, sides, width):
    for axis, dim in sides:
        count = lax.axis_size(axis)
        forward = [(i, i + 1) for i in range(count - 1)]
        backward = [(target, source) for source, target in forward]
        low = lax.ppermute(
            lax.slice_in_dim(block, block.shape[dim] - width, None, axis=dim), axis, forward
        )
        high = lax.ppermute(lax.slice_in_dim(block, 0, width, axis=dim), axis, backward)
        block = jnp.concatenate([low, block, high], axis=dim)
    return block


def from_behind(array, axis, by):
    devices = lax.axis_size(axis)
    pairs = [(i, i + by) for i in range(devices) if 0 <= i + by < devices]
    return lax.ppermute(array, axis, pairs)


def spatial(source, kernel, layout):
    return lax.conv_general_dilated(
        source,
        kernel,
        (1, 1),
        ((0, 0), (1, 1)),
        dimension_numbers=(layout, "HWOI", layout),
        preferred_element_type=jnp.float32,
    )


def temporal(source, kernel, layout):
    return lax.conv_general_dilated(
        source,
        kernel[:, None],
        (1, 1),
        ((0, 0), (0, 0)),
        dimension_numbers=(layout, "HWOI", layout),
        preferred_element_type=jnp.float32,
    )


def residual_block(source, spatial_kernel, temporal_kernel, space_layout, time_layout):
    padded = padded_2(source, (("tm", 0), ("row", 1)), 1)
    framed = jax.nn.relu(spatial(padded, spatial_kernel, space_layout)).astype(jnp.bfloat16)
    summed = source.astype(jnp.float32) + temporal(framed, temporal_kernel, time_layout)
    return jax.nn.relu(summed).astype(jnp.bfloat16)


def _lane_shift(x, by):
    width = x.shape[-1]
    rolled = pltpu.roll(x, (-by) % width, x.ndim - 1)
    lane = lax.broadcasted_iota(jnp.int32, x.shape, x.ndim - 1)
    inside = jnp.logical_and(lane + by >= 0, lane + by < width)
    return jnp.where(inside, rolled, jnp.zeros_like(rolled))


def _middle_one(xp_ref, f, w9_ref):
    rows = xp_ref.shape[1] - 2
    slab = xp_ref[f].astype(jnp.float32)
    shifted = [_lane_shift(slab, b - 1).astype(jnp.bfloat16) for b in range(3)]
    parts = []
    for a in range(3):
        for b in range(3):
            parts.append(jnp.concatenate([shifted[b][h + a] for h in range(rows)], axis=1))
    stacked = jnp.concatenate(parts, axis=0)
    m = jnp.dot(w9_ref[...], stacked, preferred_element_type=jnp.float32)
    return jnp.maximum(m, 0.0).astype(jnp.bfloat16)


def _section_down(stacked, xp_ref, t, t3_ref, wd_ref, keep_ref, out_ref, slot):
    rows = xp_ref.shape[1] - 2
    width = xp_ref.shape[-1]
    reduced_rows = (rows - 1) // 2
    lane = lax.broadcasted_iota(jnp.int32, (width // 2, width), 1)
    column = lax.broadcasted_iota(jnp.int32, (width // 2, width), 0)
    pick = (lane == 2 * column).astype(jnp.bfloat16)
    s = jnp.dot(t3_ref[...], stacked, preferred_element_type=jnp.float32)
    sec = []
    for h in range(rows):
        v = s[:, h * width : (h + 1) * width] + xp_ref[t, h + 1].astype(jnp.float32)
        v = jnp.maximum(v, 0.0)
        if h == 0:
            v = v * keep_ref[0].astype(jnp.float32)
        sec.append(v.astype(jnp.bfloat16).astype(jnp.float32))
    shifted = [[_lane_shift(r, b - 1).astype(jnp.bfloat16) for b in range(3)] for r in sec]
    parts = []
    for a in range(3):
        for b in range(3):
            parts.append(jnp.concatenate([shifted[2 * i + a][b] for i in range(reduced_rows)], axis=1))
    stacked = jnp.concatenate(parts, axis=0)
    full = jnp.dot(wd_ref[...], stacked, preferred_element_type=jnp.float32)
    full = jnp.maximum(full, 0.0).astype(jnp.bfloat16)
    for i in range(reduced_rows):
        r = lax.dot_general(
            pick,
            full[:, i * width : (i + 1) * width],
            (((1,), (1,)), ((), ())),
            preferred_element_type=jnp.float32,
        )
        out_ref[slot, i] = r.astype(out_ref.dtype)


def _edges_one_kernel(xp_ref, w9_ref, edge_ref):
    frames = xp_ref.shape[0]
    edge_ref[0] = _middle_one(xp_ref, 0, w9_ref)
    edge_ref[1] = _middle_one(xp_ref, frames - 1, w9_ref)


def _inner_one_kernel(keep_ref, xp_ref, w9_ref, t3_ref, wd_ref, out_ref, side_ref, mid_ref):
    frames = xp_ref.shape[0]

    def middle(f, carry):
        mid_ref[f] = _middle_one(xp_ref, f, w9_ref)
        return carry

    lax.fori_loop(0, frames, middle, 0)
    side_ref[0] = mid_ref[1]
    side_ref[1] = mid_ref[frames - 2]

    def section(t, carry):
        stacked = jnp.concatenate([mid_ref[t - 1], mid_ref[t], mid_ref[t + 1]], axis=0)
        _section_down(stacked, xp_ref, t, t3_ref, wd_ref, keep_ref, out_ref, t - 1)
        return carry

    lax.fori_loop(1, frames - 1, section, 0)


def _outer_one_kernel(keep_ref, xp_ref, t3_ref, wd_ref, before_ref, after_ref, edge_ref, side_ref, out_ref):
    frames = xp_ref.shape[0]
    stacked = jnp.concatenate([before_ref[0], edge_ref[0], side_ref[0]], axis=0)
    _section_down(stacked, xp_ref, 0, t3_ref, wd_ref, keep_ref, out_ref, 0)
    stacked = jnp.concatenate([side_ref[1], edge_ref[1], after_ref[0]], axis=0)
    _section_down(stacked, xp_ref, frames - 1, t3_ref, wd_ref, keep_ref, out_ref, 1)


def block_one(rowed, keep_first, spatial_kernel, temporal_kernel, down_kernel):
    frames, rows_p, channels, width = rowed.shape
    rows = rows_p - 2
    mids = spatial_kernel.shape[2]
    outs = down_kernel.shape[2]
    w9 = jnp.transpose(spatial_kernel, (2, 0, 1, 3)).reshape(mids, 9 * channels)
    t3 = jnp.transpose(temporal_kernel, (1, 0, 2)).reshape(channels, 3 * mids)
    wd = jnp.transpose(down_kernel, (2, 0, 1, 3)).reshape(outs, 9 * channels)
    vmem = pltpu.MemorySpace.VMEM if hasattr(pltpu, "MemorySpace") else pltpu.VMEM
    smem = pltpu.MemorySpace.SMEM if hasattr(pltpu, "MemorySpace") else pltpu.SMEM
    params = pltpu.CompilerParams(vmem_limit_bytes=48 * 1024 * 1024)
    spec = pl.BlockSpec(memory_space=vmem)
    sspec = pl.BlockSpec(memory_space=smem)
    reduced_rows = (rows - 1) // 2
    plane = (mids, rows * width)
    out_plane = (reduced_rows, width // 2, outs)
    spatial_flops = 2 * rows * width * 9 * channels * mids
    section_flops = 2 * rows * width * 3 * mids * channels + 2 * reduced_rows * width * 9 * channels * outs
    edges = pl.pallas_call(
        _edges_one_kernel,
        out_shape=jax.ShapeDtypeStruct((2,) + plane, rowed.dtype),
        in_specs=[spec] * 2,
        out_specs=spec,
        compiler_params=params,
        cost_estimate=pl.CostEstimate(flops=2 * spatial_flops, bytes_accessed=2 * rowed.size, transcendentals=0),
    )(rowed, w9)
    before = from_behind(edges[1:], "tm", 1)
    after = from_behind(edges[:1], "tm", -1)
    inner, side = pl.pallas_call(
        _inner_one_kernel,
        out_shape=(
            jax.ShapeDtypeStruct((frames - 2,) + out_plane, rowed.dtype),
            jax.ShapeDtypeStruct((2,) + plane, rowed.dtype),
        ),
        in_specs=[sspec] + [spec] * 4,
        out_specs=(spec, spec),
        scratch_shapes=[pltpu.VMEM((frames,) + plane, jnp.bfloat16)],
        compiler_params=params,
        cost_estimate=pl.CostEstimate(
            flops=frames * (spatial_flops + section_flops), bytes_accessed=4 * rowed.size, transcendentals=0
        ),
    )(keep_first, rowed, w9, t3, wd)
    outer = pl.pallas_call(
        _outer_one_kernel,
        out_shape=jax.ShapeDtypeStruct((2,) + out_plane, rowed.dtype),
        in_specs=[sspec] + [spec] * 7,
        out_specs=spec,
        compiler_params=params,
    )(keep_first, rowed, t3, wd, before, after, edges, side)
    return jnp.concatenate([outer[:1], inner, outer[1:]], axis=0)


def _sublane_shift(x, by, axis):
    size = x.shape[axis]
    rolled = pltpu.roll(x, (-by) % size, axis)
    index = lax.broadcasted_iota(jnp.int32, x.shape, axis)
    inside = jnp.logical_and(index + by >= 0, index + by < size)
    return jnp.where(inside, rolled, jnp.zeros_like(rolled))


def _middle_two(xp_ref, f, w9_ref):
    rows = xp_ref.shape[1] - 2
    slab = xp_ref[f].astype(jnp.float32)
    shifted = [_sublane_shift(slab, b - 1, 1).astype(jnp.bfloat16) for b in range(3)]
    stacked = jnp.concatenate(
        [
            jnp.concatenate([shifted[b][i + a] for a in range(3) for b in range(3)], axis=1)
            for i in range(rows)
        ],
        axis=0,
    )
    m = jnp.dot(stacked, w9_ref[...], preferred_element_type=jnp.float32)
    return jnp.maximum(m, 0.0).astype(jnp.bfloat16)


def _edges_two_kernel(xp_ref, w9_ref, edge_ref):
    frames = xp_ref.shape[0]
    edge_ref[0] = _middle_two(xp_ref, 0, w9_ref)
    edge_ref[1] = _middle_two(xp_ref, frames - 1, w9_ref)


def _finish(s, xp_ref, t, out_ref, slot):
    rows, width = xp_ref.shape[1] - 2, xp_ref.shape[2]
    for i in range(rows):
        v = s[i * width : (i + 1) * width] + xp_ref[t, i + 1].astype(jnp.float32)
        out_ref[slot, i] = jnp.maximum(v, 0.0).astype(out_ref.dtype)


def _inner_two_kernel(xp_ref, w9_ref, t3_ref, out_ref, side_ref, mid_ref):
    frames = xp_ref.shape[0]

    def middle(f, carry):
        mid_ref[f] = _middle_two(xp_ref, f, w9_ref)
        return carry

    lax.fori_loop(0, frames, middle, 0)
    side_ref[0] = mid_ref[1]
    side_ref[1] = mid_ref[frames - 2]

    def section(t, carry):
        s = jnp.dot(mid_ref[t - 1], t3_ref[0], preferred_element_type=jnp.float32)
        s = s + jnp.dot(mid_ref[t], t3_ref[1], preferred_element_type=jnp.float32)
        s = s + jnp.dot(mid_ref[t + 1], t3_ref[2], preferred_element_type=jnp.float32)
        _finish(s, xp_ref, t, out_ref, t - 1)
        return carry

    lax.fori_loop(1, frames - 1, section, 0)


def _outer_two_kernel(xp_ref, t3_ref, before_ref, after_ref, edge_ref, side_ref, out_ref):
    frames = xp_ref.shape[0]
    s = jnp.dot(before_ref[0], t3_ref[0], preferred_element_type=jnp.float32)
    s = s + jnp.dot(edge_ref[0], t3_ref[1], preferred_element_type=jnp.float32)
    s = s + jnp.dot(side_ref[0], t3_ref[2], preferred_element_type=jnp.float32)
    _finish(s, xp_ref, 0, out_ref, 0)
    s = jnp.dot(side_ref[1], t3_ref[0], preferred_element_type=jnp.float32)
    s = s + jnp.dot(edge_ref[1], t3_ref[1], preferred_element_type=jnp.float32)
    s = s + jnp.dot(after_ref[0], t3_ref[2], preferred_element_type=jnp.float32)
    _finish(s, xp_ref, frames - 1, out_ref, 1)


def block_two(rowed, spatial_kernel, temporal_kernel):
    frames, rows_p, width, channels = rowed.shape
    rows = rows_p - 2
    mids = spatial_kernel.shape[2]
    w9 = jnp.transpose(spatial_kernel, (0, 1, 3, 2)).reshape(9 * channels, mids)
    t3 = jnp.transpose(temporal_kernel, (0, 2, 1))
    vmem = pltpu.MemorySpace.VMEM if hasattr(pltpu, "MemorySpace") else pltpu.VMEM
    params = pltpu.CompilerParams(vmem_limit_bytes=48 * 1024 * 1024)
    spec = pl.BlockSpec(memory_space=vmem)
    plane = (rows * width, mids)
    edges = pl.pallas_call(
        _edges_two_kernel,
        out_shape=jax.ShapeDtypeStruct((2,) + plane, rowed.dtype),
        in_specs=[spec] * 2,
        out_specs=spec,
        compiler_params=params,
        cost_estimate=pl.CostEstimate(
            flops=2 * 2 * rows * width * 9 * channels * mids, bytes_accessed=2 * rowed.size, transcendentals=0
        ),
    )(rowed, w9)
    before = from_behind(edges[1:], "tm", 1)
    after = from_behind(edges[:1], "tm", -1)
    inner, side = pl.pallas_call(
        _inner_two_kernel,
        out_shape=(
            jax.ShapeDtypeStruct((frames - 2, rows, width, channels), rowed.dtype),
            jax.ShapeDtypeStruct((2,) + plane, rowed.dtype),
        ),
        in_specs=[spec] * 3,
        out_specs=(spec, spec),
        scratch_shapes=[pltpu.VMEM((frames,) + plane, jnp.bfloat16)],
        compiler_params=params,
        cost_estimate=pl.CostEstimate(
            flops=2 * frames * rows * width * (9 * channels * mids + 3 * mids * channels),
            bytes_accessed=4 * rowed.size,
            transcendentals=0,
        ),
    )(rowed, w9, t3)
    outer = pl.pallas_call(
        _outer_two_kernel,
        out_shape=jax.ShapeDtypeStruct((2, rows, width, channels), rowed.dtype),
        in_specs=[spec] * 6,
        out_specs=spec,
        compiler_params=params,
    )(rowed, t3, before, after, edges, side)
    return jnp.concatenate([outer[:1], inner, outer[1:]], axis=0)


def on_device(video_clip, spatial_one, temporal_one, down_weight, spatial_two, temporal_two):
    rows = video_clip.shape[1]
    above = from_behind(video_clip[:, rows - 2 :], "row", 1)
    below = from_behind(video_clip[:, :1], "row", -1)
    padded = jnp.concatenate([above, video_clip, below], axis=1)
    keep_first = (lax.axis_index("row") > 0).astype(jnp.int32).reshape(1)
    reduced = block_one(padded, keep_first, spatial_one, temporal_one, down_weight)
    rows = reduced.shape[1]
    above = from_behind(reduced[:, rows - 1 :], "row", 1)
    below = from_behind(reduced[:, :1], "row", -1)
    return block_two(jnp.concatenate([above, reduced, below], axis=1), spatial_two, temporal_two)


def solution(mesh):
    placed = (P("tm", "row", None, None), P(), P(), P(), P(), P())
    return jax.shard_map(
        on_device, mesh=mesh, in_specs=placed, out_specs=P("tm", "row", None, None), check_vma=False
    )
```

```python
import functools

import jax
import jax.numpy as jnp
from jax import lax
from jax.experimental import pallas as pl
from jax.experimental.pallas import tpu as pltpu
from jax.sharding import PartitionSpec as P


def padded_2(block, sides, width):
    for axis, dim in sides:
        count = lax.axis_size(axis)
        forward = [(i, i + 1) for i in range(count - 1)]
        backward = [(target, source) for source, target in forward]
        low = lax.ppermute(
            lax.slice_in_dim(block, block.shape[dim] - width, None, axis=dim), axis, forward
        )
        high = lax.ppermute(lax.slice_in_dim(block, 0, width, axis=dim), axis, backward)
        block = jnp.concatenate([low, block, high], axis=dim)
    return block


def from_behind(array, axis, by):
    devices = lax.axis_size(axis)
    pairs = [(i, i + by) for i in range(devices) if 0 <= i + by < devices]
    return lax.ppermute(array, axis, pairs)


def spatial(source, kernel, layout):
    return lax.conv_general_dilated(
        source,
        kernel,
        (1, 1),
        ((0, 0), (1, 1)),
        dimension_numbers=(layout, "HWOI", layout),
        preferred_element_type=jnp.float32,
    )


def temporal(source, kernel, layout):
    return lax.conv_general_dilated(
        source,
        kernel[:, None],
        (1, 1),
        ((0, 0), (0, 0)),
        dimension_numbers=(layout, "HWOI", layout),
        preferred_element_type=jnp.float32,
    )


def residual_block(source, spatial_kernel, temporal_kernel, space_layout, time_layout):
    padded = padded_2(source, (("tm", 0), ("row", 1)), 1)
    framed = jax.nn.relu(spatial(padded, spatial_kernel, space_layout)).astype(jnp.bfloat16)
    summed = source.astype(jnp.float32) + temporal(framed, temporal_kernel, time_layout)
    return jax.nn.relu(summed).astype(jnp.bfloat16)


def _lane_shift(x, by):
    width = x.shape[-1]
    rolled = pltpu.roll(x, (-by) % width, x.ndim - 1)
    lane = lax.broadcasted_iota(jnp.int32, x.shape, x.ndim - 1)
    inside = jnp.logical_and(lane + by >= 0, lane + by < width)
    return jnp.where(inside, rolled, jnp.zeros_like(rolled))


def _middle_one(refs, f, w9_ref):
    above_ref, xp_ref, below_ref = refs
    rows = xp_ref.shape[1] + 1
    slab = jnp.concatenate([above_ref[f], xp_ref[f], below_ref[f]], axis=0).astype(jnp.float32)
    shifted = [_lane_shift(slab, b - 1).astype(jnp.bfloat16) for b in range(3)]
    parts = []
    for a in range(3):
        for b in range(3):
            parts.append(jnp.concatenate([shifted[b][h + a] for h in range(rows)], axis=1))
    stacked = jnp.concatenate(parts, axis=0)
    m = jnp.dot(w9_ref[...], stacked, preferred_element_type=jnp.float32)
    return jnp.maximum(m, 0.0).astype(jnp.bfloat16)


def _section_down(stacked, refs, t, t3_ref, wd_ref, keep_ref, out_ref, slot):
    above_ref, xp_ref, _ = refs
    rows = xp_ref.shape[1] + 1
    width = xp_ref.shape[-1]
    reduced_rows = (rows - 1) // 2
    lane = lax.broadcasted_iota(jnp.int32, (width // 2, width), 1)
    column = lax.broadcasted_iota(jnp.int32, (width // 2, width), 0)
    pick = (lane == 2 * column).astype(jnp.bfloat16)
    s = jnp.dot(t3_ref[...], stacked, preferred_element_type=jnp.float32)
    sec = []
    for h in range(rows):
        own = above_ref[t, 1] if h == 0 else xp_ref[t, h - 1]
        v = s[:, h * width : (h + 1) * width] + own.astype(jnp.float32)
        v = jnp.maximum(v, 0.0)
        if h == 0:
            v = v * keep_ref[0].astype(jnp.float32)
        sec.append(v.astype(jnp.bfloat16).astype(jnp.float32))
    shifted = [[_lane_shift(r, b - 1).astype(jnp.bfloat16) for b in range(3)] for r in sec]
    parts = []
    for a in range(3):
        for b in range(3):
            parts.append(jnp.concatenate([shifted[2 * i + a][b] for i in range(reduced_rows)], axis=1))
    stacked = jnp.concatenate(parts, axis=0)
    full = jnp.dot(wd_ref[...], stacked, preferred_element_type=jnp.float32)
    full = jnp.maximum(full, 0.0).astype(jnp.bfloat16)
    for i in range(reduced_rows):
        r = lax.dot_general(
            pick,
            full[:, i * width : (i + 1) * width],
            (((1,), (1,)), ((), ())),
            preferred_element_type=jnp.float32,
        )
        out_ref[slot, i] = r.astype(out_ref.dtype)


def _edges_one_kernel(above_ref, xp_ref, below_ref, w9_ref, edge_ref):
    refs = (above_ref, xp_ref, below_ref)
    frames = xp_ref.shape[0]
    edge_ref[0] = _middle_one(refs, 0, w9_ref)
    edge_ref[1] = _middle_one(refs, frames - 1, w9_ref)


def _inner_one_kernel(keep_ref, above_ref, xp_ref, below_ref, w9_ref, t3_ref, wd_ref, out_ref, side_ref, mid_ref):
    refs = (above_ref, xp_ref, below_ref)
    frames = xp_ref.shape[0]

    def middle(f, carry):
        mid_ref[f] = _middle_one(refs, f, w9_ref)
        return carry

    lax.fori_loop(0, frames, middle, 0)
    side_ref[0] = mid_ref[1]
    side_ref[1] = mid_ref[frames - 2]

    def section(t, carry):
        stacked = jnp.concatenate([mid_ref[t - 1], mid_ref[t], mid_ref[t + 1]], axis=0)
        _section_down(stacked, refs, t, t3_ref, wd_ref, keep_ref, out_ref, t - 1)
        return carry

    lax.fori_loop(1, frames - 1, section, 0)


def _outer_one_kernel(
    keep_ref, above_ref, xp_ref, below_ref, t3_ref, wd_ref, before_ref, after_ref, edge_ref, side_ref, out_ref
):
    refs = (above_ref, xp_ref, below_ref)
    frames = xp_ref.shape[0]
    stacked = jnp.concatenate([before_ref[0], edge_ref[0], side_ref[0]], axis=0)
    _section_down(stacked, refs, 0, t3_ref, wd_ref, keep_ref, out_ref, 0)
    stacked = jnp.concatenate([side_ref[1], edge_ref[1], after_ref[0]], axis=0)
    _section_down(stacked, refs, frames - 1, t3_ref, wd_ref, keep_ref, out_ref, 1)


def block_one(above, rowed, below, keep_first, spatial_kernel, temporal_kernel, down_kernel):
    frames, rows, channels, width = rowed.shape
    rows = rows + 1
    mids = spatial_kernel.shape[2]
    outs = down_kernel.shape[2]
    w9 = jnp.transpose(spatial_kernel, (2, 0, 1, 3)).reshape(mids, 9 * channels)
    t3 = jnp.transpose(temporal_kernel, (1, 0, 2)).reshape(channels, 3 * mids)
    wd = jnp.transpose(down_kernel, (2, 0, 1, 3)).reshape(outs, 9 * channels)
    vmem = pltpu.MemorySpace.VMEM if hasattr(pltpu, "MemorySpace") else pltpu.VMEM
    smem = pltpu.MemorySpace.SMEM if hasattr(pltpu, "MemorySpace") else pltpu.SMEM
    params = pltpu.CompilerParams(vmem_limit_bytes=48 * 1024 * 1024)
    spec = pl.BlockSpec(memory_space=vmem)
    sspec = pl.BlockSpec(memory_space=smem)
    reduced_rows = (rows - 1) // 2
    plane = (mids, rows * width)
    out_plane = (reduced_rows, width // 2, outs)
    spatial_flops = 2 * rows * width * 9 * channels * mids
    section_flops = 2 * rows * width * 3 * mids * channels + 2 * reduced_rows * width * 9 * channels * outs
    edges = pl.pallas_call(
        _edges_one_kernel,
        out_shape=jax.ShapeDtypeStruct((2,) + plane, rowed.dtype),
        in_specs=[spec] * 4,
        out_specs=spec,
        compiler_params=params,
        cost_estimate=pl.CostEstimate(flops=2 * spatial_flops, bytes_accessed=2 * rowed.size, transcendentals=0),
    )(above, rowed, below, w9)
    before = from_behind(edges[1:], "tm", 1)
    after = from_behind(edges[:1], "tm", -1)
    inner, side = pl.pallas_call(
        _inner_one_kernel,
        out_shape=(
            jax.ShapeDtypeStruct((frames - 2,) + out_plane, rowed.dtype),
            jax.ShapeDtypeStruct((2,) + plane, rowed.dtype),
        ),
        in_specs=[sspec] + [spec] * 6,
        out_specs=(spec, spec),
        scratch_shapes=[pltpu.VMEM((frames,) + plane, jnp.bfloat16)],
        compiler_params=params,
        cost_estimate=pl.CostEstimate(
            flops=frames * (spatial_flops + section_flops), bytes_accessed=4 * rowed.size, transcendentals=0
        ),
    )(keep_first, above, rowed, below, w9, t3, wd)
    outer = pl.pallas_call(
        _outer_one_kernel,
        out_shape=jax.ShapeDtypeStruct((2,) + out_plane, rowed.dtype),
        in_specs=[sspec] + [spec] * 9,
        out_specs=spec,
        compiler_params=params,
    )(keep_first, above, rowed, below, t3, wd, before, after, edges, side)
    return jnp.concatenate([outer[:1], inner, outer[1:]], axis=0)


def _sublane_shift(x, by, axis):
    size = x.shape[axis]
    rolled = pltpu.roll(x, (-by) % size, axis)
    index = lax.broadcasted_iota(jnp.int32, x.shape, axis)
    inside = jnp.logical_and(index + by >= 0, index + by < size)
    return jnp.where(inside, rolled, jnp.zeros_like(rolled))


def _slab_two(above_ref, xp_ref, below_ref, f):
    return jnp.concatenate([above_ref[f], xp_ref[f], below_ref[f]], axis=0).astype(jnp.float32)


def _middle_two(slabs, w9_ref):
    rows = slabs[0].shape[0] - 2
    pieces = []
    for slab in slabs:
        shifted = [_sublane_shift(slab, b - 1, 1).astype(jnp.bfloat16) for b in range(3)]
        for i in range(rows):
            pieces.append(jnp.concatenate([shifted[b][i + a] for a in range(3) for b in range(3)], axis=1))
    stacked = jnp.concatenate(pieces, axis=0)
    m = jnp.dot(stacked, w9_ref[...], preferred_element_type=jnp.float32)
    return jnp.maximum(m, 0.0).astype(jnp.bfloat16)


def _edges_two_kernel(above_ref, xp_ref, below_ref, w9_ref, edge_ref):
    frames = xp_ref.shape[0]
    plane = edge_ref.shape[1]
    m = _middle_two(
        [_slab_two(above_ref, xp_ref, below_ref, 0), _slab_two(above_ref, xp_ref, below_ref, frames - 1)], w9_ref
    )
    edge_ref[0] = m[:plane]
    edge_ref[1] = m[plane:]


def _finish(s, xp_ref, t, out_ref, slot):
    rows, width = xp_ref.shape[1], xp_ref.shape[2]
    for i in range(rows):
        v = s[i * width : (i + 1) * width] + xp_ref[t, i].astype(jnp.float32)
        out_ref[slot, i] = jnp.maximum(v, 0.0).astype(out_ref.dtype)


def _inner_two_kernel(above_ref, xp_ref, below_ref, w9_ref, t3_ref, out_ref, side_ref, mid_ref):
    frames = xp_ref.shape[0]
    plane = mid_ref.shape[1]

    def middle(g, carry):
        f = 2 * g
        m = _middle_two(
            [_slab_two(above_ref, xp_ref, below_ref, f), _slab_two(above_ref, xp_ref, below_ref, f + 1)], w9_ref
        )
        mid_ref[f] = m[:plane]
        mid_ref[f + 1] = m[plane:]
        return carry

    lax.fori_loop(0, frames // 2, middle, 0)
    side_ref[0] = mid_ref[1]
    side_ref[1] = mid_ref[frames - 2]

    def section(g, carry):
        t = 2 * g + 1
        s = None
        for k in range(3):
            pair = jnp.concatenate([mid_ref[t - 1 + k], mid_ref[t + k]], axis=0)
            d = jnp.dot(pair, t3_ref[k], preferred_element_type=jnp.float32)
            s = d if s is None else s + d
        _finish(s[:plane], xp_ref, t, out_ref, t - 1)
        _finish(s[plane:], xp_ref, t + 1, out_ref, t)
        return carry

    lax.fori_loop(0, (frames - 2) // 2, section, 0)


def _outer_two_kernel(xp_ref, t3_ref, before_ref, after_ref, edge_ref, side_ref, out_ref):
    frames = xp_ref.shape[0]
    s = jnp.dot(before_ref[0], t3_ref[0], preferred_element_type=jnp.float32)
    s = s + jnp.dot(edge_ref[0], t3_ref[1], preferred_element_type=jnp.float32)
    s = s + jnp.dot(side_ref[0], t3_ref[2], preferred_element_type=jnp.float32)
    _finish(s, xp_ref, 0, out_ref, 0)
    s = jnp.dot(side_ref[1], t3_ref[0], preferred_element_type=jnp.float32)
    s = s + jnp.dot(edge_ref[1], t3_ref[1], preferred_element_type=jnp.float32)
    s = s + jnp.dot(after_ref[0], t3_ref[2], preferred_element_type=jnp.float32)
    _finish(s, xp_ref, frames - 1, out_ref, 1)


def block_two(above, rowed, below, spatial_kernel, temporal_kernel):
    frames, rows, width, channels = rowed.shape
    mids = spatial_kernel.shape[2]
    w9 = jnp.transpose(spatial_kernel, (0, 1, 3, 2)).reshape(9 * channels, mids)
    t3 = jnp.transpose(temporal_kernel, (0, 2, 1))
    vmem = pltpu.MemorySpace.VMEM if hasattr(pltpu, "MemorySpace") else pltpu.VMEM
    params = pltpu.CompilerParams(vmem_limit_bytes=48 * 1024 * 1024)
    spec = pl.BlockSpec(memory_space=vmem)
    plane = (rows * width, mids)
    edges = pl.pallas_call(
        _edges_two_kernel,
        out_shape=jax.ShapeDtypeStruct((2,) + plane, rowed.dtype),
        in_specs=[spec] * 4,
        out_specs=spec,
        compiler_params=params,
        cost_estimate=pl.CostEstimate(
            flops=2 * 2 * rows * width * 9 * channels * mids, bytes_accessed=2 * rowed.size, transcendentals=0
        ),
    )(above, rowed, below, w9)
    before = from_behind(edges[1:], "tm", 1)
    after = from_behind(edges[:1], "tm", -1)
    inner, side = pl.pallas_call(
        _inner_two_kernel,
        out_shape=(
            jax.ShapeDtypeStruct((frames - 2, rows, width, channels), rowed.dtype),
            jax.ShapeDtypeStruct((2,) + plane, rowed.dtype),
        ),
        in_specs=[spec] * 5,
        out_specs=(spec, spec),
        scratch_shapes=[pltpu.VMEM((frames,) + plane, jnp.bfloat16)],
        compiler_params=params,
        cost_estimate=pl.CostEstimate(
            flops=2 * frames * rows * width * (9 * channels * mids + 3 * mids * channels),
            bytes_accessed=4 * rowed.size,
            transcendentals=0,
        ),
    )(above, rowed, below, w9, t3)
    outer = pl.pallas_call(
        _outer_two_kernel,
        out_shape=jax.ShapeDtypeStruct((2, rows, width, channels), rowed.dtype),
        in_specs=[spec] * 6,
        out_specs=spec,
        compiler_params=params,
    )(rowed, t3, before, after, edges, side)
    return jnp.concatenate([outer[:1], inner, outer[1:]], axis=0)


def on_device(video_clip, spatial_one, temporal_one, down_weight, spatial_two, temporal_two):
    rows = video_clip.shape[1]
    above = from_behind(video_clip[:, rows - 2 :], "row", 1)
    below = from_behind(video_clip[:, :1], "row", -1)
    keep_first = (lax.axis_index("row") > 0).astype(jnp.int32).reshape(1)
    reduced = block_one(above, video_clip, below, keep_first, spatial_one, temporal_one, down_weight)
    rows = reduced.shape[1]
    above = from_behind(reduced[:, rows - 1 :], "row", 1)
    below = from_behind(reduced[:, :1], "row", -1)
    return block_two(above, reduced, below, spatial_two, temporal_two)


def solution(mesh):
    placed = (P("tm", "row", None, None), P(), P(), P(), P(), P())
    return jax.shard_map(
        on_device, mesh=mesh, in_specs=placed, out_specs=P("tm", "row", None, None), check_vma=False
    )
```

```python
import functools

import jax
import jax.numpy as jnp
from jax import lax
from jax.experimental import pallas as pl
from jax.experimental.pallas import tpu as pltpu
from jax.sharding import PartitionSpec as P


def padded_2(block, sides, width):
    for axis, dim in sides:
        count = lax.axis_size(axis)
        forward = [(i, i + 1) for i in range(count - 1)]
        backward = [(target, source) for source, target in forward]
        low = lax.ppermute(
            lax.slice_in_dim(block, block.shape[dim] - width, None, axis=dim), axis, forward
        )
        high = lax.ppermute(lax.slice_in_dim(block, 0, width, axis=dim), axis, backward)
        block = jnp.concatenate([low, block, high], axis=dim)
    return block


def from_behind(array, axis, by):
    devices = lax.axis_size(axis)
    pairs = [(i, i + by) for i in range(devices) if 0 <= i + by < devices]
    return lax.ppermute(array, axis, pairs)


def spatial(source, kernel, layout):
    return lax.conv_general_dilated(
        source,
        kernel,
        (1, 1),
        ((0, 0), (1, 1)),
        dimension_numbers=(layout, "HWOI", layout),
        preferred_element_type=jnp.float32,
    )


def temporal(source, kernel, layout):
    return lax.conv_general_dilated(
        source,
        kernel[:, None],
        (1, 1),
        ((0, 0), (0, 0)),
        dimension_numbers=(layout, "HWOI", layout),
        preferred_element_type=jnp.float32,
    )


def residual_block(source, spatial_kernel, temporal_kernel, space_layout, time_layout):
    padded = padded_2(source, (("tm", 0), ("row", 1)), 1)
    framed = jax.nn.relu(spatial(padded, spatial_kernel, space_layout)).astype(jnp.bfloat16)
    summed = source.astype(jnp.float32) + temporal(framed, temporal_kernel, time_layout)
    return jax.nn.relu(summed).astype(jnp.bfloat16)


_ANY = pl.ANY


def _lane_shift(x, by):
    width = x.shape[-1]
    rolled = pltpu.roll(x, (-by) % width, x.ndim - 1)
    lane = lax.broadcasted_iota(jnp.int32, x.shape, x.ndim - 1)
    inside = jnp.logical_and(lane + by >= 0, lane + by < width)
    return jnp.where(inside, rolled, jnp.zeros_like(rolled))


def _middle_one(refs, f, w9_ref):
    above_ref, xp_ref, below_ref = refs
    rows = xp_ref.shape[1] + 1
    slab = jnp.concatenate([above_ref[f], xp_ref[f], below_ref[f]], axis=0).astype(jnp.float32)
    shifted = [_lane_shift(slab, b - 1).astype(jnp.bfloat16) for b in range(3)]
    parts = []
    for a in range(3):
        for b in range(3):
            parts.append(jnp.concatenate([shifted[b][h + a] for h in range(rows)], axis=1))
    stacked = jnp.concatenate(parts, axis=0)
    m = jnp.dot(w9_ref[...], stacked, preferred_element_type=jnp.float32)
    return jnp.maximum(m, 0.0).astype(jnp.bfloat16)


def _section_down(stacked, refs, t, t3_ref, wd_ref, keep_ref, out_ref, slot):
    above_ref, xp_ref, _ = refs
    rows = xp_ref.shape[1] + 1
    width = xp_ref.shape[-1]
    reduced_rows = (rows - 1) // 2
    lane = lax.broadcasted_iota(jnp.int32, (width // 2, width), 1)
    column = lax.broadcasted_iota(jnp.int32, (width // 2, width), 0)
    pick = (lane == 2 * column).astype(jnp.bfloat16)
    s = jnp.dot(t3_ref[...], stacked, preferred_element_type=jnp.float32)
    sec = []
    for h in range(rows):
        own = above_ref[t, 1] if h == 0 else xp_ref[t, h - 1]
        v = s[:, h * width : (h + 1) * width] + own.astype(jnp.float32)
        v = jnp.maximum(v, 0.0)
        if h == 0:
            v = v * keep_ref[0].astype(jnp.float32)
        sec.append(v.astype(jnp.bfloat16).astype(jnp.float32))
    shifted = [[_lane_shift(r, b - 1).astype(jnp.bfloat16) for b in range(3)] for r in sec]
    parts = []
    for a in range(3):
        for b in range(3):
            parts.append(jnp.concatenate([shifted[2 * i + a][b] for i in range(reduced_rows)], axis=1))
    stacked = jnp.concatenate(parts, axis=0)
    full = jnp.dot(wd_ref[...], stacked, preferred_element_type=jnp.float32)
    full = jnp.maximum(full, 0.0).astype(jnp.bfloat16)
    for i in range(reduced_rows):
        r = lax.dot_general(
            pick,
            full[:, i * width : (i + 1) * width],
            (((1,), (1,)), ((), ())),
            preferred_element_type=jnp.float32,
        )
        out_ref[slot, i] = r.astype(out_ref.dtype)


def _edges_one_kernel(above_ref, xp_ref, below_ref, w9_ref, edge_ref):
    refs = (above_ref, xp_ref, below_ref)
    frames = xp_ref.shape[0]
    edge_ref[0] = _middle_one(refs, 0, w9_ref)
    edge_ref[1] = _middle_one(refs, frames - 1, w9_ref)


def _inner_one_kernel(keep_ref, above_ref, xp_ref, below_ref, w9_ref, t3_ref, wd_ref, out_ref, side_ref, mid_ref):
    refs = (above_ref, xp_ref, below_ref)
    frames = xp_ref.shape[0]

    def middle(f, carry):
        mid_ref[f] = _middle_one(refs, f, w9_ref)
        return carry

    lax.fori_loop(0, frames, middle, 0)
    side_ref[0] = mid_ref[1]
    side_ref[1] = mid_ref[frames - 2]

    def section(t, carry):
        stacked = jnp.concatenate([mid_ref[t - 1], mid_ref[t], mid_ref[t + 1]], axis=0)
        _section_down(stacked, refs, t, t3_ref, wd_ref, keep_ref, out_ref, t)
        return carry

    lax.fori_loop(1, frames - 1, section, 0)


def _outer_one_kernel(
    keep_ref, above_ref, xp_ref, below_ref, t3_ref, wd_ref, before_ref, after_ref, edge_ref, side_ref, full_ref,
    out_ref, buf, sem
):
    refs = (above_ref, xp_ref, below_ref)
    frames = xp_ref.shape[0]
    stacked = jnp.concatenate([before_ref[0], edge_ref[0], side_ref[0]], axis=0)
    _section_down(stacked, refs, 0, t3_ref, wd_ref, keep_ref, buf, 0)
    stacked = jnp.concatenate([side_ref[1], edge_ref[1], after_ref[0]], axis=0)
    _section_down(stacked, refs, frames - 1, t3_ref, wd_ref, keep_ref, buf, 1)
    _put_ends(buf, out_ref, sem)


def block_one(above, rowed, below, keep_first, spatial_kernel, temporal_kernel, down_kernel):
    frames, rows, channels, width = rowed.shape
    rows = rows + 1
    mids = spatial_kernel.shape[2]
    outs = down_kernel.shape[2]
    w9 = jnp.transpose(spatial_kernel, (2, 0, 1, 3)).reshape(mids, 9 * channels)
    t3 = jnp.transpose(temporal_kernel, (1, 0, 2)).reshape(channels, 3 * mids)
    wd = jnp.transpose(down_kernel, (2, 0, 1, 3)).reshape(outs, 9 * channels)
    vmem = pltpu.MemorySpace.VMEM if hasattr(pltpu, "MemorySpace") else pltpu.VMEM
    smem = pltpu.MemorySpace.SMEM if hasattr(pltpu, "MemorySpace") else pltpu.SMEM
    params = pltpu.CompilerParams(vmem_limit_bytes=48 * 1024 * 1024)
    spec = pl.BlockSpec(memory_space=vmem)
    sspec = pl.BlockSpec(memory_space=smem)
    reduced_rows = (rows - 1) // 2
    plane = (mids, rows * width)
    out_plane = (reduced_rows, width // 2, outs)
    spatial_flops = 2 * rows * width * 9 * channels * mids
    section_flops = 2 * rows * width * 3 * mids * channels + 2 * reduced_rows * width * 9 * channels * outs
    edges = pl.pallas_call(
        _edges_one_kernel,
        out_shape=jax.ShapeDtypeStruct((2,) + plane, rowed.dtype),
        in_specs=[spec] * 4,
        out_specs=spec,
        compiler_params=params,
        cost_estimate=pl.CostEstimate(flops=2 * spatial_flops, bytes_accessed=2 * rowed.size, transcendentals=0),
    )(above, rowed, below, w9)
    before = from_behind(edges[1:], "tm", 1)
    after = from_behind(edges[:1], "tm", -1)
    inner, side = pl.pallas_call(
        _inner_one_kernel,
        out_shape=(
            jax.ShapeDtypeStruct((frames,) + out_plane, rowed.dtype),
            jax.ShapeDtypeStruct((2,) + plane, rowed.dtype),
        ),
        in_specs=[sspec] + [spec] * 6,
        out_specs=(spec, spec),
        scratch_shapes=[pltpu.VMEM((frames,) + plane, jnp.bfloat16)],
        compiler_params=params,
        cost_estimate=pl.CostEstimate(
            flops=frames * (spatial_flops + section_flops), bytes_accessed=4 * rowed.size, transcendentals=0
        ),
    )(keep_first, above, rowed, below, w9, t3, wd)
    anywhere = pl.BlockSpec(memory_space=_ANY)
    return pl.pallas_call(
        _outer_one_kernel,
        out_shape=jax.ShapeDtypeStruct(inner.shape, rowed.dtype),
        in_specs=[sspec] + [spec] * 9 + [anywhere],
        out_specs=anywhere,
        scratch_shapes=[pltpu.VMEM((2,) + out_plane, rowed.dtype), pltpu.SemaphoreType.DMA((2,))],
        input_output_aliases={10: 0},
        compiler_params=params,
    )(keep_first, above, rowed, below, t3, wd, before, after, edges, side, inner)


def _sublane_shift(x, by, axis):
    size = x.shape[axis]
    rolled = pltpu.roll(x, (-by) % size, axis)
    index = lax.broadcasted_iota(jnp.int32, x.shape, axis)
    inside = jnp.logical_and(index + by >= 0, index + by < size)
    return jnp.where(inside, rolled, jnp.zeros_like(rolled))


def _slab_two(above_ref, xp_ref, below_ref, f):
    return jnp.concatenate([above_ref[f], xp_ref[f], below_ref[f]], axis=0).astype(jnp.float32)


def _middle_two(slabs, w9_ref):
    rows = slabs[0].shape[0] - 2
    pieces = []
    for slab in slabs:
        shifted = [_sublane_shift(slab, b - 1, 1).astype(jnp.bfloat16) for b in range(3)]
        for i in range(rows):
            pieces.append(jnp.concatenate([shifted[b][i + a] for a in range(3) for b in range(3)], axis=1))
    stacked = jnp.concatenate(pieces, axis=0)
    m = jnp.dot(stacked, w9_ref[...], preferred_element_type=jnp.float32)
    return jnp.maximum(m, 0.0).astype(jnp.bfloat16)


def _edges_two_kernel(above_ref, xp_ref, below_ref, w9_ref, edge_ref):
    frames = xp_ref.shape[0]
    plane = edge_ref.shape[1]
    m = _middle_two(
        [_slab_two(above_ref, xp_ref, below_ref, 0), _slab_two(above_ref, xp_ref, below_ref, frames - 1)], w9_ref
    )
    edge_ref[0] = m[:plane]
    edge_ref[1] = m[plane:]


def _finish(s, xp_ref, t, out_ref, slot):
    rows, width = xp_ref.shape[1], xp_ref.shape[2]
    for i in range(rows):
        v = s[i * width : (i + 1) * width] + xp_ref[t, i].astype(jnp.float32)
        out_ref[slot, i] = jnp.maximum(v, 0.0).astype(out_ref.dtype)


def _inner_two_kernel(above_ref, xp_ref, below_ref, w9_ref, t3_ref, out_ref, side_ref, mid_ref):
    frames = xp_ref.shape[0]
    plane = mid_ref.shape[1]

    def middle(g, carry):
        f = 2 * g
        m = _middle_two(
            [_slab_two(above_ref, xp_ref, below_ref, f), _slab_two(above_ref, xp_ref, below_ref, f + 1)], w9_ref
        )
        mid_ref[f] = m[:plane]
        mid_ref[f + 1] = m[plane:]
        return carry

    lax.fori_loop(0, frames // 2, middle, 0)
    side_ref[0] = mid_ref[1]
    side_ref[1] = mid_ref[frames - 2]

    def section(g, carry):
        t = 2 * g + 1
        s = None
        for k in range(3):
            pair = jnp.concatenate([mid_ref[t - 1 + k], mid_ref[t + k]], axis=0)
            d = jnp.dot(pair, t3_ref[k], preferred_element_type=jnp.float32)
            s = d if s is None else s + d
        _finish(s[:plane], xp_ref, t, out_ref, t)
        _finish(s[plane:], xp_ref, t + 1, out_ref, t + 1)
        return carry

    lax.fori_loop(0, (frames - 2) // 2, section, 0)


def _outer_two_kernel(xp_ref, t3_ref, before_ref, after_ref, edge_ref, side_ref, full_ref, out_ref, buf, sem):
    frames = xp_ref.shape[0]
    s = jnp.dot(before_ref[0], t3_ref[0], preferred_element_type=jnp.float32)
    s = s + jnp.dot(edge_ref[0], t3_ref[1], preferred_element_type=jnp.float32)
    s = s + jnp.dot(side_ref[0], t3_ref[2], preferred_element_type=jnp.float32)
    _finish(s, xp_ref, 0, buf, 0)
    s = jnp.dot(side_ref[1], t3_ref[0], preferred_element_type=jnp.float32)
    s = s + jnp.dot(edge_ref[1], t3_ref[1], preferred_element_type=jnp.float32)
    s = s + jnp.dot(after_ref[0], t3_ref[2], preferred_element_type=jnp.float32)
    _finish(s, xp_ref, frames - 1, buf, 1)
    _put_ends(buf, out_ref, sem)


def _put_ends(buf, out_ref, sem):
    frames = out_ref.shape[0]
    first = pltpu.make_async_copy(buf.at[0], out_ref.at[0], sem.at[0])
    last = pltpu.make_async_copy(buf.at[1], out_ref.at[frames - 1], sem.at[1])
    first.start()
    last.start()
    first.wait()
    last.wait()


def block_two(above, rowed, below, spatial_kernel, temporal_kernel):
    frames, rows, width, channels = rowed.shape
    mids = spatial_kernel.shape[2]
    w9 = jnp.transpose(spatial_kernel, (0, 1, 3, 2)).reshape(9 * channels, mids)
    t3 = jnp.transpose(temporal_kernel, (0, 2, 1))
    vmem = pltpu.MemorySpace.VMEM if hasattr(pltpu, "MemorySpace") else pltpu.VMEM
    params = pltpu.CompilerParams(vmem_limit_bytes=48 * 1024 * 1024)
    spec = pl.BlockSpec(memory_space=vmem)
    plane = (rows * width, mids)
    edges = pl.pallas_call(
        _edges_two_kernel,
        out_shape=jax.ShapeDtypeStruct((2,) + plane, rowed.dtype),
        in_specs=[spec] * 4,
        out_specs=spec,
        compiler_params=params,
        cost_estimate=pl.CostEstimate(
            flops=2 * 2 * rows * width * 9 * channels * mids, bytes_accessed=2 * rowed.size, transcendentals=0
        ),
    )(above, rowed, below, w9)
    before = from_behind(edges[1:], "tm", 1)
    after = from_behind(edges[:1], "tm", -1)
    inner, side = pl.pallas_call(
        _inner_two_kernel,
        out_shape=(
            jax.ShapeDtypeStruct((frames, rows, width, channels), rowed.dtype),
            jax.ShapeDtypeStruct((2,) + plane, rowed.dtype),
        ),
        in_specs=[spec] * 5,
        out_specs=(spec, spec),
        scratch_shapes=[pltpu.VMEM((frames,) + plane, jnp.bfloat16)],
        compiler_params=params,
        cost_estimate=pl.CostEstimate(
            flops=2 * frames * rows * width * (9 * channels * mids + 3 * mids * channels),
            bytes_accessed=4 * rowed.size,
            transcendentals=0,
        ),
    )(above, rowed, below, w9, t3)
    anywhere = pl.BlockSpec(memory_space=_ANY)
    return pl.pallas_call(
        _outer_two_kernel,
        out_shape=jax.ShapeDtypeStruct(inner.shape, rowed.dtype),
        in_specs=[spec] * 6 + [anywhere],
        out_specs=anywhere,
        scratch_shapes=[pltpu.VMEM((2, rows, width, channels), rowed.dtype), pltpu.SemaphoreType.DMA((2,))],
        input_output_aliases={6: 0},
        compiler_params=params,
    )(rowed, t3, before, after, edges, side, inner)


def on_device(video_clip, spatial_one, temporal_one, down_weight, spatial_two, temporal_two):
    rows = video_clip.shape[1]
    above = from_behind(video_clip[:, rows - 2 :], "row", 1)
    below = from_behind(video_clip[:, :1], "row", -1)
    keep_first = (lax.axis_index("row") > 0).astype(jnp.int32).reshape(1)
    reduced = block_one(above, video_clip, below, keep_first, spatial_one, temporal_one, down_weight)
    rows = reduced.shape[1]
    above = from_behind(reduced[:, rows - 1 :], "row", 1)
    below = from_behind(reduced[:, :1], "row", -1)
    return block_two(above, reduced, below, spatial_two, temporal_two)


def solution(mesh):
    placed = (P("tm", "row", None, None), P(), P(), P(), P(), P())
    return jax.shard_map(
        on_device, mesh=mesh, in_specs=placed, out_specs=P("tm", "row", None, None), check_vma=False
    )
```

```python
import functools

import jax
import jax.numpy as jnp
from jax import lax
from jax.experimental import pallas as pl
from jax.experimental.pallas import tpu as pltpu
from jax.sharding import PartitionSpec as P


def padded_2(block, sides, width):
    for axis, dim in sides:
        count = lax.axis_size(axis)
        forward = [(i, i + 1) for i in range(count - 1)]
        backward = [(target, source) for source, target in forward]
        low = lax.ppermute(
            lax.slice_in_dim(block, block.shape[dim] - width, None, axis=dim), axis, forward
        )
        high = lax.ppermute(lax.slice_in_dim(block, 0, width, axis=dim), axis, backward)
        block = jnp.concatenate([low, block, high], axis=dim)
    return block


def from_behind(array, axis, by):
    devices = lax.axis_size(axis)
    pairs = [(i, i + by) for i in range(devices) if 0 <= i + by < devices]
    return lax.ppermute(array, axis, pairs)


def spatial(source, kernel, layout):
    return lax.conv_general_dilated(
        source,
        kernel,
        (1, 1),
        ((0, 0), (1, 1)),
        dimension_numbers=(layout, "HWOI", layout),
        preferred_element_type=jnp.float32,
    )


def temporal(source, kernel, layout):
    return lax.conv_general_dilated(
        source,
        kernel[:, None],
        (1, 1),
        ((0, 0), (0, 0)),
        dimension_numbers=(layout, "HWOI", layout),
        preferred_element_type=jnp.float32,
    )


def residual_block(source, spatial_kernel, temporal_kernel, space_layout, time_layout):
    padded = padded_2(source, (("tm", 0), ("row", 1)), 1)
    framed = jax.nn.relu(spatial(padded, spatial_kernel, space_layout)).astype(jnp.bfloat16)
    summed = source.astype(jnp.float32) + temporal(framed, temporal_kernel, time_layout)
    return jax.nn.relu(summed).astype(jnp.bfloat16)


def _lane_shift(x, by):
    width = x.shape[-1]
    rolled = pltpu.roll(x, (-by) % width, x.ndim - 1)
    lane = lax.broadcasted_iota(jnp.int32, x.shape, x.ndim - 1)
    inside = jnp.logical_and(lane + by >= 0, lane + by < width)
    return jnp.where(inside, rolled, jnp.zeros_like(rolled))


def _middle_one(refs, f, w9_ref):
    above_ref, xp_ref, below_ref = refs
    rows = xp_ref.shape[1] + 1
    slab = jnp.concatenate([above_ref[f], xp_ref[f], below_ref[f]], axis=0).astype(jnp.float32)
    shifted = [_lane_shift(slab, b - 1).astype(jnp.bfloat16) for b in range(3)]
    parts = []
    for a in range(3):
        for b in range(3):
            parts.append(jnp.concatenate([shifted[b][h + a] for h in range(rows)], axis=1))
    stacked = jnp.concatenate(parts, axis=0)
    m = jnp.dot(w9_ref[...], stacked, preferred_element_type=jnp.float32)
    return jnp.maximum(m, 0.0).astype(jnp.bfloat16)


def _section_down(stacked, refs, t, t3_ref, wd_ref, keep_ref, out_ref, slot):
    above_ref, xp_ref, _ = refs
    rows = xp_ref.shape[1] + 1
    width = xp_ref.shape[-1]
    reduced_rows = (rows - 1) // 2
    lane = lax.broadcasted_iota(jnp.int32, (width // 2, width), 1)
    column = lax.broadcasted_iota(jnp.int32, (width // 2, width), 0)
    pick = (lane == 2 * column).astype(jnp.bfloat16)
    s = jnp.dot(t3_ref[...], stacked, preferred_element_type=jnp.float32)
    sec = []
    for h in range(rows):
        own = above_ref[t, 1] if h == 0 else xp_ref[t, h - 1]
        v = s[:, h * width : (h + 1) * width] + own.astype(jnp.float32)
        v = jnp.maximum(v, 0.0)
        if h == 0:
            v = v * keep_ref[0].astype(jnp.float32)
        sec.append(v.astype(jnp.bfloat16).astype(jnp.float32))
    shifted = [[_lane_shift(r, b - 1).astype(jnp.bfloat16) for b in range(3)] for r in sec]
    parts = []
    for a in range(3):
        for b in range(3):
            parts.append(jnp.concatenate([shifted[2 * i + a][b] for i in range(reduced_rows)], axis=1))
    stacked = jnp.concatenate(parts, axis=0)
    full = jnp.dot(wd_ref[...], stacked, preferred_element_type=jnp.float32)
    full = jnp.maximum(full, 0.0).astype(jnp.bfloat16)
    for i in range(reduced_rows):
        r = lax.dot_general(
            pick,
            full[:, i * width : (i + 1) * width],
            (((1,), (1,)), ((), ())),
            preferred_element_type=jnp.float32,
        )
        out_ref[slot, i] = r.astype(out_ref.dtype)


def _edges_one_kernel(above_ref, xp_ref, below_ref, w9_ref, edge_ref):
    refs = (above_ref, xp_ref, below_ref)
    frames = xp_ref.shape[0]
    edge_ref[0] = _middle_one(refs, 0, w9_ref)
    edge_ref[1] = _middle_one(refs, frames - 1, w9_ref)


def _inner_one_kernel(keep_ref, above_ref, xp_ref, below_ref, w9_ref, t3_ref, wd_ref, out_ref, side_ref, mid_ref):
    refs = (above_ref, xp_ref, below_ref)
    frames = xp_ref.shape[0]

    def middle(f, carry):
        mid_ref[f] = _middle_one(refs, f, w9_ref)
        return carry

    lax.fori_loop(0, frames, middle, 0)
    side_ref[0] = mid_ref[1]
    side_ref[1] = mid_ref[frames - 2]

    def section(t, carry):
        stacked = jnp.concatenate([mid_ref[t - 1], mid_ref[t], mid_ref[t + 1]], axis=0)
        _section_down(stacked, refs, t, t3_ref, wd_ref, keep_ref, out_ref, t - 1)
        return carry

    lax.fori_loop(1, frames - 1, section, 0)


def _outer_one_kernel(
    keep_ref, above_ref, xp_ref, below_ref, t3_ref, wd_ref, before_ref, after_ref, edge_ref, side_ref, out_ref
):
    refs = (above_ref, xp_ref, below_ref)
    frames = xp_ref.shape[0]
    stacked = jnp.concatenate([before_ref[0], edge_ref[0], side_ref[0]], axis=0)
    _section_down(stacked, refs, 0, t3_ref, wd_ref, keep_ref, out_ref, 0)
    stacked = jnp.concatenate([side_ref[1], edge_ref[1], after_ref[0]], axis=0)
    _section_down(stacked, refs, frames - 1, t3_ref, wd_ref, keep_ref, out_ref, 1)


def block_one(above, rowed, below, keep_first, spatial_kernel, temporal_kernel, down_kernel):
    frames, rows, channels, width = rowed.shape
    rows = rows + 1
    mids = spatial_kernel.shape[2]
    outs = down_kernel.shape[2]
    w9 = jnp.transpose(spatial_kernel, (2, 0, 1, 3)).reshape(mids, 9 * channels)
    t3 = jnp.transpose(temporal_kernel, (1, 0, 2)).reshape(channels, 3 * mids)
    wd = jnp.transpose(down_kernel, (2, 0, 1, 3)).reshape(outs, 9 * channels)
    vmem = pltpu.MemorySpace.VMEM if hasattr(pltpu, "MemorySpace") else pltpu.VMEM
    smem = pltpu.MemorySpace.SMEM if hasattr(pltpu, "MemorySpace") else pltpu.SMEM
    params = pltpu.CompilerParams(vmem_limit_bytes=48 * 1024 * 1024)
    spec = pl.BlockSpec(memory_space=vmem)
    sspec = pl.BlockSpec(memory_space=smem)
    reduced_rows = (rows - 1) // 2
    plane = (mids, rows * width)
    out_plane = (reduced_rows, width // 2, outs)
    spatial_flops = 2 * rows * width * 9 * channels * mids
    section_flops = 2 * rows * width * 3 * mids * channels + 2 * reduced_rows * width * 9 * channels * outs
    edges = pl.pallas_call(
        _edges_one_kernel,
        out_shape=jax.ShapeDtypeStruct((2,) + plane, rowed.dtype),
        in_specs=[spec] * 4,
        out_specs=spec,
        compiler_params=params,
        cost_estimate=pl.CostEstimate(flops=2 * spatial_flops, bytes_accessed=2 * rowed.size, transcendentals=0),
    )(above, rowed, below, w9)
    before = from_behind(edges[1:], "tm", 1)
    after = from_behind(edges[:1], "tm", -1)
    inner, side = pl.pallas_call(
        _inner_one_kernel,
        out_shape=(
            jax.ShapeDtypeStruct((frames - 2,) + out_plane, rowed.dtype),
            jax.ShapeDtypeStruct((2,) + plane, rowed.dtype),
        ),
        in_specs=[sspec] + [spec] * 6,
        out_specs=(spec, spec),
        scratch_shapes=[pltpu.VMEM((frames,) + plane, jnp.bfloat16)],
        compiler_params=params,
        cost_estimate=pl.CostEstimate(
            flops=frames * (spatial_flops + section_flops), bytes_accessed=4 * rowed.size, transcendentals=0
        ),
    )(keep_first, above, rowed, below, w9, t3, wd)
    outer = pl.pallas_call(
        _outer_one_kernel,
        out_shape=jax.ShapeDtypeStruct((2,) + out_plane, rowed.dtype),
        in_specs=[sspec] + [spec] * 9,
        out_specs=spec,
        compiler_params=params,
    )(keep_first, above, rowed, below, t3, wd, before, after, edges, side)
    return jnp.concatenate([outer[:1], inner, outer[1:]], axis=0)


def _sublane_shift(x, by, axis):
    size = x.shape[axis]
    rolled = pltpu.roll(x, (-by) % size, axis)
    index = lax.broadcasted_iota(jnp.int32, x.shape, axis)
    inside = jnp.logical_and(index + by >= 0, index + by < size)
    return jnp.where(inside, rolled, jnp.zeros_like(rolled))


def _slab_two(above_ref, xp_ref, below_ref, f):
    return jnp.concatenate([above_ref[f], xp_ref[f], below_ref[f]], axis=0).astype(jnp.float32)


def _middle_two(slabs, w9_ref):
    rows = slabs[0].shape[0] - 2
    pieces = []
    for slab in slabs:
        shifted = [_sublane_shift(slab, b - 1, 1).astype(jnp.bfloat16) for b in range(3)]
        for i in range(rows):
            pieces.append(jnp.concatenate([shifted[b][i + a] for a in range(3) for b in range(3)], axis=1))
    stacked = jnp.concatenate(pieces, axis=0)
    m = jnp.dot(stacked, w9_ref[...], preferred_element_type=jnp.float32)
    return jnp.maximum(m, 0.0).astype(jnp.bfloat16)


def _edges_two_kernel(above_ref, xp_ref, below_ref, w9_ref, edge_ref):
    frames = xp_ref.shape[0]
    plane = edge_ref.shape[1]
    m = _middle_two(
        [_slab_two(above_ref, xp_ref, below_ref, 0), _slab_two(above_ref, xp_ref, below_ref, frames - 1)], w9_ref
    )
    edge_ref[0] = m[:plane]
    edge_ref[1] = m[plane:]


def _finish(s, xp_ref, t, out_ref, slot):
    rows, width = xp_ref.shape[1], xp_ref.shape[2]
    for i in range(rows):
        v = s[i * width : (i + 1) * width] + xp_ref[t, i].astype(jnp.float32)
        out_ref[slot, i] = jnp.maximum(v, 0.0).astype(out_ref.dtype)


def _inner_two_kernel(above_ref, xp_ref, below_ref, w9_ref, t3_ref, out_ref, side_ref, mid_ref):
    frames = xp_ref.shape[0]
    plane = mid_ref.shape[1]

    def middle(g, carry):
        f = 2 * g
        m = _middle_two(
            [_slab_two(above_ref, xp_ref, below_ref, f), _slab_two(above_ref, xp_ref, below_ref, f + 1)], w9_ref
        )
        mid_ref[f] = m[:plane]
        mid_ref[f + 1] = m[plane:]
        return carry

    lax.fori_loop(0, frames // 2, middle, 0)
    side_ref[0] = mid_ref[1]
    side_ref[1] = mid_ref[frames - 2]

    def section(g, carry):
        t = 2 * g + 1
        s = None
        for k in range(3):
            pair = jnp.concatenate([mid_ref[t - 1 + k], mid_ref[t + k]], axis=0)
            d = jnp.dot(pair, t3_ref[k], preferred_element_type=jnp.float32)
            s = d if s is None else s + d
        _finish(s[:plane], xp_ref, t, out_ref, t - 1)
        _finish(s[plane:], xp_ref, t + 1, out_ref, t)
        return carry

    lax.fori_loop(0, (frames - 2) // 2, section, 0)


def _outer_two_kernel(xp_ref, t3_ref, before_ref, after_ref, edge_ref, side_ref, out_ref):
    frames = xp_ref.shape[0]
    s = jnp.dot(before_ref[0], t3_ref[0], preferred_element_type=jnp.float32)
    s = s + jnp.dot(edge_ref[0], t3_ref[1], preferred_element_type=jnp.float32)
    s = s + jnp.dot(side_ref[0], t3_ref[2], preferred_element_type=jnp.float32)
    _finish(s, xp_ref, 0, out_ref, 0)
    s = jnp.dot(side_ref[1], t3_ref[0], preferred_element_type=jnp.float32)
    s = s + jnp.dot(edge_ref[1], t3_ref[1], preferred_element_type=jnp.float32)
    s = s + jnp.dot(after_ref[0], t3_ref[2], preferred_element_type=jnp.float32)
    _finish(s, xp_ref, frames - 1, out_ref, 1)


def block_two(above, rowed, below, spatial_kernel, temporal_kernel):
    frames, rows, width, channels = rowed.shape
    mids = spatial_kernel.shape[2]
    w9 = jnp.transpose(spatial_kernel, (0, 1, 3, 2)).reshape(9 * channels, mids)
    t3 = jnp.transpose(temporal_kernel, (0, 2, 1))
    vmem = pltpu.MemorySpace.VMEM if hasattr(pltpu, "MemorySpace") else pltpu.VMEM
    params = pltpu.CompilerParams(vmem_limit_bytes=48 * 1024 * 1024)
    spec = pl.BlockSpec(memory_space=vmem)
    plane = (rows * width, mids)
    edges = pl.pallas_call(
        _edges_two_kernel,
        out_shape=jax.ShapeDtypeStruct((2,) + plane, rowed.dtype),
        in_specs=[spec] * 4,
        out_specs=spec,
        compiler_params=params,
        cost_estimate=pl.CostEstimate(
            flops=2 * 2 * rows * width * 9 * channels * mids, bytes_accessed=2 * rowed.size, transcendentals=0
        ),
    )(above, rowed, below, w9)
    before = from_behind(edges[1:], "tm", 1)
    after = from_behind(edges[:1], "tm", -1)
    inner, side = pl.pallas_call(
        _inner_two_kernel,
        out_shape=(
            jax.ShapeDtypeStruct((frames - 2, rows, width, channels), rowed.dtype),
            jax.ShapeDtypeStruct((2,) + plane, rowed.dtype),
        ),
        in_specs=[spec] * 5,
        out_specs=(spec, spec),
        scratch_shapes=[pltpu.VMEM((frames,) + plane, jnp.bfloat16)],
        compiler_params=params,
        cost_estimate=pl.CostEstimate(
            flops=2 * frames * rows * width * (9 * channels * mids + 3 * mids * channels),
            bytes_accessed=4 * rowed.size,
            transcendentals=0,
        ),
    )(above, rowed, below, w9, t3)
    outer = pl.pallas_call(
        _outer_two_kernel,
        out_shape=jax.ShapeDtypeStruct((2, rows, width, channels), rowed.dtype),
        in_specs=[spec] * 6,
        out_specs=spec,
        compiler_params=params,
    )(rowed, t3, before, after, edges, side)
    return jnp.concatenate([outer[:1], inner, outer[1:]], axis=0)


def _copy_kernel(top_ref, bottom_ref, top_out, bottom_out):
    top_out[...] = top_ref[...]
    bottom_out[...] = bottom_ref[...]


def edge_rows(block, top, bottom):
    frames, rows, channels, width = block.shape
    top_spec = pl.BlockSpec((frames, top, channels, width), lambda i: (0, rows // top - 1, 0, 0))
    bottom_spec = pl.BlockSpec((frames, bottom, channels, width), lambda i: (0, 0, 0, 0))
    return pl.pallas_call(
        _copy_kernel,
        grid=(1,),
        out_shape=(
            jax.ShapeDtypeStruct((frames, top, channels, width), block.dtype),
            jax.ShapeDtypeStruct((frames, bottom, channels, width), block.dtype),
        ),
        in_specs=[top_spec, bottom_spec],
        out_specs=(pl.BlockSpec((frames, top, channels, width), lambda i: (0, 0, 0, 0)), bottom_spec),
    )(block, block)


def on_device(video_clip, spatial_one, temporal_one, down_weight, spatial_two, temporal_two):
    rows = video_clip.shape[1]
    top, bottom = edge_rows(video_clip, 2, 1)
    above = from_behind(top, "row", 1)
    below = from_behind(bottom, "row", -1)
    keep_first = (lax.axis_index("row") > 0).astype(jnp.int32).reshape(1)
    reduced = block_one(above, video_clip, below, keep_first, spatial_one, temporal_one, down_weight)
    rows = reduced.shape[1]
    above = from_behind(reduced[:, rows - 1 :], "row", 1)
    below = from_behind(reduced[:, :1], "row", -1)
    return block_two(above, reduced, below, spatial_two, temporal_two)


def solution(mesh):
    placed = (P("tm", "row", None, None), P(), P(), P(), P(), P())
    return jax.shard_map(
        on_device, mesh=mesh, in_specs=placed, out_specs=P("tm", "row", None, None), check_vma=False
    )
```

```python
import functools

import jax
import jax.numpy as jnp
from jax import lax
from jax.experimental import pallas as pl
from jax.experimental.pallas import tpu as pltpu
from jax.sharding import PartitionSpec as P


def padded_2(block, sides, width):
    for axis, dim in sides:
        count = lax.axis_size(axis)
        forward = [(i, i + 1) for i in range(count - 1)]
        backward = [(target, source) for source, target in forward]
        low = lax.ppermute(
            lax.slice_in_dim(block, block.shape[dim] - width, None, axis=dim), axis, forward
        )
        high = lax.ppermute(lax.slice_in_dim(block, 0, width, axis=dim), axis, backward)
        block = jnp.concatenate([low, block, high], axis=dim)
    return block


def from_behind(array, axis, by):
    devices = lax.axis_size(axis)
    pairs = [(i, i + by) for i in range(devices) if 0 <= i + by < devices]
    return lax.ppermute(array, axis, pairs)


def spatial(source, kernel, layout):
    return lax.conv_general_dilated(
        source,
        kernel,
        (1, 1),
        ((0, 0), (1, 1)),
        dimension_numbers=(layout, "HWOI", layout),
        preferred_element_type=jnp.float32,
    )


def temporal(source, kernel, layout):
    return lax.conv_general_dilated(
        source,
        kernel[:, None],
        (1, 1),
        ((0, 0), (0, 0)),
        dimension_numbers=(layout, "HWOI", layout),
        preferred_element_type=jnp.float32,
    )


def residual_block(source, spatial_kernel, temporal_kernel, space_layout, time_layout):
    padded = padded_2(source, (("tm", 0), ("row", 1)), 1)
    framed = jax.nn.relu(spatial(padded, spatial_kernel, space_layout)).astype(jnp.bfloat16)
    summed = source.astype(jnp.float32) + temporal(framed, temporal_kernel, time_layout)
    return jax.nn.relu(summed).astype(jnp.bfloat16)


def _lane_shift(x, by):
    width = x.shape[-1]
    rolled = pltpu.roll(x, (-by) % width, x.ndim - 1)
    lane = lax.broadcasted_iota(jnp.int32, x.shape, x.ndim - 1)
    inside = jnp.logical_and(lane + by >= 0, lane + by < width)
    return jnp.where(inside, rolled, jnp.zeros_like(rolled))


def _middle_one(refs, f, w9_ref):
    above_ref, xp_ref, below_ref = refs
    rows = xp_ref.shape[1] + 1
    slab = jnp.concatenate([above_ref[f], xp_ref[f], below_ref[f]], axis=0).astype(jnp.float32)
    shifted = [_lane_shift(slab, b - 1).astype(jnp.bfloat16) for b in range(3)]
    parts = []
    for a in range(3):
        for b in range(3):
            parts.append(jnp.concatenate([shifted[b][h + a] for h in range(rows)], axis=1))
    stacked = jnp.concatenate(parts, axis=0)
    m = jnp.dot(w9_ref[...], stacked, preferred_element_type=jnp.float32)
    return jnp.maximum(m, 0.0).astype(jnp.bfloat16)


def _section_down(stacked, refs, t, t3_ref, wd_ref, keep_ref, out_ref, slot):
    above_ref, xp_ref, _ = refs
    rows = xp_ref.shape[1] + 1
    width = xp_ref.shape[-1]
    reduced_rows = (rows - 1) // 2
    lane = lax.broadcasted_iota(jnp.int32, (width // 2, width), 1)
    column = lax.broadcasted_iota(jnp.int32, (width // 2, width), 0)
    pick = (lane == 2 * column).astype(jnp.bfloat16)
    s = jnp.dot(t3_ref[...], stacked, preferred_element_type=jnp.float32)
    sec = []
    for h in range(rows):
        own = above_ref[t, 1] if h == 0 else xp_ref[t, h - 1]
        v = s[:, h * width : (h + 1) * width] + own.astype(jnp.float32)
        v = jnp.maximum(v, 0.0)
        if h == 0:
            v = v * keep_ref[0].astype(jnp.float32)
        sec.append(v.astype(jnp.bfloat16).astype(jnp.float32))
    shifted = [[_lane_shift(r, b - 1).astype(jnp.bfloat16) for b in range(3)] for r in sec]
    parts = []
    for a in range(3):
        for b in range(3):
            parts.append(jnp.concatenate([shifted[2 * i + a][b] for i in range(reduced_rows)], axis=1))
    stacked = jnp.concatenate(parts, axis=0)
    full = jnp.dot(wd_ref[...], stacked, preferred_element_type=jnp.float32)
    full = jnp.maximum(full, 0.0).astype(jnp.bfloat16)
    for i in range(reduced_rows):
        r = lax.dot_general(
            pick,
            full[:, i * width : (i + 1) * width],
            (((1,), (1,)), ((), ())),
            preferred_element_type=jnp.float32,
        )
        out_ref[slot, i] = r.astype(out_ref.dtype)


def _edges_one_kernel(above_ref, xp_ref, below_ref, w9_ref, edge_ref):
    refs = (above_ref, xp_ref, below_ref)
    frames = xp_ref.shape[0]
    edge_ref[0] = _middle_one(refs, 0, w9_ref)
    edge_ref[1] = _middle_one(refs, frames - 1, w9_ref)


def _inner_one_kernel(keep_ref, above_ref, xp_ref, below_ref, w9_ref, t3_ref, wd_ref, out_ref, side_ref, mid_ref):
    refs = (above_ref, xp_ref, below_ref)
    frames = xp_ref.shape[0]

    def middle(f, carry):
        mid_ref[f] = _middle_one(refs, f, w9_ref)
        return carry

    lax.fori_loop(0, frames, middle, 0)
    side_ref[0] = mid_ref[1]
    side_ref[1] = mid_ref[frames - 2]

    def section(t, carry):
        stacked = jnp.concatenate([mid_ref[t - 1], mid_ref[t], mid_ref[t + 1]], axis=0)
        _section_down(stacked, refs, t, t3_ref, wd_ref, keep_ref, out_ref, t - 1)
        return carry

    lax.fori_loop(1, frames - 1, section, 0)


def _outer_one_kernel(
    keep_ref, above_ref, xp_ref, below_ref, t3_ref, wd_ref, before_ref, after_ref, edge_ref, side_ref, out_ref
):
    refs = (above_ref, xp_ref, below_ref)
    frames = xp_ref.shape[0]
    stacked = jnp.concatenate([before_ref[0], edge_ref[0], side_ref[0]], axis=0)
    _section_down(stacked, refs, 0, t3_ref, wd_ref, keep_ref, out_ref, 0)
    stacked = jnp.concatenate([side_ref[1], edge_ref[1], after_ref[0]], axis=0)
    _section_down(stacked, refs, frames - 1, t3_ref, wd_ref, keep_ref, out_ref, 1)


def block_one(above, rowed, below, keep_first, spatial_kernel, temporal_kernel, down_kernel):
    frames, rows, channels, width = rowed.shape
    rows = rows + 1
    mids = spatial_kernel.shape[2]
    outs = down_kernel.shape[2]
    w9 = jnp.transpose(spatial_kernel, (2, 0, 1, 3)).reshape(mids, 9 * channels)
    t3 = jnp.transpose(temporal_kernel, (1, 0, 2)).reshape(channels, 3 * mids)
    wd = jnp.transpose(down_kernel, (2, 0, 1, 3)).reshape(outs, 9 * channels)
    vmem = pltpu.MemorySpace.VMEM if hasattr(pltpu, "MemorySpace") else pltpu.VMEM
    smem = pltpu.MemorySpace.SMEM if hasattr(pltpu, "MemorySpace") else pltpu.SMEM
    params = pltpu.CompilerParams(vmem_limit_bytes=48 * 1024 * 1024)
    spec = pl.BlockSpec(memory_space=vmem)
    sspec = pl.BlockSpec(memory_space=smem)
    reduced_rows = (rows - 1) // 2
    plane = (mids, rows * width)
    out_plane = (reduced_rows, width // 2, outs)
    spatial_flops = 2 * rows * width * 9 * channels * mids
    section_flops = 2 * rows * width * 3 * mids * channels + 2 * reduced_rows * width * 9 * channels * outs
    edges = pl.pallas_call(
        _edges_one_kernel,
        out_shape=jax.ShapeDtypeStruct((2,) + plane, rowed.dtype),
        in_specs=[spec] * 4,
        out_specs=spec,
        compiler_params=params,
        cost_estimate=pl.CostEstimate(flops=2 * spatial_flops, bytes_accessed=2 * rowed.size, transcendentals=0),
    )(above, rowed, below, w9)
    before = from_behind(edges[1:], "tm", 1)
    after = from_behind(edges[:1], "tm", -1)
    inner, side = pl.pallas_call(
        _inner_one_kernel,
        out_shape=(
            jax.ShapeDtypeStruct((frames - 2,) + out_plane, rowed.dtype),
            jax.ShapeDtypeStruct((2,) + plane, rowed.dtype),
        ),
        in_specs=[sspec] + [spec] * 6,
        out_specs=(spec, spec),
        scratch_shapes=[pltpu.VMEM((frames,) + plane, jnp.bfloat16)],
        compiler_params=params,
        cost_estimate=pl.CostEstimate(
            flops=frames * (spatial_flops + section_flops), bytes_accessed=4 * rowed.size, transcendentals=0
        ),
    )(keep_first, above, rowed, below, w9, t3, wd)
    outer = pl.pallas_call(
        _outer_one_kernel,
        out_shape=jax.ShapeDtypeStruct((2,) + out_plane, rowed.dtype),
        in_specs=[sspec] + [spec] * 9,
        out_specs=spec,
        compiler_params=params,
    )(keep_first, above, rowed, below, t3, wd, before, after, edges, side)
    return jnp.concatenate([outer[:1], inner, outer[1:]], axis=0)


def _sublane_shift(x, by, axis):
    size = x.shape[axis]
    rolled = pltpu.roll(x, (-by) % size, axis)
    index = lax.broadcasted_iota(jnp.int32, x.shape, axis)
    inside = jnp.logical_and(index + by >= 0, index + by < size)
    return jnp.where(inside, rolled, jnp.zeros_like(rolled))


def _slab_two(above_ref, xp_ref, below_ref, f):
    return jnp.concatenate([above_ref[f], xp_ref[f], below_ref[f]], axis=0).astype(jnp.float32)


def _middle_two(slabs, w9_ref):
    rows = slabs[0].shape[0] - 2
    pieces = []
    for slab in slabs:
        shifted = [_sublane_shift(slab, b - 1, 1).astype(jnp.bfloat16) for b in range(3)]
        for i in range(rows):
            pieces.append(jnp.concatenate([shifted[b][i + a] for a in range(3) for b in range(3)], axis=1))
    stacked = jnp.concatenate(pieces, axis=0)
    m = jnp.dot(stacked, w9_ref[...], preferred_element_type=jnp.float32)
    return jnp.maximum(m, 0.0).astype(jnp.bfloat16)


def _edges_two_kernel(above_ref, xp_ref, below_ref, w9_ref, edge_ref):
    frames = xp_ref.shape[0]
    plane = edge_ref.shape[1]
    m = _middle_two(
        [_slab_two(above_ref, xp_ref, below_ref, 0), _slab_two(above_ref, xp_ref, below_ref, frames - 1)], w9_ref
    )
    edge_ref[0] = m[:plane]
    edge_ref[1] = m[plane:]


def _finish(s, xp_ref, t, out_ref, slot):
    rows, width = xp_ref.shape[1], xp_ref.shape[2]
    for i in range(rows):
        v = s[i * width : (i + 1) * width] + xp_ref[t, i].astype(jnp.float32)
        out_ref[slot, i] = jnp.maximum(v, 0.0).astype(out_ref.dtype)


def _inner_two_kernel(above_ref, xp_ref, below_ref, w9_ref, t3_ref, out_ref, side_ref, mid_ref):
    frames = xp_ref.shape[0]
    plane = mid_ref.shape[1]

    group = 4 if frames % 4 == 0 else 2

    def middle(g, carry):
        f = group * g
        m = _middle_two([_slab_two(above_ref, xp_ref, below_ref, f + k) for k in range(group)], w9_ref)
        for k in range(group):
            mid_ref[f + k] = m[k * plane : (k + 1) * plane]
        return carry

    lax.fori_loop(0, frames // group, middle, 0)
    side_ref[0] = mid_ref[1]
    side_ref[1] = mid_ref[frames - 2]

    def section(g, carry):
        t = 2 * g + 1
        s = None
        for k in range(3):
            pair = jnp.concatenate([mid_ref[t - 1 + k], mid_ref[t + k]], axis=0)
            d = jnp.dot(pair, t3_ref[k], preferred_element_type=jnp.float32)
            s = d if s is None else s + d
        _finish(s[:plane], xp_ref, t, out_ref, t - 1)
        _finish(s[plane:], xp_ref, t + 1, out_ref, t)
        return carry

    lax.fori_loop(0, (frames - 2) // 2, section, 0)


def _outer_two_kernel(xp_ref, t3_ref, before_ref, after_ref, edge_ref, side_ref, out_ref):
    frames = xp_ref.shape[0]
    s = jnp.dot(before_ref[0], t3_ref[0], preferred_element_type=jnp.float32)
    s = s + jnp.dot(edge_ref[0], t3_ref[1], preferred_element_type=jnp.float32)
    s = s + jnp.dot(side_ref[0], t3_ref[2], preferred_element_type=jnp.float32)
    _finish(s, xp_ref, 0, out_ref, 0)
    s = jnp.dot(side_ref[1], t3_ref[0], preferred_element_type=jnp.float32)
    s = s + jnp.dot(edge_ref[1], t3_ref[1], preferred_element_type=jnp.float32)
    s = s + jnp.dot(after_ref[0], t3_ref[2], preferred_element_type=jnp.float32)
    _finish(s, xp_ref, frames - 1, out_ref, 1)


def block_two(above, rowed, below, spatial_kernel, temporal_kernel):
    frames, rows, width, channels = rowed.shape
    mids = spatial_kernel.shape[2]
    w9 = jnp.transpose(spatial_kernel, (0, 1, 3, 2)).reshape(9 * channels, mids)
    t3 = jnp.transpose(temporal_kernel, (0, 2, 1))
    vmem = pltpu.MemorySpace.VMEM if hasattr(pltpu, "MemorySpace") else pltpu.VMEM
    params = pltpu.CompilerParams(vmem_limit_bytes=48 * 1024 * 1024)
    spec = pl.BlockSpec(memory_space=vmem)
    plane = (rows * width, mids)
    edges = pl.pallas_call(
        _edges_two_kernel,
        out_shape=jax.ShapeDtypeStruct((2,) + plane, rowed.dtype),
        in_specs=[spec] * 4,
        out_specs=spec,
        compiler_params=params,
        cost_estimate=pl.CostEstimate(
            flops=2 * 2 * rows * width * 9 * channels * mids, bytes_accessed=2 * rowed.size, transcendentals=0
        ),
    )(above, rowed, below, w9)
    before = from_behind(edges[1:], "tm", 1)
    after = from_behind(edges[:1], "tm", -1)
    inner, side = pl.pallas_call(
        _inner_two_kernel,
        out_shape=(
            jax.ShapeDtypeStruct((frames - 2, rows, width, channels), rowed.dtype),
            jax.ShapeDtypeStruct((2,) + plane, rowed.dtype),
        ),
        in_specs=[spec] * 5,
        out_specs=(spec, spec),
        scratch_shapes=[pltpu.VMEM((frames,) + plane, jnp.bfloat16)],
        compiler_params=params,
        cost_estimate=pl.CostEstimate(
            flops=2 * frames * rows * width * (9 * channels * mids + 3 * mids * channels),
            bytes_accessed=4 * rowed.size,
            transcendentals=0,
        ),
    )(above, rowed, below, w9, t3)
    outer = pl.pallas_call(
        _outer_two_kernel,
        out_shape=jax.ShapeDtypeStruct((2, rows, width, channels), rowed.dtype),
        in_specs=[spec] * 6,
        out_specs=spec,
        compiler_params=params,
    )(rowed, t3, before, after, edges, side)
    return jnp.concatenate([outer[:1], inner, outer[1:]], axis=0)


def _copy_kernel(top_ref, bottom_ref, top_out, bottom_out):
    top_out[...] = top_ref[...]
    bottom_out[...] = bottom_ref[...]


def edge_rows(block, top, bottom):
    frames, rows, channels, width = block.shape
    top_spec = pl.BlockSpec((frames, top, channels, width), lambda i: (0, rows // top - 1, 0, 0))
    bottom_spec = pl.BlockSpec((frames, bottom, channels, width), lambda i: (0, 0, 0, 0))
    return pl.pallas_call(
        _copy_kernel,
        grid=(1,),
        out_shape=(
            jax.ShapeDtypeStruct((frames, top, channels, width), block.dtype),
            jax.ShapeDtypeStruct((frames, bottom, channels, width), block.dtype),
        ),
        in_specs=[top_spec, bottom_spec],
        out_specs=(pl.BlockSpec((frames, top, channels, width), lambda i: (0, 0, 0, 0)), bottom_spec),
    )(block, block)


def on_device(video_clip, spatial_one, temporal_one, down_weight, spatial_two, temporal_two):
    rows = video_clip.shape[1]
    top, bottom = edge_rows(video_clip, 2, 1)
    above = from_behind(top, "row", 1)
    below = from_behind(bottom, "row", -1)
    keep_first = (lax.axis_index("row") > 0).astype(jnp.int32).reshape(1)
    reduced = block_one(above, video_clip, below, keep_first, spatial_one, temporal_one, down_weight)
    rows = reduced.shape[1]
    above = from_behind(reduced[:, rows - 1 :], "row", 1)
    below = from_behind(reduced[:, :1], "row", -1)
    return block_two(above, reduced, below, spatial_two, temporal_two)


def solution(mesh):
    placed = (P("tm", "row", None, None), P(), P(), P(), P(), P())
    return jax.shard_map(
        on_device, mesh=mesh, in_specs=placed, out_specs=P("tm", "row", None, None), check_vma=False
    )
```

```python
import functools

import jax
import jax.numpy as jnp
from jax import lax
from jax.experimental import pallas as pl
from jax.experimental.pallas import tpu as pltpu
from jax.sharding import PartitionSpec as P


def padded_2(block, sides, width):
    for axis, dim in sides:
        count = lax.axis_size(axis)
        forward = [(i, i + 1) for i in range(count - 1)]
        backward = [(target, source) for source, target in forward]
        low = lax.ppermute(
            lax.slice_in_dim(block, block.shape[dim] - width, None, axis=dim), axis, forward
        )
        high = lax.ppermute(lax.slice_in_dim(block, 0, width, axis=dim), axis, backward)
        block = jnp.concatenate([low, block, high], axis=dim)
    return block


def from_behind(array, axis, by):
    devices = lax.axis_size(axis)
    pairs = [(i, i + by) for i in range(devices) if 0 <= i + by < devices]
    return lax.ppermute(array, axis, pairs)


def spatial(source, kernel, layout):
    return lax.conv_general_dilated(
        source,
        kernel,
        (1, 1),
        ((0, 0), (1, 1)),
        dimension_numbers=(layout, "HWOI", layout),
        preferred_element_type=jnp.float32,
    )


def temporal(source, kernel, layout):
    return lax.conv_general_dilated(
        source,
        kernel[:, None],
        (1, 1),
        ((0, 0), (0, 0)),
        dimension_numbers=(layout, "HWOI", layout),
        preferred_element_type=jnp.float32,
    )


def residual_block(source, spatial_kernel, temporal_kernel, space_layout, time_layout):
    padded = padded_2(source, (("tm", 0), ("row", 1)), 1)
    framed = jax.nn.relu(spatial(padded, spatial_kernel, space_layout)).astype(jnp.bfloat16)
    summed = source.astype(jnp.float32) + temporal(framed, temporal_kernel, time_layout)
    return jax.nn.relu(summed).astype(jnp.bfloat16)


def _lane_shift(x, by):
    width = x.shape[-1]
    rolled = pltpu.roll(x, (-by) % width, x.ndim - 1)
    lane = lax.broadcasted_iota(jnp.int32, x.shape, x.ndim - 1)
    inside = jnp.logical_and(lane + by >= 0, lane + by < width)
    return jnp.where(inside, rolled, jnp.zeros_like(rolled))


def _middle_one(refs, f, w9_ref):
    above_ref, xp_ref, below_ref = refs
    rows = xp_ref.shape[1] + 1
    slab = jnp.concatenate([above_ref[f], xp_ref[f], below_ref[f]], axis=0).astype(jnp.float32)
    shifted = [_lane_shift(slab, b - 1).astype(jnp.bfloat16) for b in range(3)]
    parts = []
    for a in range(3):
        for b in range(3):
            parts.append(jnp.concatenate([shifted[b][h + a] for h in range(rows)], axis=1))
    stacked = jnp.concatenate(parts, axis=0)
    m = jnp.dot(w9_ref[...], stacked, preferred_element_type=jnp.float32)
    return jnp.maximum(m, 0.0).astype(jnp.bfloat16)


def _section_down(stacked, refs, t, t3_ref, wd_ref, keep_ref, out_ref, slot, full_ref):
    above_ref, xp_ref, _ = refs
    rows = xp_ref.shape[1] + 1
    width = xp_ref.shape[-1]
    reduced_rows = (rows - 1) // 2
    s = jnp.dot(t3_ref[...], stacked, preferred_element_type=jnp.float32)
    sec = []
    for h in range(rows):
        own = above_ref[t, 1] if h == 0 else xp_ref[t, h - 1]
        v = s[:, h * width : (h + 1) * width] + own.astype(jnp.float32)
        v = jnp.maximum(v, 0.0)
        if h == 0:
            v = v * keep_ref[0].astype(jnp.float32)
        sec.append(v.astype(jnp.bfloat16).astype(jnp.float32))
    shifted = [[_lane_shift(r, b - 1).astype(jnp.bfloat16) for b in range(3)] for r in sec]
    parts = []
    for a in range(3):
        for b in range(3):
            parts.append(jnp.concatenate([shifted[2 * i + a][b] for i in range(reduced_rows)], axis=1))
    stacked = jnp.concatenate(parts, axis=0)
    full = lax.dot_general(stacked, wd_ref[...], (((0,), (0,)), ((), ())), preferred_element_type=jnp.float32)
    full_ref[...] = jnp.maximum(full, 0.0)
    for i in range(reduced_rows):
        picked = full_ref[pl.ds(i * width, width // 2, stride=2), :]
        out_ref[slot, i] = picked.astype(out_ref.dtype)


def _edges_one_kernel(above_ref, xp_ref, below_ref, w9_ref, edge_ref):
    refs = (above_ref, xp_ref, below_ref)
    frames = xp_ref.shape[0]
    edge_ref[0] = _middle_one(refs, 0, w9_ref)
    edge_ref[1] = _middle_one(refs, frames - 1, w9_ref)


def _inner_one_kernel(
    keep_ref, above_ref, xp_ref, below_ref, w9_ref, t3_ref, wd_ref, out_ref, side_ref, mid_ref, full_ref
):
    refs = (above_ref, xp_ref, below_ref)
    frames = xp_ref.shape[0]

    def middle(f, carry):
        mid_ref[f] = _middle_one(refs, f, w9_ref)
        return carry

    lax.fori_loop(0, frames, middle, 0)
    side_ref[0] = mid_ref[1]
    side_ref[1] = mid_ref[frames - 2]

    def section(t, carry):
        stacked = jnp.concatenate([mid_ref[t - 1], mid_ref[t], mid_ref[t + 1]], axis=0)
        _section_down(stacked, refs, t, t3_ref, wd_ref, keep_ref, out_ref, t - 1, full_ref)
        return carry

    lax.fori_loop(1, frames - 1, section, 0)


def _outer_one_kernel(
    keep_ref, above_ref, xp_ref, below_ref, t3_ref, wd_ref, before_ref, after_ref, edge_ref, side_ref, out_ref, full_ref
):
    refs = (above_ref, xp_ref, below_ref)
    frames = xp_ref.shape[0]
    stacked = jnp.concatenate([before_ref[0], edge_ref[0], side_ref[0]], axis=0)
    _section_down(stacked, refs, 0, t3_ref, wd_ref, keep_ref, out_ref, 0, full_ref)
    stacked = jnp.concatenate([side_ref[1], edge_ref[1], after_ref[0]], axis=0)
    _section_down(stacked, refs, frames - 1, t3_ref, wd_ref, keep_ref, out_ref, 1, full_ref)


def block_one(above, rowed, below, keep_first, spatial_kernel, temporal_kernel, down_kernel):
    frames, rows, channels, width = rowed.shape
    rows = rows + 1
    mids = spatial_kernel.shape[2]
    outs = down_kernel.shape[2]
    w9 = jnp.transpose(spatial_kernel, (2, 0, 1, 3)).reshape(mids, 9 * channels)
    t3 = jnp.transpose(temporal_kernel, (1, 0, 2)).reshape(channels, 3 * mids)
    wd = jnp.transpose(down_kernel, (0, 1, 3, 2)).reshape(9 * channels, outs)
    vmem = pltpu.MemorySpace.VMEM if hasattr(pltpu, "MemorySpace") else pltpu.VMEM
    smem = pltpu.MemorySpace.SMEM if hasattr(pltpu, "MemorySpace") else pltpu.SMEM
    params = pltpu.CompilerParams(vmem_limit_bytes=48 * 1024 * 1024)
    spec = pl.BlockSpec(memory_space=vmem)
    sspec = pl.BlockSpec(memory_space=smem)
    reduced_rows = (rows - 1) // 2
    plane = (mids, rows * width)
    out_plane = (reduced_rows, width // 2, outs)
    spatial_flops = 2 * rows * width * 9 * channels * mids
    section_flops = 2 * rows * width * 3 * mids * channels + 2 * reduced_rows * width * 9 * channels * outs
    edges = pl.pallas_call(
        _edges_one_kernel,
        out_shape=jax.ShapeDtypeStruct((2,) + plane, rowed.dtype),
        in_specs=[spec] * 4,
        out_specs=spec,
        compiler_params=params,
        cost_estimate=pl.CostEstimate(flops=2 * spatial_flops, bytes_accessed=2 * rowed.size, transcendentals=0),
    )(above, rowed, below, w9)
    before = from_behind(edges[1:], "tm", 1)
    after = from_behind(edges[:1], "tm", -1)
    inner, side = pl.pallas_call(
        _inner_one_kernel,
        out_shape=(
            jax.ShapeDtypeStruct((frames - 2,) + out_plane, rowed.dtype),
            jax.ShapeDtypeStruct((2,) + plane, rowed.dtype),
        ),
        in_specs=[sspec] + [spec] * 6,
        out_specs=(spec, spec),
        scratch_shapes=[pltpu.VMEM((frames,) + plane, jnp.bfloat16), pltpu.VMEM((reduced_rows * width, outs), jnp.float32)],
        compiler_params=params,
        cost_estimate=pl.CostEstimate(
            flops=frames * (spatial_flops + section_flops), bytes_accessed=4 * rowed.size, transcendentals=0
        ),
    )(keep_first, above, rowed, below, w9, t3, wd)
    outer = pl.pallas_call(
        _outer_one_kernel,
        out_shape=jax.ShapeDtypeStruct((2,) + out_plane, rowed.dtype),
        in_specs=[sspec] + [spec] * 9,
        out_specs=spec,
        scratch_shapes=[pltpu.VMEM((reduced_rows * width, outs), jnp.float32)],
        compiler_params=params,
    )(keep_first, above, rowed, below, t3, wd, before, after, edges, side)
    return jnp.concatenate([outer[:1], inner, outer[1:]], axis=0)


def _sublane_shift(x, by, axis):
    size = x.shape[axis]
    rolled = pltpu.roll(x, (-by) % size, axis)
    index = lax.broadcasted_iota(jnp.int32, x.shape, axis)
    inside = jnp.logical_and(index + by >= 0, index + by < size)
    return jnp.where(inside, rolled, jnp.zeros_like(rolled))


def _slab_two(above_ref, xp_ref, below_ref, f):
    return jnp.concatenate([above_ref[f], xp_ref[f], below_ref[f]], axis=0).astype(jnp.float32)


def _middle_two(slabs, w9_ref):
    rows = slabs[0].shape[0] - 2
    pieces = []
    for slab in slabs:
        shifted = [_sublane_shift(slab, b - 1, 1).astype(jnp.bfloat16) for b in range(3)]
        for i in range(rows):
            pieces.append(jnp.concatenate([shifted[b][i + a] for a in range(3) for b in range(3)], axis=1))
    stacked = jnp.concatenate(pieces, axis=0)
    m = jnp.dot(stacked, w9_ref[...], preferred_element_type=jnp.float32)
    return jnp.maximum(m, 0.0).astype(jnp.bfloat16)


def _edges_two_kernel(above_ref, xp_ref, below_ref, w9_ref, edge_ref):
    frames = xp_ref.shape[0]
    plane = edge_ref.shape[1]
    m = _middle_two(
        [_slab_two(above_ref, xp_ref, below_ref, 0), _slab_two(above_ref, xp_ref, below_ref, frames - 1)], w9_ref
    )
    edge_ref[0] = m[:plane]
    edge_ref[1] = m[plane:]


def _finish(s, xp_ref, t, out_ref, slot):
    rows, width = xp_ref.shape[1], xp_ref.shape[2]
    for i in range(rows):
        v = s[i * width : (i + 1) * width] + xp_ref[t, i].astype(jnp.float32)
        out_ref[slot, i] = jnp.maximum(v, 0.0).astype(out_ref.dtype)


def _inner_two_kernel(above_ref, xp_ref, below_ref, w9_ref, t3_ref, out_ref, side_ref, mid_ref):
    frames = xp_ref.shape[0]
    plane = mid_ref.shape[1]

    group = 4 if frames % 4 == 0 else 2

    def middle(g, carry):
        f = group * g
        m = _middle_two([_slab_two(above_ref, xp_ref, below_ref, f + k) for k in range(group)], w9_ref)
        for k in range(group):
            mid_ref[f + k] = m[k * plane : (k + 1) * plane]
        return carry

    lax.fori_loop(0, frames // group, middle, 0)
    side_ref[0] = mid_ref[1]
    side_ref[1] = mid_ref[frames - 2]

    def section(g, carry):
        t = 2 * g + 1
        s = None
        for k in range(3):
            pair = jnp.concatenate([mid_ref[t - 1 + k], mid_ref[t + k]], axis=0)
            d = jnp.dot(pair, t3_ref[k], preferred_element_type=jnp.float32)
            s = d if s is None else s + d
        _finish(s[:plane], xp_ref, t, out_ref, t - 1)
        _finish(s[plane:], xp_ref, t + 1, out_ref, t)
        return carry

    lax.fori_loop(0, (frames - 2) // 2, section, 0)


def _outer_two_kernel(xp_ref, t3_ref, before_ref, after_ref, edge_ref, side_ref, out_ref):
    frames = xp_ref.shape[0]
    s = jnp.dot(before_ref[0], t3_ref[0], preferred_element_type=jnp.float32)
    s = s + jnp.dot(edge_ref[0], t3_ref[1], preferred_element_type=jnp.float32)
    s = s + jnp.dot(side_ref[0], t3_ref[2], preferred_element_type=jnp.float32)
    _finish(s, xp_ref, 0, out_ref, 0)
    s = jnp.dot(side_ref[1], t3_ref[0], preferred_element_type=jnp.float32)
    s = s + jnp.dot(edge_ref[1], t3_ref[1], preferred_element_type=jnp.float32)
    s = s + jnp.dot(after_ref[0], t3_ref[2], preferred_element_type=jnp.float32)
    _finish(s, xp_ref, frames - 1, out_ref, 1)


def block_two(above, rowed, below, spatial_kernel, temporal_kernel):
    frames, rows, width, channels = rowed.shape
    mids = spatial_kernel.shape[2]
    w9 = jnp.transpose(spatial_kernel, (0, 1, 3, 2)).reshape(9 * channels, mids)
    t3 = jnp.transpose(temporal_kernel, (0, 2, 1))
    vmem = pltpu.MemorySpace.VMEM if hasattr(pltpu, "MemorySpace") else pltpu.VMEM
    params = pltpu.CompilerParams(vmem_limit_bytes=48 * 1024 * 1024)
    spec = pl.BlockSpec(memory_space=vmem)
    plane = (rows * width, mids)
    edges = pl.pallas_call(
        _edges_two_kernel,
        out_shape=jax.ShapeDtypeStruct((2,) + plane, rowed.dtype),
        in_specs=[spec] * 4,
        out_specs=spec,
        compiler_params=params,
        cost_estimate=pl.CostEstimate(
            flops=2 * 2 * rows * width * 9 * channels * mids, bytes_accessed=2 * rowed.size, transcendentals=0
        ),
    )(above, rowed, below, w9)
    before = from_behind(edges[1:], "tm", 1)
    after = from_behind(edges[:1], "tm", -1)
    inner, side = pl.pallas_call(
        _inner_two_kernel,
        out_shape=(
            jax.ShapeDtypeStruct((frames - 2, rows, width, channels), rowed.dtype),
            jax.ShapeDtypeStruct((2,) + plane, rowed.dtype),
        ),
        in_specs=[spec] * 5,
        out_specs=(spec, spec),
        scratch_shapes=[pltpu.VMEM((frames,) + plane, jnp.bfloat16)],
        compiler_params=params,
        cost_estimate=pl.CostEstimate(
            flops=2 * frames * rows * width * (9 * channels * mids + 3 * mids * channels),
            bytes_accessed=4 * rowed.size,
            transcendentals=0,
        ),
    )(above, rowed, below, w9, t3)
    outer = pl.pallas_call(
        _outer_two_kernel,
        out_shape=jax.ShapeDtypeStruct((2, rows, width, channels), rowed.dtype),
        in_specs=[spec] * 6,
        out_specs=spec,
        compiler_params=params,
    )(rowed, t3, before, after, edges, side)
    return jnp.concatenate([outer[:1], inner, outer[1:]], axis=0)


def _copy_kernel(top_ref, bottom_ref, top_out, bottom_out):
    top_out[...] = top_ref[...]
    bottom_out[...] = bottom_ref[...]


def edge_rows(block, top, bottom):
    frames, rows, channels, width = block.shape
    top_spec = pl.BlockSpec((frames, top, channels, width), lambda i: (0, rows // top - 1, 0, 0))
    bottom_spec = pl.BlockSpec((frames, bottom, channels, width), lambda i: (0, 0, 0, 0))
    return pl.pallas_call(
        _copy_kernel,
        grid=(1,),
        out_shape=(
            jax.ShapeDtypeStruct((frames, top, channels, width), block.dtype),
            jax.ShapeDtypeStruct((frames, bottom, channels, width), block.dtype),
        ),
        in_specs=[top_spec, bottom_spec],
        out_specs=(pl.BlockSpec((frames, top, channels, width), lambda i: (0, 0, 0, 0)), bottom_spec),
    )(block, block)


def on_device(video_clip, spatial_one, temporal_one, down_weight, spatial_two, temporal_two):
    rows = video_clip.shape[1]
    top, bottom = edge_rows(video_clip, 2, 1)
    above = from_behind(top, "row", 1)
    below = from_behind(bottom, "row", -1)
    keep_first = (lax.axis_index("row") > 0).astype(jnp.int32).reshape(1)
    reduced = block_one(above, video_clip, below, keep_first, spatial_one, temporal_one, down_weight)
    rows = reduced.shape[1]
    above = from_behind(reduced[:, rows - 1 :], "row", 1)
    below = from_behind(reduced[:, :1], "row", -1)
    return block_two(above, reduced, below, spatial_two, temporal_two)


def solution(mesh):
    placed = (P("tm", "row", None, None), P(), P(), P(), P(), P())
    return jax.shard_map(
        on_device, mesh=mesh, in_specs=placed, out_specs=P("tm", "row", None, None), check_vma=False
    )
```

```python
import functools

import jax
import jax.numpy as jnp
from jax import lax
from jax.experimental import pallas as pl
from jax.experimental.pallas import tpu as pltpu
from jax.sharding import PartitionSpec as P


def padded_2(block, sides, width):
    for axis, dim in sides:
        count = lax.axis_size(axis)
        forward = [(i, i + 1) for i in range(count - 1)]
        backward = [(target, source) for source, target in forward]
        low = lax.ppermute(
            lax.slice_in_dim(block, block.shape[dim] - width, None, axis=dim), axis, forward
        )
        high = lax.ppermute(lax.slice_in_dim(block, 0, width, axis=dim), axis, backward)
        block = jnp.concatenate([low, block, high], axis=dim)
    return block


def from_behind(array, axis, by):
    devices = lax.axis_size(axis)
    pairs = [(i, i + by) for i in range(devices) if 0 <= i + by < devices]
    return lax.ppermute(array, axis, pairs)


def spatial(source, kernel, layout):
    return lax.conv_general_dilated(
        source,
        kernel,
        (1, 1),
        ((0, 0), (1, 1)),
        dimension_numbers=(layout, "HWOI", layout),
        preferred_element_type=jnp.float32,
    )


def temporal(source, kernel, layout):
    return lax.conv_general_dilated(
        source,
        kernel[:, None],
        (1, 1),
        ((0, 0), (0, 0)),
        dimension_numbers=(layout, "HWOI", layout),
        preferred_element_type=jnp.float32,
    )


def residual_block(source, spatial_kernel, temporal_kernel, space_layout, time_layout):
    padded = padded_2(source, (("tm", 0), ("row", 1)), 1)
    framed = jax.nn.relu(spatial(padded, spatial_kernel, space_layout)).astype(jnp.bfloat16)
    summed = source.astype(jnp.float32) + temporal(framed, temporal_kernel, time_layout)
    return jax.nn.relu(summed).astype(jnp.bfloat16)


def _lane_shift(x, by):
    width = x.shape[-1]
    rolled = pltpu.roll(x, (-by) % width, x.ndim - 1)
    lane = lax.broadcasted_iota(jnp.int32, x.shape, x.ndim - 1)
    inside = jnp.logical_and(lane + by >= 0, lane + by < width)
    return jnp.where(inside, rolled, jnp.zeros_like(rolled))


def _middle_one(refs, f, w9_ref):
    above_ref, xp_ref, below_ref = refs
    rows = xp_ref.shape[1] + 1
    slab = jnp.concatenate([above_ref[f], xp_ref[f], below_ref[f]], axis=0).astype(jnp.float32)
    shifted = [_lane_shift(slab, b - 1).astype(jnp.bfloat16) for b in range(3)]
    parts = []
    for a in range(3):
        for b in range(3):
            parts.append(jnp.concatenate([shifted[b][h + a] for h in range(rows)], axis=1))
    stacked = jnp.concatenate(parts, axis=0)
    m = jnp.dot(w9_ref[...], stacked, preferred_element_type=jnp.float32)
    return jnp.maximum(m, 0.0).astype(jnp.bfloat16)


def _section_down(stacked, refs, t, t3_ref, wd_ref, keep_ref, out_ref, slot):
    s = jnp.dot(t3_ref[...], stacked, preferred_element_type=jnp.float32)
    _down(s, refs, t, wd_ref, keep_ref, out_ref, slot)


def _down(s, refs, t, wd_ref, keep_ref, out_ref, slot):
    above_ref, xp_ref, _ = refs
    rows = xp_ref.shape[1] + 1
    width = xp_ref.shape[-1]
    reduced_rows = (rows - 1) // 2
    lane = lax.broadcasted_iota(jnp.int32, (width // 2, width), 1)
    column = lax.broadcasted_iota(jnp.int32, (width // 2, width), 0)
    pick = (lane == 2 * column).astype(jnp.bfloat16)
    sec = []
    for h in range(rows):
        own = above_ref[t, 1] if h == 0 else xp_ref[t, h - 1]
        v = s[:, h * width : (h + 1) * width] + own.astype(jnp.float32)
        v = jnp.maximum(v, 0.0)
        if h == 0:
            v = v * keep_ref[0].astype(jnp.float32)
        sec.append(v.astype(jnp.bfloat16).astype(jnp.float32))
    shifted = [[_lane_shift(r, b - 1).astype(jnp.bfloat16) for b in range(3)] for r in sec]
    parts = []
    for a in range(3):
        for b in range(3):
            parts.append(jnp.concatenate([shifted[2 * i + a][b] for i in range(reduced_rows)], axis=1))
    stacked = jnp.concatenate(parts, axis=0)
    full = jnp.dot(wd_ref[...], stacked, preferred_element_type=jnp.float32)
    full = jnp.maximum(full, 0.0).astype(jnp.bfloat16)
    for i in range(reduced_rows):
        r = lax.dot_general(
            pick,
            full[:, i * width : (i + 1) * width],
            (((1,), (1,)), ((), ())),
            preferred_element_type=jnp.float32,
        )
        out_ref[slot, i] = r.astype(out_ref.dtype)


def _edges_one_kernel(above_ref, xp_ref, below_ref, w9_ref, edge_ref):
    refs = (above_ref, xp_ref, below_ref)
    frames = xp_ref.shape[0]
    edge_ref[0] = _middle_one(refs, 0, w9_ref)
    edge_ref[1] = _middle_one(refs, frames - 1, w9_ref)


def _inner_one_kernel(keep_ref, above_ref, xp_ref, below_ref, w9_ref, t3_ref, wd_ref, out_ref, side_ref, mid_ref):
    refs = (above_ref, xp_ref, below_ref)
    frames = xp_ref.shape[0]

    def middle(f, carry):
        mid_ref[f] = _middle_one(refs, f, w9_ref)
        return carry

    lax.fori_loop(0, frames, middle, 0)
    side_ref[0] = mid_ref[1]
    side_ref[1] = mid_ref[frames - 2]

    channels = t3_ref.shape[0] // 2

    def section(g, carry):
        t = 2 * g + 1
        stacked = jnp.concatenate([mid_ref[t - 1], mid_ref[t], mid_ref[t + 1], mid_ref[t + 2]], axis=0)
        s = jnp.dot(t3_ref[...], stacked, preferred_element_type=jnp.float32)
        _down(s[:channels], refs, t, wd_ref, keep_ref, out_ref, t - 1)
        _down(s[channels:], refs, t + 1, wd_ref, keep_ref, out_ref, t)
        return carry

    lax.fori_loop(0, (frames - 2) // 2, section, 0)


def _outer_one_kernel(
    keep_ref, above_ref, xp_ref, below_ref, t3_ref, wd_ref, before_ref, after_ref, edge_ref, side_ref, out_ref
):
    refs = (above_ref, xp_ref, below_ref)
    frames = xp_ref.shape[0]
    stacked = jnp.concatenate([before_ref[0], edge_ref[0], side_ref[0]], axis=0)
    _section_down(stacked, refs, 0, t3_ref, wd_ref, keep_ref, out_ref, 0)
    stacked = jnp.concatenate([side_ref[1], edge_ref[1], after_ref[0]], axis=0)
    _section_down(stacked, refs, frames - 1, t3_ref, wd_ref, keep_ref, out_ref, 1)


def block_one(above, rowed, below, keep_first, spatial_kernel, temporal_kernel, down_kernel):
    frames, rows, channels, width = rowed.shape
    rows = rows + 1
    mids = spatial_kernel.shape[2]
    outs = down_kernel.shape[2]
    w9 = jnp.transpose(spatial_kernel, (2, 0, 1, 3)).reshape(mids, 9 * channels)
    t3 = jnp.transpose(temporal_kernel, (1, 0, 2)).reshape(channels, 3 * mids)
    wd = jnp.transpose(down_kernel, (2, 0, 1, 3)).reshape(outs, 9 * channels)
    gap = jnp.zeros((channels, mids), t3.dtype)
    t4 = jnp.concatenate(
        [jnp.concatenate([t3, gap], axis=1), jnp.concatenate([gap, t3], axis=1)], axis=0
    )
    vmem = pltpu.MemorySpace.VMEM if hasattr(pltpu, "MemorySpace") else pltpu.VMEM
    smem = pltpu.MemorySpace.SMEM if hasattr(pltpu, "MemorySpace") else pltpu.SMEM
    params = pltpu.CompilerParams(vmem_limit_bytes=48 * 1024 * 1024)
    spec = pl.BlockSpec(memory_space=vmem)
    sspec = pl.BlockSpec(memory_space=smem)
    reduced_rows = (rows - 1) // 2
    plane = (mids, rows * width)
    out_plane = (reduced_rows, width // 2, outs)
    spatial_flops = 2 * rows * width * 9 * channels * mids
    section_flops = 2 * rows * width * 3 * mids * channels + 2 * reduced_rows * width * 9 * channels * outs
    edges = pl.pallas_call(
        _edges_one_kernel,
        out_shape=jax.ShapeDtypeStruct((2,) + plane, rowed.dtype),
        in_specs=[spec] * 4,
        out_specs=spec,
        compiler_params=params,
        cost_estimate=pl.CostEstimate(flops=2 * spatial_flops, bytes_accessed=2 * rowed.size, transcendentals=0),
    )(above, rowed, below, w9)
    before = from_behind(edges[1:], "tm", 1)
    after = from_behind(edges[:1], "tm", -1)
    inner, side = pl.pallas_call(
        _inner_one_kernel,
        out_shape=(
            jax.ShapeDtypeStruct((frames - 2,) + out_plane, rowed.dtype),
            jax.ShapeDtypeStruct((2,) + plane, rowed.dtype),
        ),
        in_specs=[sspec] + [spec] * 6,
        out_specs=(spec, spec),
        scratch_shapes=[pltpu.VMEM((frames,) + plane, jnp.bfloat16)],
        compiler_params=params,
        cost_estimate=pl.CostEstimate(
            flops=frames * (spatial_flops + section_flops), bytes_accessed=4 * rowed.size, transcendentals=0
        ),
    )(keep_first, above, rowed, below, w9, t4, wd)
    outer = pl.pallas_call(
        _outer_one_kernel,
        out_shape=jax.ShapeDtypeStruct((2,) + out_plane, rowed.dtype),
        in_specs=[sspec] + [spec] * 9,
        out_specs=spec,
        compiler_params=params,
    )(keep_first, above, rowed, below, t3, wd, before, after, edges, side)
    return jnp.concatenate([outer[:1], inner, outer[1:]], axis=0)


def _sublane_shift(x, by, axis):
    size = x.shape[axis]
    rolled = pltpu.roll(x, (-by) % size, axis)
    index = lax.broadcasted_iota(jnp.int32, x.shape, axis)
    inside = jnp.logical_and(index + by >= 0, index + by < size)
    return jnp.where(inside, rolled, jnp.zeros_like(rolled))


def _slab_two(above_ref, xp_ref, below_ref, f):
    return jnp.concatenate([above_ref[f], xp_ref[f], below_ref[f]], axis=0).astype(jnp.float32)


def _middle_two(slabs, w9_ref):
    rows = slabs[0].shape[0] - 2
    pieces = []
    for slab in slabs:
        shifted = [_sublane_shift(slab, b - 1, 1).astype(jnp.bfloat16) for b in range(3)]
        for i in range(rows):
            pieces.append(jnp.concatenate([shifted[b][i + a] for a in range(3) for b in range(3)], axis=1))
    stacked = jnp.concatenate(pieces, axis=0)
    m = jnp.dot(stacked, w9_ref[...], preferred_element_type=jnp.float32)
    return jnp.maximum(m, 0.0).astype(jnp.bfloat16)


def _edges_two_kernel(above_ref, xp_ref, below_ref, w9_ref, edge_ref):
    frames = xp_ref.shape[0]
    plane = edge_ref.shape[1]
    m = _middle_two(
        [_slab_two(above_ref, xp_ref, below_ref, 0), _slab_two(above_ref, xp_ref, below_ref, frames - 1)], w9_ref
    )
    edge_ref[0] = m[:plane]
    edge_ref[1] = m[plane:]


def _finish(s, xp_ref, t, out_ref, slot):
    rows, width = xp_ref.shape[1], xp_ref.shape[2]
    for i in range(rows):
        v = s[i * width : (i + 1) * width] + xp_ref[t, i].astype(jnp.float32)
        out_ref[slot, i] = jnp.maximum(v, 0.0).astype(out_ref.dtype)


def _inner_two_kernel(above_ref, xp_ref, below_ref, w9_ref, t3_ref, out_ref, side_ref, mid_ref):
    frames = xp_ref.shape[0]
    plane = mid_ref.shape[1]

    group = 4 if frames % 4 == 0 else 2

    def middle(g, carry):
        f = group * g
        m = _middle_two([_slab_two(above_ref, xp_ref, below_ref, f + k) for k in range(group)], w9_ref)
        for k in range(group):
            mid_ref[f + k] = m[k * plane : (k + 1) * plane]
        return carry

    lax.fori_loop(0, frames // group, middle, 0)
    side_ref[0] = mid_ref[1]
    side_ref[1] = mid_ref[frames - 2]

    def section(g, carry):
        t = 2 * g + 1
        s = None
        for k in range(3):
            pair = jnp.concatenate([mid_ref[t - 1 + k], mid_ref[t + k]], axis=0)
            d = jnp.dot(pair, t3_ref[k], preferred_element_type=jnp.float32)
            s = d if s is None else s + d
        _finish(s[:plane], xp_ref, t, out_ref, t - 1)
        _finish(s[plane:], xp_ref, t + 1, out_ref, t)
        return carry

    lax.fori_loop(0, (frames - 2) // 2, section, 0)


def _outer_two_kernel(xp_ref, t3_ref, before_ref, after_ref, edge_ref, side_ref, out_ref):
    frames = xp_ref.shape[0]
    s = jnp.dot(before_ref[0], t3_ref[0], preferred_element_type=jnp.float32)
    s = s + jnp.dot(edge_ref[0], t3_ref[1], preferred_element_type=jnp.float32)
    s = s + jnp.dot(side_ref[0], t3_ref[2], preferred_element_type=jnp.float32)
    _finish(s, xp_ref, 0, out_ref, 0)
    s = jnp.dot(side_ref[1], t3_ref[0], preferred_element_type=jnp.float32)
    s = s + jnp.dot(edge_ref[1], t3_ref[1], preferred_element_type=jnp.float32)
    s = s + jnp.dot(after_ref[0], t3_ref[2], preferred_element_type=jnp.float32)
    _finish(s, xp_ref, frames - 1, out_ref, 1)


def block_two(above, rowed, below, spatial_kernel, temporal_kernel):
    frames, rows, width, channels = rowed.shape
    mids = spatial_kernel.shape[2]
    w9 = jnp.transpose(spatial_kernel, (0, 1, 3, 2)).reshape(9 * channels, mids)
    t3 = jnp.transpose(temporal_kernel, (0, 2, 1))
    vmem = pltpu.MemorySpace.VMEM if hasattr(pltpu, "MemorySpace") else pltpu.VMEM
    params = pltpu.CompilerParams(vmem_limit_bytes=48 * 1024 * 1024)
    spec = pl.BlockSpec(memory_space=vmem)
    plane = (rows * width, mids)
    edges = pl.pallas_call(
        _edges_two_kernel,
        out_shape=jax.ShapeDtypeStruct((2,) + plane, rowed.dtype),
        in_specs=[spec] * 4,
        out_specs=spec,
        compiler_params=params,
        cost_estimate=pl.CostEstimate(
            flops=2 * 2 * rows * width * 9 * channels * mids, bytes_accessed=2 * rowed.size, transcendentals=0
        ),
    )(above, rowed, below, w9)
    before = from_behind(edges[1:], "tm", 1)
    after = from_behind(edges[:1], "tm", -1)
    inner, side = pl.pallas_call(
        _inner_two_kernel,
        out_shape=(
            jax.ShapeDtypeStruct((frames - 2, rows, width, channels), rowed.dtype),
            jax.ShapeDtypeStruct((2,) + plane, rowed.dtype),
        ),
        in_specs=[spec] * 5,
        out_specs=(spec, spec),
        scratch_shapes=[pltpu.VMEM((frames,) + plane, jnp.bfloat16)],
        compiler_params=params,
        cost_estimate=pl.CostEstimate(
            flops=2 * frames * rows * width * (9 * channels * mids + 3 * mids * channels),
            bytes_accessed=4 * rowed.size,
            transcendentals=0,
        ),
    )(above, rowed, below, w9, t3)
    outer = pl.pallas_call(
        _outer_two_kernel,
        out_shape=jax.ShapeDtypeStruct((2, rows, width, channels), rowed.dtype),
        in_specs=[spec] * 6,
        out_specs=spec,
        compiler_params=params,
    )(rowed, t3, before, after, edges, side)
    return jnp.concatenate([outer[:1], inner, outer[1:]], axis=0)


def _copy_kernel(top_ref, bottom_ref, top_out, bottom_out):
    top_out[...] = top_ref[...]
    bottom_out[...] = bottom_ref[...]


def edge_rows(block, top, bottom):
    frames, rows, channels, width = block.shape
    top_spec = pl.BlockSpec((frames, top, channels, width), lambda i: (0, rows // top - 1, 0, 0))
    bottom_spec = pl.BlockSpec((frames, bottom, channels, width), lambda i: (0, 0, 0, 0))
    return pl.pallas_call(
        _copy_kernel,
        grid=(1,),
        out_shape=(
            jax.ShapeDtypeStruct((frames, top, channels, width), block.dtype),
            jax.ShapeDtypeStruct((frames, bottom, channels, width), block.dtype),
        ),
        in_specs=[top_spec, bottom_spec],
        out_specs=(pl.BlockSpec((frames, top, channels, width), lambda i: (0, 0, 0, 0)), bottom_spec),
    )(block, block)


def on_device(video_clip, spatial_one, temporal_one, down_weight, spatial_two, temporal_two):
    rows = video_clip.shape[1]
    top, bottom = edge_rows(video_clip, 2, 1)
    above = from_behind(top, "row", 1)
    below = from_behind(bottom, "row", -1)
    keep_first = (lax.axis_index("row") > 0).astype(jnp.int32).reshape(1)
    reduced = block_one(above, video_clip, below, keep_first, spatial_one, temporal_one, down_weight)
    rows = reduced.shape[1]
    above = from_behind(reduced[:, rows - 1 :], "row", 1)
    below = from_behind(reduced[:, :1], "row", -1)
    return block_two(above, reduced, below, spatial_two, temporal_two)


def solution(mesh):
    placed = (P("tm", "row", None, None), P(), P(), P(), P(), P())
    return jax.shard_map(
        on_device, mesh=mesh, in_specs=placed, out_specs=P("tm", "row", None, None), check_vma=False
    )
```

```python
import functools

import jax
import jax.numpy as jnp
from jax import lax
from jax.experimental import pallas as pl
from jax.experimental.pallas import tpu as pltpu
from jax.sharding import PartitionSpec as P


def padded_2(block, sides, width):
    for axis, dim in sides:
        count = lax.axis_size(axis)
        forward = [(i, i + 1) for i in range(count - 1)]
        backward = [(target, source) for source, target in forward]
        low = lax.ppermute(
            lax.slice_in_dim(block, block.shape[dim] - width, None, axis=dim), axis, forward
        )
        high = lax.ppermute(lax.slice_in_dim(block, 0, width, axis=dim), axis, backward)
        block = jnp.concatenate([low, block, high], axis=dim)
    return block


def from_behind(array, axis, by):
    devices = lax.axis_size(axis)
    pairs = [(i, i + by) for i in range(devices) if 0 <= i + by < devices]
    return lax.ppermute(array, axis, pairs)


def spatial(source, kernel, layout):
    return lax.conv_general_dilated(
        source,
        kernel,
        (1, 1),
        ((0, 0), (1, 1)),
        dimension_numbers=(layout, "HWOI", layout),
        preferred_element_type=jnp.float32,
    )


def temporal(source, kernel, layout):
    return lax.conv_general_dilated(
        source,
        kernel[:, None],
        (1, 1),
        ((0, 0), (0, 0)),
        dimension_numbers=(layout, "HWOI", layout),
        preferred_element_type=jnp.float32,
    )


def residual_block(source, spatial_kernel, temporal_kernel, space_layout, time_layout):
    padded = padded_2(source, (("tm", 0), ("row", 1)), 1)
    framed = jax.nn.relu(spatial(padded, spatial_kernel, space_layout)).astype(jnp.bfloat16)
    summed = source.astype(jnp.float32) + temporal(framed, temporal_kernel, time_layout)
    return jax.nn.relu(summed).astype(jnp.bfloat16)


def _lane_shift(x, by):
    width = x.shape[-1]
    rolled = pltpu.roll(x, (-by) % width, x.ndim - 1)
    lane = lax.broadcasted_iota(jnp.int32, x.shape, x.ndim - 1)
    inside = jnp.logical_and(lane + by >= 0, lane + by < width)
    return jnp.where(inside, rolled, jnp.zeros_like(rolled))


def _middle_one(refs, f, w9_ref):
    above_ref, xp_ref, below_ref = refs
    rows = xp_ref.shape[1] + 1
    width = xp_ref.shape[-1]
    mids = w9_ref.shape[0] // 3
    slab = jnp.concatenate([above_ref[f], xp_ref[f], below_ref[f]], axis=0).astype(jnp.float32)
    shifted = [_lane_shift(slab, b - 1).astype(jnp.bfloat16) for b in range(3)]
    stacked = jnp.concatenate(
        [jnp.concatenate([shifted[b][r] for b in range(3)], axis=0) for r in range(rows + 2)], axis=1
    )
    q = jnp.dot(w9_ref[...], stacked, preferred_element_type=jnp.float32)
    m = q[:mids, : rows * width]
    for a in range(1, 3):
        m = m + q[a * mids : (a + 1) * mids, a * width : (a + rows) * width]
    return jnp.maximum(m, 0.0).astype(jnp.bfloat16)


def _section_down(stacked, refs, t, t3_ref, wd_ref, keep_ref, out_ref, slot):
    s = jnp.dot(t3_ref[...], stacked, preferred_element_type=jnp.float32)
    _down(s, refs, t, wd_ref, keep_ref, out_ref, slot)


def _down(s, refs, t, wd_ref, keep_ref, out_ref, slot):
    above_ref, xp_ref, _ = refs
    rows = xp_ref.shape[1] + 1
    width = xp_ref.shape[-1]
    reduced_rows = (rows - 1) // 2
    lane = lax.broadcasted_iota(jnp.int32, (width // 2, width), 1)
    column = lax.broadcasted_iota(jnp.int32, (width // 2, width), 0)
    pick = (lane == 2 * column).astype(jnp.bfloat16)
    sec = []
    for h in range(rows):
        own = above_ref[t, 1] if h == 0 else xp_ref[t, h - 1]
        v = s[:, h * width : (h + 1) * width] + own.astype(jnp.float32)
        v = jnp.maximum(v, 0.0)
        if h == 0:
            v = v * keep_ref[0].astype(jnp.float32)
        sec.append(v.astype(jnp.bfloat16).astype(jnp.float32))
    shifted = [[_lane_shift(r, b - 1).astype(jnp.bfloat16) for b in range(3)] for r in sec]
    parts = []
    for a in range(3):
        for b in range(3):
            parts.append(jnp.concatenate([shifted[2 * i + a][b] for i in range(reduced_rows)], axis=1))
    stacked = jnp.concatenate(parts, axis=0)
    full = jnp.dot(wd_ref[...], stacked, preferred_element_type=jnp.float32)
    full = jnp.maximum(full, 0.0).astype(jnp.bfloat16)
    for i in range(reduced_rows):
        r = lax.dot_general(
            pick,
            full[:, i * width : (i + 1) * width],
            (((1,), (1,)), ((), ())),
            preferred_element_type=jnp.float32,
        )
        out_ref[slot, i] = r.astype(out_ref.dtype)


def _edges_one_kernel(above_ref, xp_ref, below_ref, w9_ref, edge_ref):
    refs = (above_ref, xp_ref, below_ref)
    frames = xp_ref.shape[0]
    edge_ref[0] = _middle_one(refs, 0, w9_ref)
    edge_ref[1] = _middle_one(refs, frames - 1, w9_ref)


def _inner_one_kernel(keep_ref, above_ref, xp_ref, below_ref, w9_ref, t3_ref, wd_ref, out_ref, side_ref, mid_ref):
    refs = (above_ref, xp_ref, below_ref)
    frames = xp_ref.shape[0]

    def middle(f, carry):
        mid_ref[f] = _middle_one(refs, f, w9_ref)
        return carry

    lax.fori_loop(0, frames, middle, 0)
    side_ref[0] = mid_ref[1]
    side_ref[1] = mid_ref[frames - 2]

    channels = t3_ref.shape[0] // 2

    def section(g, carry):
        t = 2 * g + 1
        stacked = jnp.concatenate([mid_ref[t - 1], mid_ref[t], mid_ref[t + 1], mid_ref[t + 2]], axis=0)
        s = jnp.dot(t3_ref[...], stacked, preferred_element_type=jnp.float32)
        _down(s[:channels], refs, t, wd_ref, keep_ref, out_ref, t - 1)
        _down(s[channels:], refs, t + 1, wd_ref, keep_ref, out_ref, t)
        return carry

    lax.fori_loop(0, (frames - 2) // 2, section, 0)


def _outer_one_kernel(
    keep_ref, above_ref, xp_ref, below_ref, t3_ref, wd_ref, before_ref, after_ref, edge_ref, side_ref, out_ref
):
    refs = (above_ref, xp_ref, below_ref)
    frames = xp_ref.shape[0]
    stacked = jnp.concatenate([before_ref[0], edge_ref[0], side_ref[0]], axis=0)
    _section_down(stacked, refs, 0, t3_ref, wd_ref, keep_ref, out_ref, 0)
    stacked = jnp.concatenate([side_ref[1], edge_ref[1], after_ref[0]], axis=0)
    _section_down(stacked, refs, frames - 1, t3_ref, wd_ref, keep_ref, out_ref, 1)


def block_one(above, rowed, below, keep_first, spatial_kernel, temporal_kernel, down_kernel):
    frames, rows, channels, width = rowed.shape
    rows = rows + 1
    mids = spatial_kernel.shape[2]
    outs = down_kernel.shape[2]
    w9 = jnp.transpose(spatial_kernel, (0, 2, 1, 3)).reshape(3 * mids, 3 * channels)
    t3 = jnp.transpose(temporal_kernel, (1, 0, 2)).reshape(channels, 3 * mids)
    wd = jnp.transpose(down_kernel, (2, 0, 1, 3)).reshape(outs, 9 * channels)
    gap = jnp.zeros((channels, mids), t3.dtype)
    t4 = jnp.concatenate(
        [jnp.concatenate([t3, gap], axis=1), jnp.concatenate([gap, t3], axis=1)], axis=0
    )
    vmem = pltpu.MemorySpace.VMEM if hasattr(pltpu, "MemorySpace") else pltpu.VMEM
    smem = pltpu.MemorySpace.SMEM if hasattr(pltpu, "MemorySpace") else pltpu.SMEM
    params = pltpu.CompilerParams(vmem_limit_bytes=48 * 1024 * 1024)
    spec = pl.BlockSpec(memory_space=vmem)
    sspec = pl.BlockSpec(memory_space=smem)
    reduced_rows = (rows - 1) // 2
    plane = (mids, rows * width)
    out_plane = (reduced_rows, width // 2, outs)
    spatial_flops = 2 * rows * width * 9 * channels * mids
    section_flops = 2 * rows * width * 3 * mids * channels + 2 * reduced_rows * width * 9 * channels * outs
    edges = pl.pallas_call(
        _edges_one_kernel,
        out_shape=jax.ShapeDtypeStruct((2,) + plane, rowed.dtype),
        in_specs=[spec] * 4,
        out_specs=spec,
        compiler_params=params,
        cost_estimate=pl.CostEstimate(flops=2 * spatial_flops, bytes_accessed=2 * rowed.size, transcendentals=0),
    )(above, rowed, below, w9)
    before = from_behind(edges[1:], "tm", 1)
    after = from_behind(edges[:1], "tm", -1)
    inner, side = pl.pallas_call(
        _inner_one_kernel,
        out_shape=(
            jax.ShapeDtypeStruct((frames - 2,) + out_plane, rowed.dtype),
            jax.ShapeDtypeStruct((2,) + plane, rowed.dtype),
        ),
        in_specs=[sspec] + [spec] * 6,
        out_specs=(spec, spec),
        scratch_shapes=[pltpu.VMEM((frames,) + plane, jnp.bfloat16)],
        compiler_params=params,
        cost_estimate=pl.CostEstimate(
            flops=frames * (spatial_flops + section_flops), bytes_accessed=4 * rowed.size, transcendentals=0
        ),
    )(keep_first, above, rowed, below, w9, t4, wd)
    outer = pl.pallas_call(
        _outer_one_kernel,
        out_shape=jax.ShapeDtypeStruct((2,) + out_plane, rowed.dtype),
        in_specs=[sspec] + [spec] * 9,
        out_specs=spec,
        compiler_params=params,
    )(keep_first, above, rowed, below, t3, wd, before, after, edges, side)
    return jnp.concatenate([outer[:1], inner, outer[1:]], axis=0)


def _sublane_shift(x, by, axis):
    size = x.shape[axis]
    rolled = pltpu.roll(x, (-by) % size, axis)
    index = lax.broadcasted_iota(jnp.int32, x.shape, axis)
    inside = jnp.logical_and(index + by >= 0, index + by < size)
    return jnp.where(inside, rolled, jnp.zeros_like(rolled))


def _slab_two(above_ref, xp_ref, below_ref, f):
    return jnp.concatenate([above_ref[f], xp_ref[f], below_ref[f]], axis=0).astype(jnp.float32)


def _middle_two(slabs, w9_ref):
    rows = slabs[0].shape[0] - 2
    pieces = []
    for slab in slabs:
        shifted = [_sublane_shift(slab, b - 1, 1).astype(jnp.bfloat16) for b in range(3)]
        for i in range(rows):
            pieces.append(jnp.concatenate([shifted[b][i + a] for a in range(3) for b in range(3)], axis=1))
    stacked = jnp.concatenate(pieces, axis=0)
    m = jnp.dot(stacked, w9_ref[...], preferred_element_type=jnp.float32)
    return jnp.maximum(m, 0.0).astype(jnp.bfloat16)


def _edges_two_kernel(above_ref, xp_ref, below_ref, w9_ref, edge_ref):
    frames = xp_ref.shape[0]
    plane = edge_ref.shape[1]
    m = _middle_two(
        [_slab_two(above_ref, xp_ref, below_ref, 0), _slab_two(above_ref, xp_ref, below_ref, frames - 1)], w9_ref
    )
    edge_ref[0] = m[:plane]
    edge_ref[1] = m[plane:]


def _finish(s, xp_ref, t, out_ref, slot):
    rows, width = xp_ref.shape[1], xp_ref.shape[2]
    for i in range(rows):
        v = s[i * width : (i + 1) * width] + xp_ref[t, i].astype(jnp.float32)
        out_ref[slot, i] = jnp.maximum(v, 0.0).astype(out_ref.dtype)


def _inner_two_kernel(above_ref, xp_ref, below_ref, w9_ref, t3_ref, out_ref, side_ref, mid_ref):
    frames = xp_ref.shape[0]
    plane = mid_ref.shape[1]

    group = 4 if frames % 4 == 0 else 2

    def middle(g, carry):
        f = group * g
        m = _middle_two([_slab_two(above_ref, xp_ref, below_ref, f + k) for k in range(group)], w9_ref)
        for k in range(group):
            mid_ref[f + k] = m[k * plane : (k + 1) * plane]
        return carry

    lax.fori_loop(0, frames // group, middle, 0)
    side_ref[0] = mid_ref[1]
    side_ref[1] = mid_ref[frames - 2]

    def section(g, carry):
        t = 2 * g + 1
        s = None
        for k in range(3):
            pair = jnp.concatenate([mid_ref[t - 1 + k], mid_ref[t + k]], axis=0)
            d = jnp.dot(pair, t3_ref[k], preferred_element_type=jnp.float32)
            s = d if s is None else s + d
        _finish(s[:plane], xp_ref, t, out_ref, t - 1)
        _finish(s[plane:], xp_ref, t + 1, out_ref, t)
        return carry

    lax.fori_loop(0, (frames - 2) // 2, section, 0)


def _outer_two_kernel(xp_ref, t3_ref, before_ref, after_ref, edge_ref, side_ref, out_ref):
    frames = xp_ref.shape[0]
    s = jnp.dot(before_ref[0], t3_ref[0], preferred_element_type=jnp.float32)
    s = s + jnp.dot(edge_ref[0], t3_ref[1], preferred_element_type=jnp.float32)
    s = s + jnp.dot(side_ref[0], t3_ref[2], preferred_element_type=jnp.float32)
    _finish(s, xp_ref, 0, out_ref, 0)
    s = jnp.dot(side_ref[1], t3_ref[0], preferred_element_type=jnp.float32)
    s = s + jnp.dot(edge_ref[1], t3_ref[1], preferred_element_type=jnp.float32)
    s = s + jnp.dot(after_ref[0], t3_ref[2], preferred_element_type=jnp.float32)
    _finish(s, xp_ref, frames - 1, out_ref, 1)


def block_two(above, rowed, below, spatial_kernel, temporal_kernel):
    frames, rows, width, channels = rowed.shape
    mids = spatial_kernel.shape[2]
    w9 = jnp.transpose(spatial_kernel, (0, 1, 3, 2)).reshape(9 * channels, mids)
    t3 = jnp.transpose(temporal_kernel, (0, 2, 1))
    vmem = pltpu.MemorySpace.VMEM if hasattr(pltpu, "MemorySpace") else pltpu.VMEM
    params = pltpu.CompilerParams(vmem_limit_bytes=48 * 1024 * 1024)
    spec = pl.BlockSpec(memory_space=vmem)
    plane = (rows * width, mids)
    edges = pl.pallas_call(
        _edges_two_kernel,
        out_shape=jax.ShapeDtypeStruct((2,) + plane, rowed.dtype),
        in_specs=[spec] * 4,
        out_specs=spec,
        compiler_params=params,
        cost_estimate=pl.CostEstimate(
            flops=2 * 2 * rows * width * 9 * channels * mids, bytes_accessed=2 * rowed.size, transcendentals=0
        ),
    )(above, rowed, below, w9)
    before = from_behind(edges[1:], "tm", 1)
    after = from_behind(edges[:1], "tm", -1)
    inner, side = pl.pallas_call(
        _inner_two_kernel,
        out_shape=(
            jax.ShapeDtypeStruct((frames - 2, rows, width, channels), rowed.dtype),
            jax.ShapeDtypeStruct((2,) + plane, rowed.dtype),
        ),
        in_specs=[spec] * 5,
        out_specs=(spec, spec),
        scratch_shapes=[pltpu.VMEM((frames,) + plane, jnp.bfloat16)],
        compiler_params=params,
        cost_estimate=pl.CostEstimate(
            flops=2 * frames * rows * width * (9 * channels * mids + 3 * mids * channels),
            bytes_accessed=4 * rowed.size,
            transcendentals=0,
        ),
    )(above, rowed, below, w9, t3)
    outer = pl.pallas_call(
        _outer_two_kernel,
        out_shape=jax.ShapeDtypeStruct((2, rows, width, channels), rowed.dtype),
        in_specs=[spec] * 6,
        out_specs=spec,
        compiler_params=params,
    )(rowed, t3, before, after, edges, side)
    return jnp.concatenate([outer[:1], inner, outer[1:]], axis=0)


def _copy_kernel(top_ref, bottom_ref, top_out, bottom_out):
    top_out[...] = top_ref[...]
    bottom_out[...] = bottom_ref[...]


def edge_rows(block, top, bottom):
    frames, rows, channels, width = block.shape
    top_spec = pl.BlockSpec((frames, top, channels, width), lambda i: (0, rows // top - 1, 0, 0))
    bottom_spec = pl.BlockSpec((frames, bottom, channels, width), lambda i: (0, 0, 0, 0))
    return pl.pallas_call(
        _copy_kernel,
        grid=(1,),
        out_shape=(
            jax.ShapeDtypeStruct((frames, top, channels, width), block.dtype),
            jax.ShapeDtypeStruct((frames, bottom, channels, width), block.dtype),
        ),
        in_specs=[top_spec, bottom_spec],
        out_specs=(pl.BlockSpec((frames, top, channels, width), lambda i: (0, 0, 0, 0)), bottom_spec),
    )(block, block)


def on_device(video_clip, spatial_one, temporal_one, down_weight, spatial_two, temporal_two):
    rows = video_clip.shape[1]
    top, bottom = edge_rows(video_clip, 2, 1)
    above = from_behind(top, "row", 1)
    below = from_behind(bottom, "row", -1)
    keep_first = (lax.axis_index("row") > 0).astype(jnp.int32).reshape(1)
    reduced = block_one(above, video_clip, below, keep_first, spatial_one, temporal_one, down_weight)
    rows = reduced.shape[1]
    above = from_behind(reduced[:, rows - 1 :], "row", 1)
    below = from_behind(reduced[:, :1], "row", -1)
    return block_two(above, reduced, below, spatial_two, temporal_two)


def solution(mesh):
    placed = (P("tm", "row", None, None), P(), P(), P(), P(), P())
    return jax.shard_map(
        on_device, mesh=mesh, in_specs=placed, out_specs=P("tm", "row", None, None), check_vma=False
    )
```

```python
import functools

import jax
import jax.numpy as jnp
from jax import lax
from jax.experimental import pallas as pl
from jax.experimental.pallas import tpu as pltpu
from jax.sharding import PartitionSpec as P


def padded_2(block, sides, width):
    for axis, dim in sides:
        count = lax.axis_size(axis)
        forward = [(i, i + 1) for i in range(count - 1)]
        backward = [(target, source) for source, target in forward]
        low = lax.ppermute(
            lax.slice_in_dim(block, block.shape[dim] - width, None, axis=dim), axis, forward
        )
        high = lax.ppermute(lax.slice_in_dim(block, 0, width, axis=dim), axis, backward)
        block = jnp.concatenate([low, block, high], axis=dim)
    return block


def from_behind(array, axis, by):
    devices = lax.axis_size(axis)
    pairs = [(i, i + by) for i in range(devices) if 0 <= i + by < devices]
    return lax.ppermute(array, axis, pairs)


def spatial(source, kernel, layout):
    return lax.conv_general_dilated(
        source,
        kernel,
        (1, 1),
        ((0, 0), (1, 1)),
        dimension_numbers=(layout, "HWOI", layout),
        preferred_element_type=jnp.float32,
    )


def temporal(source, kernel, layout):
    return lax.conv_general_dilated(
        source,
        kernel[:, None],
        (1, 1),
        ((0, 0), (0, 0)),
        dimension_numbers=(layout, "HWOI", layout),
        preferred_element_type=jnp.float32,
    )


def residual_block(source, spatial_kernel, temporal_kernel, space_layout, time_layout):
    padded = padded_2(source, (("tm", 0), ("row", 1)), 1)
    framed = jax.nn.relu(spatial(padded, spatial_kernel, space_layout)).astype(jnp.bfloat16)
    summed = source.astype(jnp.float32) + temporal(framed, temporal_kernel, time_layout)
    return jax.nn.relu(summed).astype(jnp.bfloat16)


def _lane_shift(x, by):
    width = x.shape[-1]
    rolled = pltpu.roll(x, (-by) % width, x.ndim - 1)
    lane = lax.broadcasted_iota(jnp.int32, x.shape, x.ndim - 1)
    inside = jnp.logical_and(lane + by >= 0, lane + by < width)
    return jnp.where(inside, rolled, jnp.zeros_like(rolled))


def _middle_one(refs, f, w9_ref):
    above_ref, xp_ref, below_ref = refs
    rows = xp_ref.shape[1] + 1
    slab = jnp.concatenate([above_ref[f], xp_ref[f], below_ref[f]], axis=0).astype(jnp.float32)
    shifted = [_lane_shift(slab, b - 1).astype(jnp.bfloat16) for b in range(3)]
    parts = []
    for a in range(3):
        for b in range(3):
            parts.append(jnp.concatenate([shifted[b][h + a] for h in range(rows)], axis=1))
    stacked = jnp.concatenate(parts, axis=0)
    m = jnp.dot(w9_ref[...], stacked, preferred_element_type=jnp.float32)
    return jnp.maximum(m, 0.0).astype(jnp.bfloat16)


def _section_down(stacked, refs, t, t3_ref, wd_ref, keep_ref, out_ref, slot):
    s = jnp.dot(t3_ref[...], stacked, preferred_element_type=jnp.float32)
    _down(s, refs, t, wd_ref, keep_ref, out_ref, slot)


def _down(s, refs, t, wd_ref, keep_ref, out_ref, slot):
    above_ref, xp_ref, _ = refs
    rows = xp_ref.shape[1] + 1
    width = xp_ref.shape[-1]
    reduced_rows = (rows - 1) // 2
    lane = lax.broadcasted_iota(jnp.int32, (width // 2, width), 1)
    column = lax.broadcasted_iota(jnp.int32, (width // 2, width), 0)
    pick = (lane == 2 * column).astype(jnp.bfloat16)
    sec = []
    for h in range(rows):
        own = above_ref[t, 1] if h == 0 else xp_ref[t, h - 1]
        v = s[:, h * width : (h + 1) * width] + own.astype(jnp.float32)
        v = jnp.maximum(v, 0.0)
        if h == 0:
            v = v * keep_ref[0].astype(jnp.float32)
        sec.append(v.astype(jnp.bfloat16).astype(jnp.float32))
    shifted = [[_lane_shift(r, b - 1).astype(jnp.bfloat16) for b in range(3)] for r in sec]
    parts = []
    for a in range(3):
        for b in range(3):
            parts.append(jnp.concatenate([shifted[2 * i + a][b] for i in range(reduced_rows)], axis=1))
    stacked = jnp.concatenate(parts, axis=0)
    full = jnp.dot(wd_ref[...], stacked, preferred_element_type=jnp.float32)
    full = jnp.maximum(full, 0.0).astype(jnp.bfloat16)
    outs = full.shape[0]
    rows_by_d = jnp.concatenate([full[:, i * width : (i + 1) * width] for i in range(reduced_rows)], axis=0)
    r = lax.dot_general(pick, rows_by_d, (((1,), (1,)), ((), ())), preferred_element_type=jnp.float32)
    for i in range(reduced_rows):
        out_ref[slot, i] = r[:, i * outs : (i + 1) * outs].astype(out_ref.dtype)


def _edges_one_kernel(above_ref, xp_ref, below_ref, w9_ref, edge_ref):
    refs = (above_ref, xp_ref, below_ref)
    frames = xp_ref.shape[0]
    edge_ref[0] = _middle_one(refs, 0, w9_ref)
    edge_ref[1] = _middle_one(refs, frames - 1, w9_ref)


def _inner_one_kernel(keep_ref, above_ref, xp_ref, below_ref, w9_ref, t3_ref, wd_ref, out_ref, side_ref, mid_ref):
    refs = (above_ref, xp_ref, below_ref)
    frames = xp_ref.shape[0]

    def middle(f, carry):
        mid_ref[f] = _middle_one(refs, f, w9_ref)
        return carry

    lax.fori_loop(0, frames, middle, 0)
    side_ref[0] = mid_ref[1]
    side_ref[1] = mid_ref[frames - 2]

    channels = t3_ref.shape[0] // 2

    def section(g, carry):
        t = 2 * g + 1
        stacked = jnp.concatenate([mid_ref[t - 1], mid_ref[t], mid_ref[t + 1], mid_ref[t + 2]], axis=0)
        s = jnp.dot(t3_ref[...], stacked, preferred_element_type=jnp.float32)
        _down(s[:channels], refs, t, wd_ref, keep_ref, out_ref, t - 1)
        _down(s[channels:], refs, t + 1, wd_ref, keep_ref, out_ref, t)
        return carry

    lax.fori_loop(0, (frames - 2) // 2, section, 0)


def _outer_one_kernel(
    keep_ref, above_ref, xp_ref, below_ref, t3_ref, wd_ref, before_ref, after_ref, edge_ref, side_ref, out_ref
):
    refs = (above_ref, xp_ref, below_ref)
    frames = xp_ref.shape[0]
    stacked = jnp.concatenate([before_ref[0], edge_ref[0], side_ref[0]], axis=0)
    _section_down(stacked, refs, 0, t3_ref, wd_ref, keep_ref, out_ref, 0)
    stacked = jnp.concatenate([side_ref[1], edge_ref[1], after_ref[0]], axis=0)
    _section_down(stacked, refs, frames - 1, t3_ref, wd_ref, keep_ref, out_ref, 1)


def block_one(above, rowed, below, keep_first, spatial_kernel, temporal_kernel, down_kernel):
    frames, rows, channels, width = rowed.shape
    rows = rows + 1
    mids = spatial_kernel.shape[2]
    outs = down_kernel.shape[2]
    w9 = jnp.transpose(spatial_kernel, (2, 0, 1, 3)).reshape(mids, 9 * channels)
    t3 = jnp.transpose(temporal_kernel, (1, 0, 2)).reshape(channels, 3 * mids)
    wd = jnp.transpose(down_kernel, (2, 0, 1, 3)).reshape(outs, 9 * channels)
    gap = jnp.zeros((channels, mids), t3.dtype)
    t4 = jnp.concatenate(
        [jnp.concatenate([t3, gap], axis=1), jnp.concatenate([gap, t3], axis=1)], axis=0
    )
    vmem = pltpu.MemorySpace.VMEM if hasattr(pltpu, "MemorySpace") else pltpu.VMEM
    smem = pltpu.MemorySpace.SMEM if hasattr(pltpu, "MemorySpace") else pltpu.SMEM
    params = pltpu.CompilerParams(vmem_limit_bytes=48 * 1024 * 1024)
    spec = pl.BlockSpec(memory_space=vmem)
    sspec = pl.BlockSpec(memory_space=smem)
    reduced_rows = (rows - 1) // 2
    plane = (mids, rows * width)
    out_plane = (reduced_rows, width // 2, outs)
    spatial_flops = 2 * rows * width * 9 * channels * mids
    section_flops = 2 * rows * width * 3 * mids * channels + 2 * reduced_rows * width * 9 * channels * outs
    edges = pl.pallas_call(
        _edges_one_kernel,
        out_shape=jax.ShapeDtypeStruct((2,) + plane, rowed.dtype),
        in_specs=[spec] * 4,
        out_specs=spec,
        compiler_params=params,
        cost_estimate=pl.CostEstimate(flops=2 * spatial_flops, bytes_accessed=2 * rowed.size, transcendentals=0),
    )(above, rowed, below, w9)
    before = from_behind(edges[1:], "tm", 1)
    after = from_behind(edges[:1], "tm", -1)
    inner, side = pl.pallas_call(
        _inner_one_kernel,
        out_shape=(
            jax.ShapeDtypeStruct((frames - 2,) + out_plane, rowed.dtype),
            jax.ShapeDtypeStruct((2,) + plane, rowed.dtype),
        ),
        in_specs=[sspec] + [spec] * 6,
        out_specs=(spec, spec),
        scratch_shapes=[pltpu.VMEM((frames,) + plane, jnp.bfloat16)],
        compiler_params=params,
        cost_estimate=pl.CostEstimate(
            flops=frames * (spatial_flops + section_flops), bytes_accessed=4 * rowed.size, transcendentals=0
        ),
    )(keep_first, above, rowed, below, w9, t4, wd)
    outer = pl.pallas_call(
        _outer_one_kernel,
        out_shape=jax.ShapeDtypeStruct((2,) + out_plane, rowed.dtype),
        in_specs=[sspec] + [spec] * 9,
        out_specs=spec,
        compiler_params=params,
    )(keep_first, above, rowed, below, t3, wd, before, after, edges, side)
    return jnp.concatenate([outer[:1], inner, outer[1:]], axis=0)


def _sublane_shift(x, by, axis):
    size = x.shape[axis]
    rolled = pltpu.roll(x, (-by) % size, axis)
    index = lax.broadcasted_iota(jnp.int32, x.shape, axis)
    inside = jnp.logical_and(index + by >= 0, index + by < size)
    return jnp.where(inside, rolled, jnp.zeros_like(rolled))


def _slab_two(above_ref, xp_ref, below_ref, f):
    return jnp.concatenate([above_ref[f], xp_ref[f], below_ref[f]], axis=0).astype(jnp.float32)


def _middle_two(slabs, w9_ref):
    rows = slabs[0].shape[0] - 2
    pieces = []
    for slab in slabs:
        shifted = [_sublane_shift(slab, b - 1, 1).astype(jnp.bfloat16) for b in range(3)]
        for i in range(rows):
            pieces.append(jnp.concatenate([shifted[b][i + a] for a in range(3) for b in range(3)], axis=1))
    stacked = jnp.concatenate(pieces, axis=0)
    m = jnp.dot(stacked, w9_ref[...], preferred_element_type=jnp.float32)
    return jnp.maximum(m, 0.0).astype(jnp.bfloat16)


def _edges_two_kernel(above_ref, xp_ref, below_ref, w9_ref, edge_ref):
    frames = xp_ref.shape[0]
    plane = edge_ref.shape[1]
    m = _middle_two(
        [_slab_two(above_ref, xp_ref, below_ref, 0), _slab_two(above_ref, xp_ref, below_ref, frames - 1)], w9_ref
    )
    edge_ref[0] = m[:plane]
    edge_ref[1] = m[plane:]


def _finish(s, xp_ref, t, out_ref, slot):
    rows, width = xp_ref.shape[1], xp_ref.shape[2]
    for i in range(rows):
        v = s[i * width : (i + 1) * width] + xp_ref[t, i].astype(jnp.float32)
        out_ref[slot, i] = jnp.maximum(v, 0.0).astype(out_ref.dtype)


def _inner_two_kernel(above_ref, xp_ref, below_ref, w9_ref, t3_ref, out_ref, side_ref, mid_ref):
    frames = xp_ref.shape[0]
    plane = mid_ref.shape[1]

    group = 4 if frames % 4 == 0 else 2

    def middle(g, carry):
        f = group * g
        m = _middle_two([_slab_two(above_ref, xp_ref, below_ref, f + k) for k in range(group)], w9_ref)
        for k in range(group):
            mid_ref[f + k] = m[k * plane : (k + 1) * plane]
        return carry

    lax.fori_loop(0, frames // group, middle, 0)
    side_ref[0] = mid_ref[1]
    side_ref[1] = mid_ref[frames - 2]

    def section(g, carry):
        t = 2 * g + 1
        s = None
        for k in range(3):
            pair = jnp.concatenate([mid_ref[t - 1 + k], mid_ref[t + k]], axis=0)
            d = jnp.dot(pair, t3_ref[k], preferred_element_type=jnp.float32)
            s = d if s is None else s + d
        _finish(s[:plane], xp_ref, t, out_ref, t - 1)
        _finish(s[plane:], xp_ref, t + 1, out_ref, t)
        return carry

    lax.fori_loop(0, (frames - 2) // 2, section, 0)


def _outer_two_kernel(xp_ref, t3_ref, before_ref, after_ref, edge_ref, side_ref, out_ref):
    frames = xp_ref.shape[0]
    s = jnp.dot(before_ref[0], t3_ref[0], preferred_element_type=jnp.float32)
    s = s + jnp.dot(edge_ref[0], t3_ref[1], preferred_element_type=jnp.float32)
    s = s + jnp.dot(side_ref[0], t3_ref[2], preferred_element_type=jnp.float32)
    _finish(s, xp_ref, 0, out_ref, 0)
    s = jnp.dot(side_ref[1], t3_ref[0], preferred_element_type=jnp.float32)
    s = s + jnp.dot(edge_ref[1], t3_ref[1], preferred_element_type=jnp.float32)
    s = s + jnp.dot(after_ref[0], t3_ref[2], preferred_element_type=jnp.float32)
    _finish(s, xp_ref, frames - 1, out_ref, 1)


def block_two(above, rowed, below, spatial_kernel, temporal_kernel):
    frames, rows, width, channels = rowed.shape
    mids = spatial_kernel.shape[2]
    w9 = jnp.transpose(spatial_kernel, (0, 1, 3, 2)).reshape(9 * channels, mids)
    t3 = jnp.transpose(temporal_kernel, (0, 2, 1))
    vmem = pltpu.MemorySpace.VMEM if hasattr(pltpu, "MemorySpace") else pltpu.VMEM
    params = pltpu.CompilerParams(vmem_limit_bytes=48 * 1024 * 1024)
    spec = pl.BlockSpec(memory_space=vmem)
    plane = (rows * width, mids)
    edges = pl.pallas_call(
        _edges_two_kernel,
        out_shape=jax.ShapeDtypeStruct((2,) + plane, rowed.dtype),
        in_specs=[spec] * 4,
        out_specs=spec,
        compiler_params=params,
        cost_estimate=pl.CostEstimate(
            flops=2 * 2 * rows * width * 9 * channels * mids, bytes_accessed=2 * rowed.size, transcendentals=0
        ),
    )(above, rowed, below, w9)
    before = from_behind(edges[1:], "tm", 1)
    after = from_behind(edges[:1], "tm", -1)
    inner, side = pl.pallas_call(
        _inner_two_kernel,
        out_shape=(
            jax.ShapeDtypeStruct((frames - 2, rows, width, channels), rowed.dtype),
            jax.ShapeDtypeStruct((2,) + plane, rowed.dtype),
        ),
        in_specs=[spec] * 5,
        out_specs=(spec, spec),
        scratch_shapes=[pltpu.VMEM((frames,) + plane, jnp.bfloat16)],
        compiler_params=params,
        cost_estimate=pl.CostEstimate(
            flops=2 * frames * rows * width * (9 * channels * mids + 3 * mids * channels),
            bytes_accessed=4 * rowed.size,
            transcendentals=0,
        ),
    )(above, rowed, below, w9, t3)
    outer = pl.pallas_call(
        _outer_two_kernel,
        out_shape=jax.ShapeDtypeStruct((2, rows, width, channels), rowed.dtype),
        in_specs=[spec] * 6,
        out_specs=spec,
        compiler_params=params,
    )(rowed, t3, before, after, edges, side)
    return jnp.concatenate([outer[:1], inner, outer[1:]], axis=0)


def _copy_kernel(top_ref, bottom_ref, top_out, bottom_out):
    top_out[...] = top_ref[...]
    bottom_out[...] = bottom_ref[...]


def edge_rows(block, top, bottom):
    frames, rows, channels, width = block.shape
    top_spec = pl.BlockSpec((frames, top, channels, width), lambda i: (0, rows // top - 1, 0, 0))
    bottom_spec = pl.BlockSpec((frames, bottom, channels, width), lambda i: (0, 0, 0, 0))
    return pl.pallas_call(
        _copy_kernel,
        grid=(1,),
        out_shape=(
            jax.ShapeDtypeStruct((frames, top, channels, width), block.dtype),
            jax.ShapeDtypeStruct((frames, bottom, channels, width), block.dtype),
        ),
        in_specs=[top_spec, bottom_spec],
        out_specs=(pl.BlockSpec((frames, top, channels, width), lambda i: (0, 0, 0, 0)), bottom_spec),
    )(block, block)


def on_device(video_clip, spatial_one, temporal_one, down_weight, spatial_two, temporal_two):
    rows = video_clip.shape[1]
    top, bottom = edge_rows(video_clip, 2, 1)
    above = from_behind(top, "row", 1)
    below = from_behind(bottom, "row", -1)
    keep_first = (lax.axis_index("row") > 0).astype(jnp.int32).reshape(1)
    reduced = block_one(above, video_clip, below, keep_first, spatial_one, temporal_one, down_weight)
    rows = reduced.shape[1]
    above = from_behind(reduced[:, rows - 1 :], "row", 1)
    below = from_behind(reduced[:, :1], "row", -1)
    return block_two(above, reduced, below, spatial_two, temporal_two)


def solution(mesh):
    placed = (P("tm", "row", None, None), P(), P(), P(), P(), P())
    return jax.shard_map(
        on_device, mesh=mesh, in_specs=placed, out_specs=P("tm", "row", None, None), check_vma=False
    )
```

```python
import functools

import jax
import jax.numpy as jnp
from jax import lax
from jax.experimental import pallas as pl
from jax.experimental.pallas import tpu as pltpu
from jax.sharding import PartitionSpec as P


def padded_2(block, sides, width):
    for axis, dim in sides:
        count = lax.axis_size(axis)
        forward = [(i, i + 1) for i in range(count - 1)]
        backward = [(target, source) for source, target in forward]
        low = lax.ppermute(
            lax.slice_in_dim(block, block.shape[dim] - width, None, axis=dim), axis, forward
        )
        high = lax.ppermute(lax.slice_in_dim(block, 0, width, axis=dim), axis, backward)
        block = jnp.concatenate([low, block, high], axis=dim)
    return block


def from_behind(array, axis, by):
    devices = lax.axis_size(axis)
    pairs = [(i, i + by) for i in range(devices) if 0 <= i + by < devices]
    return lax.ppermute(array, axis, pairs)


def spatial(source, kernel, layout):
    return lax.conv_general_dilated(
        source,
        kernel,
        (1, 1),
        ((0, 0), (1, 1)),
        dimension_numbers=(layout, "HWOI", layout),
        preferred_element_type=jnp.float32,
    )


def temporal(source, kernel, layout):
    return lax.conv_general_dilated(
        source,
        kernel[:, None],
        (1, 1),
        ((0, 0), (0, 0)),
        dimension_numbers=(layout, "HWOI", layout),
        preferred_element_type=jnp.float32,
    )


def residual_block(source, spatial_kernel, temporal_kernel, space_layout, time_layout):
    padded = padded_2(source, (("tm", 0), ("row", 1)), 1)
    framed = jax.nn.relu(spatial(padded, spatial_kernel, space_layout)).astype(jnp.bfloat16)
    summed = source.astype(jnp.float32) + temporal(framed, temporal_kernel, time_layout)
    return jax.nn.relu(summed).astype(jnp.bfloat16)


def _lane_shift(x, by):
    width = x.shape[-1]
    rolled = pltpu.roll(x, (-by) % width, x.ndim - 1)
    lane = lax.broadcasted_iota(jnp.int32, x.shape, x.ndim - 1)
    inside = jnp.logical_and(lane + by >= 0, lane + by < width)
    return jnp.where(inside, rolled, jnp.zeros_like(rolled))


def _middle_one(refs, f, w9_ref, count=1):
    above_ref, xp_ref, below_ref = refs
    rows = xp_ref.shape[1] + 1
    columns = []
    for k in range(count):
        slab = jnp.concatenate([above_ref[f + k], xp_ref[f + k], below_ref[f + k]], axis=0).astype(jnp.float32)
        shifted = [_lane_shift(slab, b - 1).astype(jnp.bfloat16) for b in range(3)]
        parts = []
        for a in range(3):
            for b in range(3):
                parts.append(jnp.concatenate([shifted[b][h + a] for h in range(rows)], axis=1))
        columns.append(jnp.concatenate(parts, axis=0))
    stacked = columns[0] if count == 1 else jnp.concatenate(columns, axis=1)
    m = jnp.dot(w9_ref[...], stacked, preferred_element_type=jnp.float32)
    return jnp.maximum(m, 0.0).astype(jnp.bfloat16)


def _section_down(stacked, refs, t, t3_ref, wd_ref, keep_ref, out_ref, slot):
    s = jnp.dot(t3_ref[...], stacked, preferred_element_type=jnp.float32)
    _down(s, refs, t, wd_ref, keep_ref, out_ref, slot)


def _down(s, refs, t, wd_ref, keep_ref, out_ref, slot):
    above_ref, xp_ref, _ = refs
    rows = xp_ref.shape[1] + 1
    width = xp_ref.shape[-1]
    reduced_rows = (rows - 1) // 2
    lane = lax.broadcasted_iota(jnp.int32, (width // 2, width), 1)
    column = lax.broadcasted_iota(jnp.int32, (width // 2, width), 0)
    pick = (lane == 2 * column).astype(jnp.bfloat16)
    sec = []
    for h in range(rows):
        own = above_ref[t, 1] if h == 0 else xp_ref[t, h - 1]
        v = s[:, h * width : (h + 1) * width] + own.astype(jnp.float32)
        v = jnp.maximum(v, 0.0)
        if h == 0:
            v = v * keep_ref[0].astype(jnp.float32)
        sec.append(v.astype(jnp.bfloat16).astype(jnp.float32))
    shifted = [[_lane_shift(r, b - 1).astype(jnp.bfloat16) for b in range(3)] for r in sec]
    parts = []
    for a in range(3):
        for b in range(3):
            parts.append(jnp.concatenate([shifted[2 * i + a][b] for i in range(reduced_rows)], axis=1))
    stacked = jnp.concatenate(parts, axis=0)
    full = jnp.dot(wd_ref[...], stacked, preferred_element_type=jnp.float32)
    full = jnp.maximum(full, 0.0).astype(jnp.bfloat16)
    outs = full.shape[0]
    rows_by_d = jnp.concatenate([full[:, i * width : (i + 1) * width] for i in range(reduced_rows)], axis=0)
    r = lax.dot_general(pick, rows_by_d, (((1,), (1,)), ((), ())), preferred_element_type=jnp.float32)
    for i in range(reduced_rows):
        out_ref[slot, i] = r[:, i * outs : (i + 1) * outs].astype(out_ref.dtype)


def _edges_one_kernel(above_ref, xp_ref, below_ref, w9_ref, edge_ref):
    refs = (above_ref, xp_ref, below_ref)
    frames = xp_ref.shape[0]
    edge_ref[0] = _middle_one(refs, 0, w9_ref)
    edge_ref[1] = _middle_one(refs, frames - 1, w9_ref)


def _inner_one_kernel(keep_ref, above_ref, xp_ref, below_ref, w9_ref, t3_ref, wd_ref, out_ref, side_ref, mid_ref):
    refs = (above_ref, xp_ref, below_ref)
    frames = xp_ref.shape[0]

    span = mid_ref.shape[-1]

    def middle(g, carry):
        m = _middle_one(refs, 2 * g, w9_ref, 2)
        mid_ref[2 * g] = m[:, :span]
        mid_ref[2 * g + 1] = m[:, span:]
        return carry

    lax.fori_loop(0, frames // 2, middle, 0)
    side_ref[0] = mid_ref[1]
    side_ref[1] = mid_ref[frames - 2]

    channels = t3_ref.shape[0] // 2

    def section(g, carry):
        t = 2 * g + 1
        stacked = jnp.concatenate([mid_ref[t - 1], mid_ref[t], mid_ref[t + 1], mid_ref[t + 2]], axis=0)
        s = jnp.dot(t3_ref[...], stacked, preferred_element_type=jnp.float32)
        _down(s[:channels], refs, t, wd_ref, keep_ref, out_ref, t - 1)
        _down(s[channels:], refs, t + 1, wd_ref, keep_ref, out_ref, t)
        return carry

    lax.fori_loop(0, (frames - 2) // 2, section, 0)


def _outer_one_kernel(
    keep_ref, above_ref, xp_ref, below_ref, t3_ref, wd_ref, before_ref, after_ref, edge_ref, side_ref, out_ref
):
    refs = (above_ref, xp_ref, below_ref)
    frames = xp_ref.shape[0]
    stacked = jnp.concatenate([before_ref[0], edge_ref[0], side_ref[0]], axis=0)
    _section_down(stacked, refs, 0, t3_ref, wd_ref, keep_ref, out_ref, 0)
    stacked = jnp.concatenate([side_ref[1], edge_ref[1], after_ref[0]], axis=0)
    _section_down(stacked, refs, frames - 1, t3_ref, wd_ref, keep_ref, out_ref, 1)


def block_one(above, rowed, below, keep_first, spatial_kernel, temporal_kernel, down_kernel):
    frames, rows, channels, width = rowed.shape
    rows = rows + 1
    mids = spatial_kernel.shape[2]
    outs = down_kernel.shape[2]
    w9 = jnp.transpose(spatial_kernel, (2, 0, 1, 3)).reshape(mids, 9 * channels)
    t3 = jnp.transpose(temporal_kernel, (1, 0, 2)).reshape(channels, 3 * mids)
    wd = jnp.transpose(down_kernel, (2, 0, 1, 3)).reshape(outs, 9 * channels)
    gap = jnp.zeros((channels, mids), t3.dtype)
    t4 = jnp.concatenate(
        [jnp.concatenate([t3, gap], axis=1), jnp.concatenate([gap, t3], axis=1)], axis=0
    )
    vmem = pltpu.MemorySpace.VMEM if hasattr(pltpu, "MemorySpace") else pltpu.VMEM
    smem = pltpu.MemorySpace.SMEM if hasattr(pltpu, "MemorySpace") else pltpu.SMEM
    params = pltpu.CompilerParams(vmem_limit_bytes=48 * 1024 * 1024)
    spec = pl.BlockSpec(memory_space=vmem)
    sspec = pl.BlockSpec(memory_space=smem)
    reduced_rows = (rows - 1) // 2
    plane = (mids, rows * width)
    out_plane = (reduced_rows, width // 2, outs)
    spatial_flops = 2 * rows * width * 9 * channels * mids
    section_flops = 2 * rows * width * 3 * mids * channels + 2 * reduced_rows * width * 9 * channels * outs
    edges = pl.pallas_call(
        _edges_one_kernel,
        out_shape=jax.ShapeDtypeStruct((2,) + plane, rowed.dtype),
        in_specs=[spec] * 4,
        out_specs=spec,
        compiler_params=params,
        cost_estimate=pl.CostEstimate(flops=2 * spatial_flops, bytes_accessed=2 * rowed.size, transcendentals=0),
    )(above, rowed, below, w9)
    before = from_behind(edges[1:], "tm", 1)
    after = from_behind(edges[:1], "tm", -1)
    inner, side = pl.pallas_call(
        _inner_one_kernel,
        out_shape=(
            jax.ShapeDtypeStruct((frames - 2,) + out_plane, rowed.dtype),
            jax.ShapeDtypeStruct((2,) + plane, rowed.dtype),
        ),
        in_specs=[sspec] + [spec] * 6,
        out_specs=(spec, spec),
        scratch_shapes=[pltpu.VMEM((frames,) + plane, jnp.bfloat16)],
        compiler_params=params,
        cost_estimate=pl.CostEstimate(
            flops=frames * (spatial_flops + section_flops), bytes_accessed=4 * rowed.size, transcendentals=0
        ),
    )(keep_first, above, rowed, below, w9, t4, wd)
    outer = pl.pallas_call(
        _outer_one_kernel,
        out_shape=jax.ShapeDtypeStruct((2,) + out_plane, rowed.dtype),
        in_specs=[sspec] + [spec] * 9,
        out_specs=spec,
        compiler_params=params,
    )(keep_first, above, rowed, below, t3, wd, before, after, edges, side)
    return jnp.concatenate([outer[:1], inner, outer[1:]], axis=0)


def _sublane_shift(x, by, axis):
    size = x.shape[axis]
    rolled = pltpu.roll(x, (-by) % size, axis)
    index = lax.broadcasted_iota(jnp.int32, x.shape, axis)
    inside = jnp.logical_and(index + by >= 0, index + by < size)
    return jnp.where(inside, rolled, jnp.zeros_like(rolled))


def _slab_two(above_ref, xp_ref, below_ref, f):
    return jnp.concatenate([above_ref[f], xp_ref[f], below_ref[f]], axis=0).astype(jnp.float32)


def _middle_two(slabs, w9_ref):
    rows = slabs[0].shape[0] - 2
    pieces = []
    for slab in slabs:
        shifted = [_sublane_shift(slab, b - 1, 1).astype(jnp.bfloat16) for b in range(3)]
        for i in range(rows):
            pieces.append(jnp.concatenate([shifted[b][i + a] for a in range(3) for b in range(3)], axis=1))
    stacked = jnp.concatenate(pieces, axis=0)
    m = jnp.dot(stacked, w9_ref[...], preferred_element_type=jnp.float32)
    return jnp.maximum(m, 0.0).astype(jnp.bfloat16)


def _edges_two_kernel(above_ref, xp_ref, below_ref, w9_ref, edge_ref):
    frames = xp_ref.shape[0]
    plane = edge_ref.shape[1]
    m = _middle_two(
        [_slab_two(above_ref, xp_ref, below_ref, 0), _slab_two(above_ref, xp_ref, below_ref, frames - 1)], w9_ref
    )
    edge_ref[0] = m[:plane]
    edge_ref[1] = m[plane:]


def _finish(s, xp_ref, t, out_ref, slot):
    rows, width = xp_ref.shape[1], xp_ref.shape[2]
    for i in range(rows):
        v = s[i * width : (i + 1) * width] + xp_ref[t, i].astype(jnp.float32)
        out_ref[slot, i] = jnp.maximum(v, 0.0).astype(out_ref.dtype)


def _inner_two_kernel(above_ref, xp_ref, below_ref, w9_ref, t3_ref, out_ref, side_ref, mid_ref):
    frames = xp_ref.shape[0]
    plane = mid_ref.shape[1]

    group = 4 if frames % 4 == 0 else 2

    def middle(g, carry):
        f = group * g
        m = _middle_two([_slab_two(above_ref, xp_ref, below_ref, f + k) for k in range(group)], w9_ref)
        for k in range(group):
            mid_ref[f + k] = m[k * plane : (k + 1) * plane]
        return carry

    lax.fori_loop(0, frames // group, middle, 0)
    side_ref[0] = mid_ref[1]
    side_ref[1] = mid_ref[frames - 2]

    def section(g, carry):
        t = 2 * g + 1
        s = None
        for k in range(3):
            pair = jnp.concatenate([mid_ref[t - 1 + k], mid_ref[t + k]], axis=0)
            d = jnp.dot(pair, t3_ref[k], preferred_element_type=jnp.float32)
            s = d if s is None else s + d
        _finish(s[:plane], xp_ref, t, out_ref, t - 1)
        _finish(s[plane:], xp_ref, t + 1, out_ref, t)
        return carry

    lax.fori_loop(0, (frames - 2) // 2, section, 0)


def _outer_two_kernel(xp_ref, t3_ref, before_ref, after_ref, edge_ref, side_ref, out_ref):
    frames = xp_ref.shape[0]
    s = jnp.dot(before_ref[0], t3_ref[0], preferred_element_type=jnp.float32)
    s = s + jnp.dot(edge_ref[0], t3_ref[1], preferred_element_type=jnp.float32)
    s = s + jnp.dot(side_ref[0], t3_ref[2], preferred_element_type=jnp.float32)
    _finish(s, xp_ref, 0, out_ref, 0)
    s = jnp.dot(side_ref[1], t3_ref[0], preferred_element_type=jnp.float32)
    s = s + jnp.dot(edge_ref[1], t3_ref[1], preferred_element_type=jnp.float32)
    s = s + jnp.dot(after_ref[0], t3_ref[2], preferred_element_type=jnp.float32)
    _finish(s, xp_ref, frames - 1, out_ref, 1)


def block_two(above, rowed, below, spatial_kernel, temporal_kernel):
    frames, rows, width, channels = rowed.shape
    mids = spatial_kernel.shape[2]
    w9 = jnp.transpose(spatial_kernel, (0, 1, 3, 2)).reshape(9 * channels, mids)
    t3 = jnp.transpose(temporal_kernel, (0, 2, 1))
    vmem = pltpu.MemorySpace.VMEM if hasattr(pltpu, "MemorySpace") else pltpu.VMEM
    params = pltpu.CompilerParams(vmem_limit_bytes=48 * 1024 * 1024)
    spec = pl.BlockSpec(memory_space=vmem)
    plane = (rows * width, mids)
    edges = pl.pallas_call(
        _edges_two_kernel,
        out_shape=jax.ShapeDtypeStruct((2,) + plane, rowed.dtype),
        in_specs=[spec] * 4,
        out_specs=spec,
        compiler_params=params,
        cost_estimate=pl.CostEstimate(
            flops=2 * 2 * rows * width * 9 * channels * mids, bytes_accessed=2 * rowed.size, transcendentals=0
        ),
    )(above, rowed, below, w9)
    before = from_behind(edges[1:], "tm", 1)
    after = from_behind(edges[:1], "tm", -1)
    inner, side = pl.pallas_call(
        _inner_two_kernel,
        out_shape=(
            jax.ShapeDtypeStruct((frames - 2, rows, width, channels), rowed.dtype),
            jax.ShapeDtypeStruct((2,) + plane, rowed.dtype),
        ),
        in_specs=[spec] * 5,
        out_specs=(spec, spec),
        scratch_shapes=[pltpu.VMEM((frames,) + plane, jnp.bfloat16)],
        compiler_params=params,
        cost_estimate=pl.CostEstimate(
            flops=2 * frames * rows * width * (9 * channels * mids + 3 * mids * channels),
            bytes_accessed=4 * rowed.size,
            transcendentals=0,
        ),
    )(above, rowed, below, w9, t3)
    outer = pl.pallas_call(
        _outer_two_kernel,
        out_shape=jax.ShapeDtypeStruct((2, rows, width, channels), rowed.dtype),
        in_specs=[spec] * 6,
        out_specs=spec,
        compiler_params=params,
    )(rowed, t3, before, after, edges, side)
    return jnp.concatenate([outer[:1], inner, outer[1:]], axis=0)


def _copy_kernel(top_ref, bottom_ref, top_out, bottom_out):
    top_out[...] = top_ref[...]
    bottom_out[...] = bottom_ref[...]


def edge_rows(block, top, bottom):
    frames, rows, channels, width = block.shape
    top_spec = pl.BlockSpec((frames, top, channels, width), lambda i: (0, rows // top - 1, 0, 0))
    bottom_spec = pl.BlockSpec((frames, bottom, channels, width), lambda i: (0, 0, 0, 0))
    return pl.pallas_call(
        _copy_kernel,
        grid=(1,),
        out_shape=(
            jax.ShapeDtypeStruct((frames, top, channels, width), block.dtype),
            jax.ShapeDtypeStruct((frames, bottom, channels, width), block.dtype),
        ),
        in_specs=[top_spec, bottom_spec],
        out_specs=(pl.BlockSpec((frames, top, channels, width), lambda i: (0, 0, 0, 0)), bottom_spec),
    )(block, block)


def on_device(video_clip, spatial_one, temporal_one, down_weight, spatial_two, temporal_two):
    rows = video_clip.shape[1]
    top, bottom = edge_rows(video_clip, 2, 1)
    above = from_behind(top, "row", 1)
    below = from_behind(bottom, "row", -1)
    keep_first = (lax.axis_index("row") > 0).astype(jnp.int32).reshape(1)
    reduced = block_one(above, video_clip, below, keep_first, spatial_one, temporal_one, down_weight)
    rows = reduced.shape[1]
    above = from_behind(reduced[:, rows - 1 :], "row", 1)
    below = from_behind(reduced[:, :1], "row", -1)
    return block_two(above, reduced, below, spatial_two, temporal_two)


def solution(mesh):
    placed = (P("tm", "row", None, None), P(), P(), P(), P(), P())
    return jax.shard_map(
        on_device, mesh=mesh, in_specs=placed, out_specs=P("tm", "row", None, None), check_vma=False
    )
```

```python
import functools

import jax
import jax.numpy as jnp
from jax import lax
from jax.experimental import pallas as pl
from jax.experimental.pallas import tpu as pltpu
from jax.sharding import PartitionSpec as P


def padded_2(block, sides, width):
    for axis, dim in sides:
        count = lax.axis_size(axis)
        forward = [(i, i + 1) for i in range(count - 1)]
        backward = [(target, source) for source, target in forward]
        low = lax.ppermute(
            lax.slice_in_dim(block, block.shape[dim] - width, None, axis=dim), axis, forward
        )
        high = lax.ppermute(lax.slice_in_dim(block, 0, width, axis=dim), axis, backward)
        block = jnp.concatenate([low, block, high], axis=dim)
    return block


def from_behind(array, axis, by):
    devices = lax.axis_size(axis)
    pairs = [(i, i + by) for i in range(devices) if 0 <= i + by < devices]
    return lax.ppermute(array, axis, pairs)


def spatial(source, kernel, layout):
    return lax.conv_general_dilated(
        source,
        kernel,
        (1, 1),
        ((0, 0), (1, 1)),
        dimension_numbers=(layout, "HWOI", layout),
        preferred_element_type=jnp.float32,
    )


def temporal(source, kernel, layout):
    return lax.conv_general_dilated(
        source,
        kernel[:, None],
        (1, 1),
        ((0, 0), (0, 0)),
        dimension_numbers=(layout, "HWOI", layout),
        preferred_element_type=jnp.float32,
    )


def residual_block(source, spatial_kernel, temporal_kernel, space_layout, time_layout):
    padded = padded_2(source, (("tm", 0), ("row", 1)), 1)
    framed = jax.nn.relu(spatial(padded, spatial_kernel, space_layout)).astype(jnp.bfloat16)
    summed = source.astype(jnp.float32) + temporal(framed, temporal_kernel, time_layout)
    return jax.nn.relu(summed).astype(jnp.bfloat16)


def _lane_shift(x, by):
    width = x.shape[-1]
    rolled = pltpu.roll(x, (-by) % width, x.ndim - 1)
    lane = lax.broadcasted_iota(jnp.int32, x.shape, x.ndim - 1)
    inside = jnp.logical_and(lane + by >= 0, lane + by < width)
    return jnp.where(inside, rolled, jnp.zeros_like(rolled))


def _middle_one(refs, f, w9_ref, count=1):
    above_ref, xp_ref, below_ref = refs
    rows = xp_ref.shape[1] + 1
    columns = []
    for k in range(count):
        slab = jnp.concatenate([above_ref[f + k], xp_ref[f + k], below_ref[f + k]], axis=0).astype(jnp.float32)
        shifted = [_lane_shift(slab, b - 1).astype(jnp.bfloat16) for b in range(3)]
        parts = []
        for a in range(3):
            for b in range(3):
                parts.append(jnp.concatenate([shifted[b][h + a] for h in range(rows)], axis=1))
        columns.append(jnp.concatenate(parts, axis=0))
    stacked = columns[0] if count == 1 else jnp.concatenate(columns, axis=1)
    m = jnp.dot(w9_ref[...], stacked, preferred_element_type=jnp.float32)
    return jnp.maximum(m, 0.0).astype(jnp.bfloat16)


def _section_down(stacked, refs, t, t3_ref, wd_ref, keep_ref, out_ref, slot):
    s = jnp.dot(t3_ref[...], stacked, preferred_element_type=jnp.float32)
    _down(s, refs, t, wd_ref, keep_ref, out_ref, slot)


def _down(s, refs, t, wd_ref, keep_ref, out_ref, slot):
    above_ref, xp_ref, _ = refs
    rows = xp_ref.shape[1] + 1
    width = xp_ref.shape[-1]
    reduced_rows = (rows - 1) // 2
    lane = lax.broadcasted_iota(jnp.int32, (width // 2, width), 1)
    column = lax.broadcasted_iota(jnp.int32, (width // 2, width), 0)
    pick = (lane == 2 * column).astype(jnp.bfloat16)
    sec = []
    for h in range(rows):
        own = above_ref[t, 1] if h == 0 else xp_ref[t, h - 1]
        v = s[:, h * width : (h + 1) * width] + own.astype(jnp.float32)
        v = jnp.maximum(v, 0.0)
        if h == 0:
            v = v * keep_ref[0].astype(jnp.float32)
        sec.append(v.astype(jnp.bfloat16).astype(jnp.float32))
    shifted = [[_lane_shift(r, b - 1).astype(jnp.bfloat16) for b in range(3)] for r in sec]
    parts = []
    for a in range(3):
        for b in range(3):
            parts.append(jnp.concatenate([shifted[2 * i + a][b] for i in range(reduced_rows)], axis=1))
    stacked = jnp.concatenate(parts, axis=0)
    full = jnp.dot(wd_ref[...], stacked, preferred_element_type=jnp.float32)
    full = jnp.maximum(full, 0.0).astype(jnp.bfloat16)
    outs = full.shape[0]
    rows_by_d = jnp.concatenate([full[:, i * width : (i + 1) * width] for i in range(reduced_rows)], axis=0)
    r = lax.dot_general(pick, rows_by_d, (((1,), (1,)), ((), ())), preferred_element_type=jnp.float32)
    for i in range(reduced_rows):
        out_ref[slot, i] = r[:, i * outs : (i + 1) * outs].astype(out_ref.dtype)


def _edges_one_kernel(above_ref, xp_ref, below_ref, w9_ref, edge_ref):
    refs = (above_ref, xp_ref, below_ref)
    frames = xp_ref.shape[0]
    edge_ref[0] = _middle_one(refs, 0, w9_ref)
    edge_ref[1] = _middle_one(refs, frames - 1, w9_ref)


def _inner_one_kernel(keep_ref, above_ref, xp_ref, below_ref, w9_ref, t3_ref, wd_ref, out_ref, side_ref, mid_ref):
    refs = (above_ref, xp_ref, below_ref)
    frames = xp_ref.shape[0]

    span = mid_ref.shape[-1]
    group = 4 if frames % 4 == 0 else 2

    def middle(g, carry):
        m = _middle_one(refs, group * g, w9_ref, group)
        for k in range(group):
            mid_ref[group * g + k] = m[:, k * span : (k + 1) * span]
        return carry

    lax.fori_loop(0, frames // group, middle, 0)
    side_ref[0] = mid_ref[1]
    side_ref[1] = mid_ref[frames - 2]

    channels = t3_ref.shape[0] // 2

    def section(g, carry):
        t = 2 * g + 1
        stacked = jnp.concatenate([mid_ref[t - 1], mid_ref[t], mid_ref[t + 1], mid_ref[t + 2]], axis=0)
        s = jnp.dot(t3_ref[...], stacked, preferred_element_type=jnp.float32)
        _down(s[:channels], refs, t, wd_ref, keep_ref, out_ref, t - 1)
        _down(s[channels:], refs, t + 1, wd_ref, keep_ref, out_ref, t)
        return carry

    lax.fori_loop(0, (frames - 2) // 2, section, 0)


def _outer_one_kernel(
    keep_ref, above_ref, xp_ref, below_ref, t3_ref, wd_ref, before_ref, after_ref, edge_ref, side_ref, out_ref
):
    refs = (above_ref, xp_ref, below_ref)
    frames = xp_ref.shape[0]
    stacked = jnp.concatenate([before_ref[0], edge_ref[0], side_ref[0]], axis=0)
    _section_down(stacked, refs, 0, t3_ref, wd_ref, keep_ref, out_ref, 0)
    stacked = jnp.concatenate([side_ref[1], edge_ref[1], after_ref[0]], axis=0)
    _section_down(stacked, refs, frames - 1, t3_ref, wd_ref, keep_ref, out_ref, 1)


def block_one(above, rowed, below, keep_first, spatial_kernel, temporal_kernel, down_kernel):
    frames, rows, channels, width = rowed.shape
    rows = rows + 1
    mids = spatial_kernel.shape[2]
    outs = down_kernel.shape[2]
    w9 = jnp.transpose(spatial_kernel, (2, 0, 1, 3)).reshape(mids, 9 * channels)
    t3 = jnp.transpose(temporal_kernel, (1, 0, 2)).reshape(channels, 3 * mids)
    wd = jnp.transpose(down_kernel, (2, 0, 1, 3)).reshape(outs, 9 * channels)
    gap = jnp.zeros((channels, mids), t3.dtype)
    t4 = jnp.concatenate(
        [jnp.concatenate([t3, gap], axis=1), jnp.concatenate([gap, t3], axis=1)], axis=0
    )
    vmem = pltpu.MemorySpace.VMEM if hasattr(pltpu, "MemorySpace") else pltpu.VMEM
    smem = pltpu.MemorySpace.SMEM if hasattr(pltpu, "MemorySpace") else pltpu.SMEM
    params = pltpu.CompilerParams(vmem_limit_bytes=48 * 1024 * 1024)
    spec = pl.BlockSpec(memory_space=vmem)
    sspec = pl.BlockSpec(memory_space=smem)
    reduced_rows = (rows - 1) // 2
    plane = (mids, rows * width)
    out_plane = (reduced_rows, width // 2, outs)
    spatial_flops = 2 * rows * width * 9 * channels * mids
    section_flops = 2 * rows * width * 3 * mids * channels + 2 * reduced_rows * width * 9 * channels * outs
    edges = pl.pallas_call(
        _edges_one_kernel,
        out_shape=jax.ShapeDtypeStruct((2,) + plane, rowed.dtype),
        in_specs=[spec] * 4,
        out_specs=spec,
        compiler_params=params,
        cost_estimate=pl.CostEstimate(flops=2 * spatial_flops, bytes_accessed=2 * rowed.size, transcendentals=0),
    )(above, rowed, below, w9)
    before = from_behind(edges[1:], "tm", 1)
    after = from_behind(edges[:1], "tm", -1)
    inner, side = pl.pallas_call(
        _inner_one_kernel,
        out_shape=(
            jax.ShapeDtypeStruct((frames - 2,) + out_plane, rowed.dtype),
            jax.ShapeDtypeStruct((2,) + plane, rowed.dtype),
        ),
        in_specs=[sspec] + [spec] * 6,
        out_specs=(spec, spec),
        scratch_shapes=[pltpu.VMEM((frames,) + plane, jnp.bfloat16)],
        compiler_params=params,
        cost_estimate=pl.CostEstimate(
            flops=frames * (spatial_flops + section_flops), bytes_accessed=4 * rowed.size, transcendentals=0
        ),
    )(keep_first, above, rowed, below, w9, t4, wd)
    outer = pl.pallas_call(
        _outer_one_kernel,
        out_shape=jax.ShapeDtypeStruct((2,) + out_plane, rowed.dtype),
        in_specs=[sspec] + [spec] * 9,
        out_specs=spec,
        compiler_params=params,
    )(keep_first, above, rowed, below, t3, wd, before, after, edges, side)
    return jnp.concatenate([outer[:1], inner, outer[1:]], axis=0)


def _sublane_shift(x, by, axis):
    size = x.shape[axis]
    rolled = pltpu.roll(x, (-by) % size, axis)
    index = lax.broadcasted_iota(jnp.int32, x.shape, axis)
    inside = jnp.logical_and(index + by >= 0, index + by < size)
    return jnp.where(inside, rolled, jnp.zeros_like(rolled))


def _slab_two(above_ref, xp_ref, below_ref, f):
    return jnp.concatenate([above_ref[f], xp_ref[f], below_ref[f]], axis=0).astype(jnp.float32)


def _middle_two(slabs, w9_ref):
    rows = slabs[0].shape[0] - 2
    pieces = []
    for slab in slabs:
        shifted = [_sublane_shift(slab, b - 1, 1).astype(jnp.bfloat16) for b in range(3)]
        for i in range(rows):
            pieces.append(jnp.concatenate([shifted[b][i + a] for a in range(3) for b in range(3)], axis=1))
    stacked = jnp.concatenate(pieces, axis=0)
    m = jnp.dot(stacked, w9_ref[...], preferred_element_type=jnp.float32)
    return jnp.maximum(m, 0.0).astype(jnp.bfloat16)


def _edges_two_kernel(above_ref, xp_ref, below_ref, w9_ref, edge_ref):
    frames = xp_ref.shape[0]
    plane = edge_ref.shape[1]
    m = _middle_two(
        [_slab_two(above_ref, xp_ref, below_ref, 0), _slab_two(above_ref, xp_ref, below_ref, frames - 1)], w9_ref
    )
    edge_ref[0] = m[:plane]
    edge_ref[1] = m[plane:]


def _finish(s, xp_ref, t, out_ref, slot):
    rows, width = xp_ref.shape[1], xp_ref.shape[2]
    for i in range(rows):
        v = s[i * width : (i + 1) * width] + xp_ref[t, i].astype(jnp.float32)
        out_ref[slot, i] = jnp.maximum(v, 0.0).astype(out_ref.dtype)


def _inner_two_kernel(above_ref, xp_ref, below_ref, w9_ref, t3_ref, out_ref, side_ref, mid_ref):
    frames = xp_ref.shape[0]
    plane = mid_ref.shape[1]

    group = 4 if frames % 4 == 0 else 2

    def middle(g, carry):
        f = group * g
        m = _middle_two([_slab_two(above_ref, xp_ref, below_ref, f + k) for k in range(group)], w9_ref)
        for k in range(group):
            mid_ref[f + k] = m[k * plane : (k + 1) * plane]
        return carry

    lax.fori_loop(0, frames // group, middle, 0)
    side_ref[0] = mid_ref[1]
    side_ref[1] = mid_ref[frames - 2]

    def section(g, carry):
        t = 2 * g + 1
        s = None
        for k in range(3):
            pair = jnp.concatenate([mid_ref[t - 1 + k], mid_ref[t + k]], axis=0)
            d = jnp.dot(pair, t3_ref[k], preferred_element_type=jnp.float32)
            s = d if s is None else s + d
        _finish(s[:plane], xp_ref, t, out_ref, t - 1)
        _finish(s[plane:], xp_ref, t + 1, out_ref, t)
        return carry

    lax.fori_loop(0, (frames - 2) // 2, section, 0)


def _outer_two_kernel(xp_ref, t3_ref, before_ref, after_ref, edge_ref, side_ref, out_ref):
    frames = xp_ref.shape[0]
    s = jnp.dot(before_ref[0], t3_ref[0], preferred_element_type=jnp.float32)
    s = s + jnp.dot(edge_ref[0], t3_ref[1], preferred_element_type=jnp.float32)
    s = s + jnp.dot(side_ref[0], t3_ref[2], preferred_element_type=jnp.float32)
    _finish(s, xp_ref, 0, out_ref, 0)
    s = jnp.dot(side_ref[1], t3_ref[0], preferred_element_type=jnp.float32)
    s = s + jnp.dot(edge_ref[1], t3_ref[1], preferred_element_type=jnp.float32)
    s = s + jnp.dot(after_ref[0], t3_ref[2], preferred_element_type=jnp.float32)
    _finish(s, xp_ref, frames - 1, out_ref, 1)


def block_two(above, rowed, below, spatial_kernel, temporal_kernel):
    frames, rows, width, channels = rowed.shape
    mids = spatial_kernel.shape[2]
    w9 = jnp.transpose(spatial_kernel, (0, 1, 3, 2)).reshape(9 * channels, mids)
    t3 = jnp.transpose(temporal_kernel, (0, 2, 1))
    vmem = pltpu.MemorySpace.VMEM if hasattr(pltpu, "MemorySpace") else pltpu.VMEM
    params = pltpu.CompilerParams(vmem_limit_bytes=48 * 1024 * 1024)
    spec = pl.BlockSpec(memory_space=vmem)
    plane = (rows * width, mids)
    edges = pl.pallas_call(
        _edges_two_kernel,
        out_shape=jax.ShapeDtypeStruct((2,) + plane, rowed.dtype),
        in_specs=[spec] * 4,
        out_specs=spec,
        compiler_params=params,
        cost_estimate=pl.CostEstimate(
            flops=2 * 2 * rows * width * 9 * channels * mids, bytes_accessed=2 * rowed.size, transcendentals=0
        ),
    )(above, rowed, below, w9)
    before = from_behind(edges[1:], "tm", 1)
    after = from_behind(edges[:1], "tm", -1)
    inner, side = pl.pallas_call(
        _inner_two_kernel,
        out_shape=(
            jax.ShapeDtypeStruct((frames - 2, rows, width, channels), rowed.dtype),
            jax.ShapeDtypeStruct((2,) + plane, rowed.dtype),
        ),
        in_specs=[spec] * 5,
        out_specs=(spec, spec),
        scratch_shapes=[pltpu.VMEM((frames,) + plane, jnp.bfloat16)],
        compiler_params=params,
        cost_estimate=pl.CostEstimate(
            flops=2 * frames * rows * width * (9 * channels * mids + 3 * mids * channels),
            bytes_accessed=4 * rowed.size,
            transcendentals=0,
        ),
    )(above, rowed, below, w9, t3)
    outer = pl.pallas_call(
        _outer_two_kernel,
        out_shape=jax.ShapeDtypeStruct((2, rows, width, channels), rowed.dtype),
        in_specs=[spec] * 6,
        out_specs=spec,
        compiler_params=params,
    )(rowed, t3, before, after, edges, side)
    return jnp.concatenate([outer[:1], inner, outer[1:]], axis=0)


def _copy_kernel(top_ref, bottom_ref, top_out, bottom_out):
    top_out[...] = top_ref[...]
    bottom_out[...] = bottom_ref[...]


def edge_rows(block, top, bottom):
    frames, rows, channels, width = block.shape
    top_spec = pl.BlockSpec((frames, top, channels, width), lambda i: (0, rows // top - 1, 0, 0))
    bottom_spec = pl.BlockSpec((frames, bottom, channels, width), lambda i: (0, 0, 0, 0))
    return pl.pallas_call(
        _copy_kernel,
        grid=(1,),
        out_shape=(
            jax.ShapeDtypeStruct((frames, top, channels, width), block.dtype),
            jax.ShapeDtypeStruct((frames, bottom, channels, width), block.dtype),
        ),
        in_specs=[top_spec, bottom_spec],
        out_specs=(pl.BlockSpec((frames, top, channels, width), lambda i: (0, 0, 0, 0)), bottom_spec),
    )(block, block)


def on_device(video_clip, spatial_one, temporal_one, down_weight, spatial_two, temporal_two):
    rows = video_clip.shape[1]
    top, bottom = edge_rows(video_clip, 2, 1)
    above = from_behind(top, "row", 1)
    below = from_behind(bottom, "row", -1)
    keep_first = (lax.axis_index("row") > 0).astype(jnp.int32).reshape(1)
    reduced = block_one(above, video_clip, below, keep_first, spatial_one, temporal_one, down_weight)
    rows = reduced.shape[1]
    above = from_behind(reduced[:, rows - 1 :], "row", 1)
    below = from_behind(reduced[:, :1], "row", -1)
    return block_two(above, reduced, below, spatial_two, temporal_two)


def solution(mesh):
    placed = (P("tm", "row", None, None), P(), P(), P(), P(), P())
    return jax.shard_map(
        on_device, mesh=mesh, in_specs=placed, out_specs=P("tm", "row", None, None), check_vma=False
    )
```

```python
import functools

import jax
import jax.numpy as jnp
from jax import lax
from jax.experimental import pallas as pl
from jax.experimental.pallas import tpu as pltpu
from jax.sharding import PartitionSpec as P


def padded_2(block, sides, width):
    for axis, dim in sides:
        count = lax.axis_size(axis)
        forward = [(i, i + 1) for i in range(count - 1)]
        backward = [(target, source) for source, target in forward]
        low = lax.ppermute(
            lax.slice_in_dim(block, block.shape[dim] - width, None, axis=dim), axis, forward
        )
        high = lax.ppermute(lax.slice_in_dim(block, 0, width, axis=dim), axis, backward)
        block = jnp.concatenate([low, block, high], axis=dim)
    return block


def from_behind(array, axis, by):
    devices = lax.axis_size(axis)
    pairs = [(i, i + by) for i in range(devices) if 0 <= i + by < devices]
    return lax.ppermute(array, axis, pairs)


def spatial(source, kernel, layout):
    return lax.conv_general_dilated(
        source,
        kernel,
        (1, 1),
        ((0, 0), (1, 1)),
        dimension_numbers=(layout, "HWOI", layout),
        preferred_element_type=jnp.float32,
    )


def temporal(source, kernel, layout):
    return lax.conv_general_dilated(
        source,
        kernel[:, None],
        (1, 1),
        ((0, 0), (0, 0)),
        dimension_numbers=(layout, "HWOI", layout),
        preferred_element_type=jnp.float32,
    )


def residual_block(source, spatial_kernel, temporal_kernel, space_layout, time_layout):
    padded = padded_2(source, (("tm", 0), ("row", 1)), 1)
    framed = jax.nn.relu(spatial(padded, spatial_kernel, space_layout)).astype(jnp.bfloat16)
    summed = source.astype(jnp.float32) + temporal(framed, temporal_kernel, time_layout)
    return jax.nn.relu(summed).astype(jnp.bfloat16)


def _lane_shift(x, by):
    width = x.shape[-1]
    rolled = pltpu.roll(x, (-by) % width, x.ndim - 1)
    lane = lax.broadcasted_iota(jnp.int32, x.shape, x.ndim - 1)
    inside = jnp.logical_and(lane + by >= 0, lane + by < width)
    return jnp.where(inside, rolled, jnp.zeros_like(rolled))


def _middle_one(refs, fs, w9_ref):
    above_ref, xp_ref, below_ref = refs
    rows = xp_ref.shape[1] + 1
    columns = []
    for f in fs:
        slab = jnp.concatenate([above_ref[f], xp_ref[f], below_ref[f]], axis=0).astype(jnp.float32)
        shifted = [_lane_shift(slab, b - 1).astype(jnp.bfloat16) for b in range(3)]
        parts = []
        for a in range(3):
            for b in range(3):
                parts.append(jnp.concatenate([shifted[b][h + a] for h in range(rows)], axis=1))
        columns.append(jnp.concatenate(parts, axis=0))
    stacked = columns[0] if len(columns) == 1 else jnp.concatenate(columns, axis=1)
    m = jnp.dot(w9_ref[...], stacked, preferred_element_type=jnp.float32)
    return jnp.maximum(m, 0.0).astype(jnp.bfloat16)


def _section_down(stacked, refs, t, t3_ref, wd_ref, keep_ref, out_ref, slot):
    s = jnp.dot(t3_ref[...], stacked, preferred_element_type=jnp.float32)
    _down(s, refs, t, wd_ref, keep_ref, out_ref, slot)


def _down(s, refs, t, wd_ref, keep_ref, out_ref, slot):
    above_ref, xp_ref, _ = refs
    rows = xp_ref.shape[1] + 1
    width = xp_ref.shape[-1]
    reduced_rows = (rows - 1) // 2
    lane = lax.broadcasted_iota(jnp.int32, (width // 2, width), 1)
    column = lax.broadcasted_iota(jnp.int32, (width // 2, width), 0)
    pick = (lane == 2 * column).astype(jnp.bfloat16)
    sec = []
    for h in range(rows):
        own = above_ref[t, 1] if h == 0 else xp_ref[t, h - 1]
        v = s[:, h * width : (h + 1) * width] + own.astype(jnp.float32)
        v = jnp.maximum(v, 0.0)
        if h == 0:
            v = v * keep_ref[0].astype(jnp.float32)
        sec.append(v.astype(jnp.bfloat16).astype(jnp.float32))
    shifted = [[_lane_shift(r, b - 1).astype(jnp.bfloat16) for b in range(3)] for r in sec]
    parts = []
    for a in range(3):
        for b in range(3):
            parts.append(jnp.concatenate([shifted[2 * i + a][b] for i in range(reduced_rows)], axis=1))
    stacked = jnp.concatenate(parts, axis=0)
    full = jnp.dot(wd_ref[...], stacked, preferred_element_type=jnp.float32)
    full = jnp.maximum(full, 0.0).astype(jnp.bfloat16)
    outs = full.shape[0]
    rows_by_d = jnp.concatenate([full[:, i * width : (i + 1) * width] for i in range(reduced_rows)], axis=0)
    r = lax.dot_general(pick, rows_by_d, (((1,), (1,)), ((), ())), preferred_element_type=jnp.float32)
    for i in range(reduced_rows):
        out_ref[slot, i] = r[:, i * outs : (i + 1) * outs].astype(out_ref.dtype)


def _edges_one_kernel(above_ref, xp_ref, below_ref, w9_ref, edge_ref):
    refs = (above_ref, xp_ref, below_ref)
    frames = xp_ref.shape[0]
    span = edge_ref.shape[-1]
    m = _middle_one(refs, [0, frames - 1], w9_ref)
    edge_ref[0] = m[:, :span]
    edge_ref[1] = m[:, span:]


def _inner_one_kernel(keep_ref, above_ref, xp_ref, below_ref, w9_ref, t3_ref, wd_ref, out_ref, side_ref, mid_ref):
    refs = (above_ref, xp_ref, below_ref)
    frames = xp_ref.shape[0]

    span = mid_ref.shape[-1]
    group = 4 if frames % 4 == 0 else 2

    def middle(g, carry):
        m = _middle_one(refs, [group * g + k for k in range(group)], w9_ref)
        for k in range(group):
            mid_ref[group * g + k] = m[:, k * span : (k + 1) * span]
        return carry

    lax.fori_loop(0, frames // group, middle, 0)
    side_ref[0] = mid_ref[1]
    side_ref[1] = mid_ref[frames - 2]

    channels = t3_ref.shape[0] // 2

    def section(g, carry):
        t = 2 * g + 1
        stacked = jnp.concatenate([mid_ref[t - 1], mid_ref[t], mid_ref[t + 1], mid_ref[t + 2]], axis=0)
        s = jnp.dot(t3_ref[...], stacked, preferred_element_type=jnp.float32)
        _down(s[:channels], refs, t, wd_ref, keep_ref, out_ref, t - 1)
        _down(s[channels:], refs, t + 1, wd_ref, keep_ref, out_ref, t)
        return carry

    lax.fori_loop(0, (frames - 2) // 2, section, 0)


def _outer_one_kernel(
    keep_ref, above_ref, xp_ref, below_ref, t3_ref, wd_ref, before_ref, after_ref, edge_ref, side_ref, out_ref
):
    refs = (above_ref, xp_ref, below_ref)
    frames = xp_ref.shape[0]
    stacked = jnp.concatenate([before_ref[0], edge_ref[0], side_ref[0]], axis=0)
    _section_down(stacked, refs, 0, t3_ref, wd_ref, keep_ref, out_ref, 0)
    stacked = jnp.concatenate([side_ref[1], edge_ref[1], after_ref[0]], axis=0)
    _section_down(stacked, refs, frames - 1, t3_ref, wd_ref, keep_ref, out_ref, 1)


def block_one(above, rowed, below, keep_first, spatial_kernel, temporal_kernel, down_kernel):
    frames, rows, channels, width = rowed.shape
    rows = rows + 1
    mids = spatial_kernel.shape[2]
    outs = down_kernel.shape[2]
    w9 = jnp.transpose(spatial_kernel, (2, 0, 1, 3)).reshape(mids, 9 * channels)
    t3 = jnp.transpose(temporal_kernel, (1, 0, 2)).reshape(channels, 3 * mids)
    wd = jnp.transpose(down_kernel, (2, 0, 1, 3)).reshape(outs, 9 * channels)
    gap = jnp.zeros((channels, mids), t3.dtype)
    t4 = jnp.concatenate(
        [jnp.concatenate([t3, gap], axis=1), jnp.concatenate([gap, t3], axis=1)], axis=0
    )
    vmem = pltpu.MemorySpace.VMEM if hasattr(pltpu, "MemorySpace") else pltpu.VMEM
    smem = pltpu.MemorySpace.SMEM if hasattr(pltpu, "MemorySpace") else pltpu.SMEM
    params = pltpu.CompilerParams(vmem_limit_bytes=48 * 1024 * 1024)
    spec = pl.BlockSpec(memory_space=vmem)
    sspec = pl.BlockSpec(memory_space=smem)
    reduced_rows = (rows - 1) // 2
    plane = (mids, rows * width)
    out_plane = (reduced_rows, width // 2, outs)
    spatial_flops = 2 * rows * width * 9 * channels * mids
    section_flops = 2 * rows * width * 3 * mids * channels + 2 * reduced_rows * width * 9 * channels * outs
    edges = pl.pallas_call(
        _edges_one_kernel,
        out_shape=jax.ShapeDtypeStruct((2,) + plane, rowed.dtype),
        in_specs=[spec] * 4,
        out_specs=spec,
        compiler_params=params,
        cost_estimate=pl.CostEstimate(flops=2 * spatial_flops, bytes_accessed=2 * rowed.size, transcendentals=0),
    )(above, rowed, below, w9)
    before = from_behind(edges[1:], "tm", 1)
    after = from_behind(edges[:1], "tm", -1)
    inner, side = pl.pallas_call(
        _inner_one_kernel,
        out_shape=(
            jax.ShapeDtypeStruct((frames - 2,) + out_plane, rowed.dtype),
            jax.ShapeDtypeStruct((2,) + plane, rowed.dtype),
        ),
        in_specs=[sspec] + [spec] * 6,
        out_specs=(spec, spec),
        scratch_shapes=[pltpu.VMEM((frames,) + plane, jnp.bfloat16)],
        compiler_params=params,
        cost_estimate=pl.CostEstimate(
            flops=frames * (spatial_flops + section_flops), bytes_accessed=4 * rowed.size, transcendentals=0
        ),
    )(keep_first, above, rowed, below, w9, t4, wd)
    outer = pl.pallas_call(
        _outer_one_kernel,
        out_shape=jax.ShapeDtypeStruct((2,) + out_plane, rowed.dtype),
        in_specs=[sspec] + [spec] * 9,
        out_specs=spec,
        compiler_params=params,
    )(keep_first, above, rowed, below, t3, wd, before, after, edges, side)
    return jnp.concatenate([outer[:1], inner, outer[1:]], axis=0)


def _sublane_shift(x, by, axis):
    size = x.shape[axis]
    rolled = pltpu.roll(x, (-by) % size, axis)
    index = lax.broadcasted_iota(jnp.int32, x.shape, axis)
    inside = jnp.logical_and(index + by >= 0, index + by < size)
    return jnp.where(inside, rolled, jnp.zeros_like(rolled))


def _slab_two(above_ref, xp_ref, below_ref, f):
    return jnp.concatenate([above_ref[f], xp_ref[f], below_ref[f]], axis=0).astype(jnp.float32)


def _middle_two(slabs, w9_ref):
    rows = slabs[0].shape[0] - 2
    pieces = []
    for slab in slabs:
        shifted = [_sublane_shift(slab, b - 1, 1).astype(jnp.bfloat16) for b in range(3)]
        for i in range(rows):
            pieces.append(jnp.concatenate([shifted[b][i + a] for a in range(3) for b in range(3)], axis=1))
    stacked = jnp.concatenate(pieces, axis=0)
    m = jnp.dot(stacked, w9_ref[...], preferred_element_type=jnp.float32)
    return jnp.maximum(m, 0.0).astype(jnp.bfloat16)


def _edges_two_kernel(above_ref, xp_ref, below_ref, w9_ref, edge_ref):
    frames = xp_ref.shape[0]
    plane = edge_ref.shape[1]
    m = _middle_two(
        [_slab_two(above_ref, xp_ref, below_ref, 0), _slab_two(above_ref, xp_ref, below_ref, frames - 1)], w9_ref
    )
    edge_ref[0] = m[:plane]
    edge_ref[1] = m[plane:]


def _finish(s, xp_ref, t, out_ref, slot):
    rows, width = xp_ref.shape[1], xp_ref.shape[2]
    for i in range(rows):
        v = s[i * width : (i + 1) * width] + xp_ref[t, i].astype(jnp.float32)
        out_ref[slot, i] = jnp.maximum(v, 0.0).astype(out_ref.dtype)


def _inner_two_kernel(above_ref, xp_ref, below_ref, w9_ref, t3_ref, out_ref, side_ref, mid_ref):
    frames = xp_ref.shape[0]
    plane = mid_ref.shape[1]

    group = 8 if frames % 8 == 0 else 2

    def middle(g, carry):
        f = group * g
        m = _middle_two([_slab_two(above_ref, xp_ref, below_ref, f + k) for k in range(group)], w9_ref)
        for k in range(group):
            mid_ref[f + k] = m[k * plane : (k + 1) * plane]
        return carry

    lax.fori_loop(0, frames // group, middle, 0)
    side_ref[0] = mid_ref[1]
    side_ref[1] = mid_ref[frames - 2]

    def section(g, carry):
        t = 2 * g + 1
        s = None
        for k in range(3):
            pair = jnp.concatenate([mid_ref[t - 1 + k], mid_ref[t + k]], axis=0)
            d = jnp.dot(pair, t3_ref[k], preferred_element_type=jnp.float32)
            s = d if s is None else s + d
        _finish(s[:plane], xp_ref, t, out_ref, t - 1)
        _finish(s[plane:], xp_ref, t + 1, out_ref, t)
        return carry

    lax.fori_loop(0, (frames - 2) // 2, section, 0)


def _outer_two_kernel(xp_ref, t3_ref, before_ref, after_ref, edge_ref, side_ref, out_ref):
    frames = xp_ref.shape[0]
    s = jnp.dot(before_ref[0], t3_ref[0], preferred_element_type=jnp.float32)
    s = s + jnp.dot(edge_ref[0], t3_ref[1], preferred_element_type=jnp.float32)
    s = s + jnp.dot(side_ref[0], t3_ref[2], preferred_element_type=jnp.float32)
    _finish(s, xp_ref, 0, out_ref, 0)
    s = jnp.dot(side_ref[1], t3_ref[0], preferred_element_type=jnp.float32)
    s = s + jnp.dot(edge_ref[1], t3_ref[1], preferred_element_type=jnp.float32)
    s = s + jnp.dot(after_ref[0], t3_ref[2], preferred_element_type=jnp.float32)
    _finish(s, xp_ref, frames - 1, out_ref, 1)


def block_two(above, rowed, below, spatial_kernel, temporal_kernel):
    frames, rows, width, channels = rowed.shape
    mids = spatial_kernel.shape[2]
    w9 = jnp.transpose(spatial_kernel, (0, 1, 3, 2)).reshape(9 * channels, mids)
    t3 = jnp.transpose(temporal_kernel, (0, 2, 1))
    vmem = pltpu.MemorySpace.VMEM if hasattr(pltpu, "MemorySpace") else pltpu.VMEM
    params = pltpu.CompilerParams(vmem_limit_bytes=48 * 1024 * 1024)
    spec = pl.BlockSpec(memory_space=vmem)
    plane = (rows * width, mids)
    edges = pl.pallas_call(
        _edges_two_kernel,
        out_shape=jax.ShapeDtypeStruct((2,) + plane, rowed.dtype),
        in_specs=[spec] * 4,
        out_specs=spec,
        compiler_params=params,
        cost_estimate=pl.CostEstimate(
            flops=2 * 2 * rows * width * 9 * channels * mids, bytes_accessed=2 * rowed.size, transcendentals=0
        ),
    )(above, rowed, below, w9)
    before = from_behind(edges[1:], "tm", 1)
    after = from_behind(edges[:1], "tm", -1)
    inner, side = pl.pallas_call(
        _inner_two_kernel,
        out_shape=(
            jax.ShapeDtypeStruct((frames - 2, rows, width, channels), rowed.dtype),
            jax.ShapeDtypeStruct((2,) + plane, rowed.dtype),
        ),
        in_specs=[spec] * 5,
        out_specs=(spec, spec),
        scratch_shapes=[pltpu.VMEM((frames,) + plane, jnp.bfloat16)],
        compiler_params=params,
        cost_estimate=pl.CostEstimate(
            flops=2 * frames * rows * width * (9 * channels * mids + 3 * mids * channels),
            bytes_accessed=4 * rowed.size,
            transcendentals=0,
        ),
    )(above, rowed, below, w9, t3)
    outer = pl.pallas_call(
        _outer_two_kernel,
        out_shape=jax.ShapeDtypeStruct((2, rows, width, channels), rowed.dtype),
        in_specs=[spec] * 6,
        out_specs=spec,
        compiler_params=params,
    )(rowed, t3, before, after, edges, side)
    return jnp.concatenate([outer[:1], inner, outer[1:]], axis=0)


def _copy_kernel(top_ref, bottom_ref, top_out, bottom_out):
    top_out[...] = top_ref[...]
    bottom_out[...] = bottom_ref[...]


def edge_rows(block, top, bottom):
    frames, rows, channels, width = block.shape
    top_spec = pl.BlockSpec((frames, top, channels, width), lambda i: (0, rows // top - 1, 0, 0))
    bottom_spec = pl.BlockSpec((frames, bottom, channels, width), lambda i: (0, 0, 0, 0))
    return pl.pallas_call(
        _copy_kernel,
        grid=(1,),
        out_shape=(
            jax.ShapeDtypeStruct((frames, top, channels, width), block.dtype),
            jax.ShapeDtypeStruct((frames, bottom, channels, width), block.dtype),
        ),
        in_specs=[top_spec, bottom_spec],
        out_specs=(pl.BlockSpec((frames, top, channels, width), lambda i: (0, 0, 0, 0)), bottom_spec),
    )(block, block)


def on_device(video_clip, spatial_one, temporal_one, down_weight, spatial_two, temporal_two):
    rows = video_clip.shape[1]
    top, bottom = edge_rows(video_clip, 2, 1)
    above = from_behind(top, "row", 1)
    below = from_behind(bottom, "row", -1)
    keep_first = (lax.axis_index("row") > 0).astype(jnp.int32).reshape(1)
    reduced = block_one(above, video_clip, below, keep_first, spatial_one, temporal_one, down_weight)
    rows = reduced.shape[1]
    above = from_behind(reduced[:, rows - 1 :], "row", 1)
    below = from_behind(reduced[:, :1], "row", -1)
    return block_two(above, reduced, below, spatial_two, temporal_two)


def solution(mesh):
    placed = (P("tm", "row", None, None), P(), P(), P(), P(), P())
    return jax.shard_map(
        on_device, mesh=mesh, in_specs=placed, out_specs=P("tm", "row", None, None), check_vma=False
    )
```

```python
import functools

import jax
import jax.numpy as jnp
from jax import lax
from jax.experimental import pallas as pl
from jax.experimental.pallas import tpu as pltpu
from jax.sharding import PartitionSpec as P


def padded_2(block, sides, width):
    for axis, dim in sides:
        count = lax.axis_size(axis)
        forward = [(i, i + 1) for i in range(count - 1)]
        backward = [(target, source) for source, target in forward]
        low = lax.ppermute(
            lax.slice_in_dim(block, block.shape[dim] - width, None, axis=dim), axis, forward
        )
        high = lax.ppermute(lax.slice_in_dim(block, 0, width, axis=dim), axis, backward)
        block = jnp.concatenate([low, block, high], axis=dim)
    return block


def from_behind(array, axis, by):
    devices = lax.axis_size(axis)
    pairs = [(i, i + by) for i in range(devices) if 0 <= i + by < devices]
    return lax.ppermute(array, axis, pairs)


def spatial(source, kernel, layout):
    return lax.conv_general_dilated(
        source,
        kernel,
        (1, 1),
        ((0, 0), (1, 1)),
        dimension_numbers=(layout, "HWOI", layout),
        preferred_element_type=jnp.float32,
    )


def temporal(source, kernel, layout):
    return lax.conv_general_dilated(
        source,
        kernel[:, None],
        (1, 1),
        ((0, 0), (0, 0)),
        dimension_numbers=(layout, "HWOI", layout),
        preferred_element_type=jnp.float32,
    )


def residual_block(source, spatial_kernel, temporal_kernel, space_layout, time_layout):
    padded = padded_2(source, (("tm", 0), ("row", 1)), 1)
    framed = jax.nn.relu(spatial(padded, spatial_kernel, space_layout)).astype(jnp.bfloat16)
    summed = source.astype(jnp.float32) + temporal(framed, temporal_kernel, time_layout)
    return jax.nn.relu(summed).astype(jnp.bfloat16)


def _lane_shift(x, by):
    width = x.shape[-1]
    rolled = pltpu.roll(x, (-by) % width, x.ndim - 1)
    lane = lax.broadcasted_iota(jnp.int32, x.shape, x.ndim - 1)
    inside = jnp.logical_and(lane + by >= 0, lane + by < width)
    return jnp.where(inside, rolled, jnp.zeros_like(rolled))


def _middle_one(refs, fs, w9_ref):
    above_ref, xp_ref, below_ref = refs
    rows = xp_ref.shape[1] + 1
    columns = []
    for f in fs:
        slab = jnp.concatenate([above_ref[f], xp_ref[f], below_ref[f]], axis=0).astype(jnp.float32)
        shifted = [_lane_shift(slab, b - 1).astype(jnp.bfloat16) for b in range(3)]
        parts = []
        for a in range(3):
            for b in range(3):
                parts.append(jnp.concatenate([shifted[b][h + a] for h in range(rows)], axis=1))
        columns.append(jnp.concatenate(parts, axis=0))
    stacked = columns[0] if len(columns) == 1 else jnp.concatenate(columns, axis=1)
    m = jnp.dot(w9_ref[...], stacked, preferred_element_type=jnp.float32)
    return jnp.maximum(m, 0.0).astype(jnp.bfloat16)


def _section_down(stacked, refs, t, t3_ref, wd_ref, keep_ref, out_ref, slot):
    s = jnp.dot(t3_ref[...], stacked, preferred_element_type=jnp.float32)
    _down(s, refs, t, wd_ref, keep_ref, out_ref, slot)


def _down(s, refs, t, wd_ref, keep_ref, out_ref, slot):
    above_ref, xp_ref, _ = refs
    rows = xp_ref.shape[1] + 1
    width = xp_ref.shape[-1]
    reduced_rows = (rows - 1) // 2
    lane = lax.broadcasted_iota(jnp.int32, (width // 2, width), 1)
    column = lax.broadcasted_iota(jnp.int32, (width // 2, width), 0)
    pick = (lane == 2 * column).astype(jnp.bfloat16)
    sec = []
    for h in range(rows):
        own = above_ref[t, 1] if h == 0 else xp_ref[t, h - 1]
        v = s[:, h * width : (h + 1) * width] + own.astype(jnp.float32)
        v = jnp.maximum(v, 0.0)
        if h == 0:
            v = v * keep_ref[0].astype(jnp.float32)
        sec.append(v.astype(jnp.bfloat16).astype(jnp.float32))
    shifted = [[_lane_shift(r, b - 1).astype(jnp.bfloat16) for b in range(3)] for r in sec]
    parts = []
    for a in range(3):
        for b in range(3):
            parts.append(jnp.concatenate([shifted[2 * i + a][b] for i in range(reduced_rows)], axis=1))
    stacked = jnp.concatenate(parts, axis=0)
    full = jnp.dot(wd_ref[...], stacked, preferred_element_type=jnp.float32)
    full = jnp.maximum(full, 0.0).astype(jnp.bfloat16)
    outs = full.shape[0]
    rows_by_d = jnp.concatenate([full[:, i * width : (i + 1) * width] for i in range(reduced_rows)], axis=0)
    r = lax.dot_general(pick, rows_by_d, (((1,), (1,)), ((), ())), preferred_element_type=jnp.float32)
    for i in range(reduced_rows):
        out_ref[slot, i] = r[:, i * outs : (i + 1) * outs].astype(out_ref.dtype)


def _edges_one_kernel(above_ref, xp_ref, below_ref, w9_ref, edge_ref):
    refs = (above_ref, xp_ref, below_ref)
    frames = xp_ref.shape[0]
    span = edge_ref.shape[-1]
    m = _middle_one(refs, [0, frames - 1], w9_ref)
    edge_ref[0] = m[:, :span]
    edge_ref[1] = m[:, span:]


def _inner_one_kernel(keep_ref, above_ref, xp_ref, below_ref, w9_ref, t3_ref, wd_ref, out_ref, side_ref, mid_ref):
    refs = (above_ref, xp_ref, below_ref)
    frames = xp_ref.shape[0]

    span = mid_ref.shape[-1]
    group = 4 if frames % 4 == 0 else 2

    def middle(g, carry):
        m = _middle_one(refs, [group * g + k for k in range(group)], w9_ref)
        for k in range(group):
            mid_ref[group * g + k] = m[:, k * span : (k + 1) * span]
        return carry

    lax.fori_loop(0, frames // group, middle, 0)
    side_ref[0] = mid_ref[1]
    side_ref[1] = mid_ref[frames - 2]

    channels = t3_ref.shape[0] // 2

    def section(g, carry):
        t = 2 * g + 1
        stacked = jnp.concatenate([mid_ref[t - 1], mid_ref[t], mid_ref[t + 1], mid_ref[t + 2]], axis=0)
        s = jnp.dot(t3_ref[...], stacked, preferred_element_type=jnp.float32)
        _down(s[:channels], refs, t, wd_ref, keep_ref, out_ref, t - 1)
        _down(s[channels:], refs, t + 1, wd_ref, keep_ref, out_ref, t)
        return carry

    lax.fori_loop(0, (frames - 2) // 2, section, 0)


def _outer_one_kernel(
    keep_ref, above_ref, xp_ref, below_ref, t3_ref, wd_ref, before_ref, after_ref, edge_ref, side_ref, out_ref
):
    refs = (above_ref, xp_ref, below_ref)
    frames = xp_ref.shape[0]
    stacked = jnp.concatenate([before_ref[0], edge_ref[0], side_ref[0]], axis=0)
    _section_down(stacked, refs, 0, t3_ref, wd_ref, keep_ref, out_ref, 0)
    stacked = jnp.concatenate([side_ref[1], edge_ref[1], after_ref[0]], axis=0)
    _section_down(stacked, refs, frames - 1, t3_ref, wd_ref, keep_ref, out_ref, 1)


def block_one(above, rowed, below, keep_first, spatial_kernel, temporal_kernel, down_kernel):
    frames, rows, channels, width = rowed.shape
    rows = rows + 1
    mids = spatial_kernel.shape[2]
    outs = down_kernel.shape[2]
    w9 = jnp.transpose(spatial_kernel, (2, 0, 1, 3)).reshape(mids, 9 * channels)
    t3 = jnp.transpose(temporal_kernel, (1, 0, 2)).reshape(channels, 3 * mids)
    wd = jnp.transpose(down_kernel, (2, 0, 1, 3)).reshape(outs, 9 * channels)
    gap = jnp.zeros((channels, mids), t3.dtype)
    t4 = jnp.concatenate(
        [jnp.concatenate([t3, gap], axis=1), jnp.concatenate([gap, t3], axis=1)], axis=0
    )
    vmem = pltpu.MemorySpace.VMEM if hasattr(pltpu, "MemorySpace") else pltpu.VMEM
    smem = pltpu.MemorySpace.SMEM if hasattr(pltpu, "MemorySpace") else pltpu.SMEM
    params = pltpu.CompilerParams(vmem_limit_bytes=48 * 1024 * 1024)
    spec = pl.BlockSpec(memory_space=vmem)
    sspec = pl.BlockSpec(memory_space=smem)
    reduced_rows = (rows - 1) // 2
    plane = (mids, rows * width)
    out_plane = (reduced_rows, width // 2, outs)
    spatial_flops = 2 * rows * width * 9 * channels * mids
    section_flops = 2 * rows * width * 3 * mids * channels + 2 * reduced_rows * width * 9 * channels * outs
    edges = pl.pallas_call(
        _edges_one_kernel,
        out_shape=jax.ShapeDtypeStruct((2,) + plane, rowed.dtype),
        in_specs=[spec] * 4,
        out_specs=spec,
        compiler_params=params,
        cost_estimate=pl.CostEstimate(flops=2 * spatial_flops, bytes_accessed=2 * rowed.size, transcendentals=0),
    )(above, rowed, below, w9)
    before = from_behind(edges[1:], "tm", 1)
    after = from_behind(edges[:1], "tm", -1)
    inner, side = pl.pallas_call(
        _inner_one_kernel,
        out_shape=(
            jax.ShapeDtypeStruct((frames - 2,) + out_plane, rowed.dtype),
            jax.ShapeDtypeStruct((2,) + plane, rowed.dtype),
        ),
        in_specs=[sspec] + [spec] * 6,
        out_specs=(spec, spec),
        scratch_shapes=[pltpu.VMEM((frames,) + plane, jnp.bfloat16)],
        compiler_params=params,
        cost_estimate=pl.CostEstimate(
            flops=frames * (spatial_flops + section_flops), bytes_accessed=4 * rowed.size, transcendentals=0
        ),
    )(keep_first, above, rowed, below, w9, t4, wd)
    outer = pl.pallas_call(
        _outer_one_kernel,
        out_shape=jax.ShapeDtypeStruct((2,) + out_plane, rowed.dtype),
        in_specs=[sspec] + [spec] * 9,
        out_specs=spec,
        compiler_params=params,
    )(keep_first, above, rowed, below, t3, wd, before, after, edges, side)
    return jnp.concatenate([outer[:1], inner, outer[1:]], axis=0)


def _sublane_shift(x, by, axis):
    size = x.shape[axis]
    rolled = pltpu.roll(x, (-by) % size, axis)
    index = lax.broadcasted_iota(jnp.int32, x.shape, axis)
    inside = jnp.logical_and(index + by >= 0, index + by < size)
    return jnp.where(inside, rolled, jnp.zeros_like(rolled))


def _slab_two(above_ref, xp_ref, below_ref, f):
    return jnp.concatenate([above_ref[f], xp_ref[f], below_ref[f]], axis=0).astype(jnp.float32)


def _middle_two(slabs, w9_ref):
    rows = slabs[0].shape[0] - 2
    pieces = []
    for slab in slabs:
        shifted = [_sublane_shift(slab, b - 1, 1).astype(jnp.bfloat16) for b in range(3)]
        for i in range(rows):
            pieces.append(jnp.concatenate([shifted[b][i + a] for a in range(3) for b in range(3)], axis=1))
    stacked = jnp.concatenate(pieces, axis=0)
    m = jnp.dot(stacked, w9_ref[...], preferred_element_type=jnp.float32)
    return jnp.maximum(m, 0.0).astype(jnp.bfloat16)


def _edges_two_kernel(above_ref, xp_ref, below_ref, w9_ref, edge_ref):
    frames = xp_ref.shape[0]
    plane = edge_ref.shape[1]
    m = _middle_two(
        [_slab_two(above_ref, xp_ref, below_ref, 0), _slab_two(above_ref, xp_ref, below_ref, frames - 1)], w9_ref
    )
    edge_ref[0] = m[:plane]
    edge_ref[1] = m[plane:]


def _finish(s, xp_ref, t, out_ref, slot):
    rows, width = xp_ref.shape[1], xp_ref.shape[2]
    for i in range(rows):
        v = s[i * width : (i + 1) * width] + xp_ref[t, i].astype(jnp.float32)
        out_ref[slot, i] = jnp.maximum(v, 0.0).astype(out_ref.dtype)


def _inner_two_kernel(above_ref, xp_ref, below_ref, w9_ref, t3_ref, out_ref, side_ref, mid_ref):
    frames = xp_ref.shape[0]
    plane = mid_ref.shape[1]

    group = 8 if frames % 8 == 0 else 2

    def middle(g, carry):
        f = group * g
        m = _middle_two([_slab_two(above_ref, xp_ref, below_ref, f + k) for k in range(group)], w9_ref)
        for k in range(group):
            mid_ref[f + k] = m[k * plane : (k + 1) * plane]
        return carry

    lax.fori_loop(0, frames // group, middle, 0)
    side_ref[0] = mid_ref[1]
    side_ref[1] = mid_ref[frames - 2]

    def run(t, count):
        s = None
        for k in range(3):
            rows = jnp.concatenate([mid_ref[t - 1 + k + j] for j in range(count)], axis=0)
            d = jnp.dot(rows, t3_ref[k], preferred_element_type=jnp.float32)
            s = d if s is None else s + d
        for j in range(count):
            _finish(s[j * plane : (j + 1) * plane], xp_ref, t + j, out_ref, t + j - 1)

    def section(g, carry):
        run(4 * g + 1, 4)
        return carry

    lax.fori_loop(0, (frames - 2) // 4, section, 0)
    left = (frames - 2) % 4
    if left:
        run(frames - 1 - left, left)


def _outer_two_kernel(xp_ref, t3_ref, before_ref, after_ref, edge_ref, side_ref, out_ref):
    frames = xp_ref.shape[0]
    s = jnp.dot(before_ref[0], t3_ref[0], preferred_element_type=jnp.float32)
    s = s + jnp.dot(edge_ref[0], t3_ref[1], preferred_element_type=jnp.float32)
    s = s + jnp.dot(side_ref[0], t3_ref[2], preferred_element_type=jnp.float32)
    _finish(s, xp_ref, 0, out_ref, 0)
    s = jnp.dot(side_ref[1], t3_ref[0], preferred_element_type=jnp.float32)
    s = s + jnp.dot(edge_ref[1], t3_ref[1], preferred_element_type=jnp.float32)
    s = s + jnp.dot(after_ref[0], t3_ref[2], preferred_element_type=jnp.float32)
    _finish(s, xp_ref, frames - 1, out_ref, 1)


def block_two(above, rowed, below, spatial_kernel, temporal_kernel):
    frames, rows, width, channels = rowed.shape
    mids = spatial_kernel.shape[2]
    w9 = jnp.transpose(spatial_kernel, (0, 1, 3, 2)).reshape(9 * channels, mids)
    t3 = jnp.transpose(temporal_kernel, (0, 2, 1))
    vmem = pltpu.MemorySpace.VMEM if hasattr(pltpu, "MemorySpace") else pltpu.VMEM
    params = pltpu.CompilerParams(vmem_limit_bytes=48 * 1024 * 1024)
    spec = pl.BlockSpec(memory_space=vmem)
    plane = (rows * width, mids)
    edges = pl.pallas_call(
        _edges_two_kernel,
        out_shape=jax.ShapeDtypeStruct((2,) + plane, rowed.dtype),
        in_specs=[spec] * 4,
        out_specs=spec,
        compiler_params=params,
        cost_estimate=pl.CostEstimate(
            flops=2 * 2 * rows * width * 9 * channels * mids, bytes_accessed=2 * rowed.size, transcendentals=0
        ),
    )(above, rowed, below, w9)
    before = from_behind(edges[1:], "tm", 1)
    after = from_behind(edges[:1], "tm", -1)
    inner, side = pl.pallas_call(
        _inner_two_kernel,
        out_shape=(
            jax.ShapeDtypeStruct((frames - 2, rows, width, channels), rowed.dtype),
            jax.ShapeDtypeStruct((2,) + plane, rowed.dtype),
        ),
        in_specs=[spec] * 5,
        out_specs=(spec, spec),
        scratch_shapes=[pltpu.VMEM((frames,) + plane, jnp.bfloat16)],
        compiler_params=params,
        cost_estimate=pl.CostEstimate(
            flops=2 * frames * rows * width * (9 * channels * mids + 3 * mids * channels),
            bytes_accessed=4 * rowed.size,
            transcendentals=0,
        ),
    )(above, rowed, below, w9, t3)
    outer = pl.pallas_call(
        _outer_two_kernel,
        out_shape=jax.ShapeDtypeStruct((2, rows, width, channels), rowed.dtype),
        in_specs=[spec] * 6,
        out_specs=spec,
        compiler_params=params,
    )(rowed, t3, before, after, edges, side)
    return jnp.concatenate([outer[:1], inner, outer[1:]], axis=0)


def _copy_kernel(top_ref, bottom_ref, top_out, bottom_out):
    top_out[...] = top_ref[...]
    bottom_out[...] = bottom_ref[...]


def edge_rows(block, top, bottom):
    frames, rows, channels, width = block.shape
    top_spec = pl.BlockSpec((frames, top, channels, width), lambda i: (0, rows // top - 1, 0, 0))
    bottom_spec = pl.BlockSpec((frames, bottom, channels, width), lambda i: (0, 0, 0, 0))
    return pl.pallas_call(
        _copy_kernel,
        grid=(1,),
        out_shape=(
            jax.ShapeDtypeStruct((frames, top, channels, width), block.dtype),
            jax.ShapeDtypeStruct((frames, bottom, channels, width), block.dtype),
        ),
        in_specs=[top_spec, bottom_spec],
        out_specs=(pl.BlockSpec((frames, top, channels, width), lambda i: (0, 0, 0, 0)), bottom_spec),
    )(block, block)


def on_device(video_clip, spatial_one, temporal_one, down_weight, spatial_two, temporal_two):
    rows = video_clip.shape[1]
    top, bottom = edge_rows(video_clip, 2, 1)
    above = from_behind(top, "row", 1)
    below = from_behind(bottom, "row", -1)
    keep_first = (lax.axis_index("row") > 0).astype(jnp.int32).reshape(1)
    reduced = block_one(above, video_clip, below, keep_first, spatial_one, temporal_one, down_weight)
    rows = reduced.shape[1]
    above = from_behind(reduced[:, rows - 1 :], "row", 1)
    below = from_behind(reduced[:, :1], "row", -1)
    return block_two(above, reduced, below, spatial_two, temporal_two)


def solution(mesh):
    placed = (P("tm", "row", None, None), P(), P(), P(), P(), P())
    return jax.shard_map(
        on_device, mesh=mesh, in_specs=placed, out_specs=P("tm", "row", None, None), check_vma=False
    )
```

```python
import functools

import jax
import jax.numpy as jnp
from jax import lax
from jax.experimental import pallas as pl
from jax.experimental.pallas import tpu as pltpu
from jax.sharding import PartitionSpec as P


def padded_2(block, sides, width):
    for axis, dim in sides:
        count = lax.axis_size(axis)
        forward = [(i, i + 1) for i in range(count - 1)]
        backward = [(target, source) for source, target in forward]
        low = lax.ppermute(
            lax.slice_in_dim(block, block.shape[dim] - width, None, axis=dim), axis, forward
        )
        high = lax.ppermute(lax.slice_in_dim(block, 0, width, axis=dim), axis, backward)
        block = jnp.concatenate([low, block, high], axis=dim)
    return block


def from_behind(array, axis, by):
    devices = lax.axis_size(axis)
    pairs = [(i, i + by) for i in range(devices) if 0 <= i + by < devices]
    return lax.ppermute(array, axis, pairs)


def spatial(source, kernel, layout):
    return lax.conv_general_dilated(
        source,
        kernel,
        (1, 1),
        ((0, 0), (1, 1)),
        dimension_numbers=(layout, "HWOI", layout),
        preferred_element_type=jnp.float32,
    )


def temporal(source, kernel, layout):
    return lax.conv_general_dilated(
        source,
        kernel[:, None],
        (1, 1),
        ((0, 0), (0, 0)),
        dimension_numbers=(layout, "HWOI", layout),
        preferred_element_type=jnp.float32,
    )


def residual_block(source, spatial_kernel, temporal_kernel, space_layout, time_layout):
    padded = padded_2(source, (("tm", 0), ("row", 1)), 1)
    framed = jax.nn.relu(spatial(padded, spatial_kernel, space_layout)).astype(jnp.bfloat16)
    summed = source.astype(jnp.float32) + temporal(framed, temporal_kernel, time_layout)
    return jax.nn.relu(summed).astype(jnp.bfloat16)


def _lane_shift(x, by):
    width = x.shape[-1]
    rolled = pltpu.roll(x, (-by) % width, x.ndim - 1)
    lane = lax.broadcasted_iota(jnp.int32, x.shape, x.ndim - 1)
    inside = jnp.logical_and(lane + by >= 0, lane + by < width)
    return jnp.where(inside, rolled, jnp.zeros_like(rolled))


def _middle_one(refs, fs, w9_ref):
    above_ref, xp_ref, below_ref = refs
    rows = xp_ref.shape[1] + 1
    columns = []
    for f in fs:
        slab = jnp.concatenate([above_ref[f], xp_ref[f], below_ref[f]], axis=0).astype(jnp.float32)
        shifted = [_lane_shift(slab, b - 1).astype(jnp.bfloat16) for b in range(3)]
        parts = []
        for a in range(3):
            for b in range(3):
                parts.append(jnp.concatenate([shifted[b][h + a] for h in range(rows)], axis=1))
        columns.append(jnp.concatenate(parts, axis=0))
    stacked = columns[0] if len(columns) == 1 else jnp.concatenate(columns, axis=1)
    m = jnp.dot(w9_ref[...], stacked, preferred_element_type=jnp.float32)
    return jnp.maximum(m, 0.0).astype(jnp.bfloat16)


def _section_down(stacked, refs, t, t3_ref, wd_ref, keep_ref, out_ref, slot):
    s = jnp.dot(t3_ref[...], stacked, preferred_element_type=jnp.float32)
    _down(s, refs, t, wd_ref, keep_ref, out_ref, slot)


def _down(s, refs, t, wd_ref, keep_ref, out_ref, slot):
    above_ref, xp_ref, _ = refs
    rows = xp_ref.shape[1] + 1
    width = xp_ref.shape[-1]
    reduced_rows = (rows - 1) // 2
    lane = lax.broadcasted_iota(jnp.int32, (width // 2, width), 1)
    column = lax.broadcasted_iota(jnp.int32, (width // 2, width), 0)
    pick = (lane == 2 * column).astype(jnp.bfloat16)
    sec = []
    for h in range(rows):
        own = above_ref[t, 1] if h == 0 else xp_ref[t, h - 1]
        v = s[:, h * width : (h + 1) * width] + own.astype(jnp.float32)
        v = jnp.maximum(v, 0.0)
        if h == 0:
            v = v * keep_ref[0].astype(jnp.float32)
        sec.append(v.astype(jnp.bfloat16).astype(jnp.float32))
    shifted = [[_lane_shift(r, b - 1).astype(jnp.bfloat16) for b in range(3)] for r in sec]
    parts = []
    for a in range(3):
        for b in range(3):
            parts.append(jnp.concatenate([shifted[2 * i + a][b] for i in range(reduced_rows)], axis=1))
    stacked = jnp.concatenate(parts, axis=0)
    full = jnp.dot(wd_ref[...], stacked, preferred_element_type=jnp.float32)
    full = jnp.maximum(full, 0.0).astype(jnp.bfloat16)
    outs = full.shape[0]
    rows_by_d = jnp.concatenate([full[:, i * width : (i + 1) * width] for i in range(reduced_rows)], axis=0)
    r = lax.dot_general(pick, rows_by_d, (((1,), (1,)), ((), ())), preferred_element_type=jnp.float32)
    for i in range(reduced_rows):
        out_ref[slot, i] = r[:, i * outs : (i + 1) * outs].astype(out_ref.dtype)


def _edges_one_kernel(above_ref, xp_ref, below_ref, w9_ref, edge_ref):
    refs = (above_ref, xp_ref, below_ref)
    frames = xp_ref.shape[0]
    span = edge_ref.shape[-1]
    m = _middle_one(refs, [0, frames - 1], w9_ref)
    edge_ref[0] = m[:, :span]
    edge_ref[1] = m[:, span:]


def _inner_one_kernel(keep_ref, above_ref, xp_ref, below_ref, w9_ref, t3_ref, wd_ref, out_ref, side_ref, mid_ref):
    refs = (above_ref, xp_ref, below_ref)
    frames = xp_ref.shape[0]

    span = mid_ref.shape[-1]
    group = 4 if frames % 4 == 0 else 2

    def middle(g, carry):
        m = _middle_one(refs, [group * g + k for k in range(group)], w9_ref)
        for k in range(group):
            mid_ref[group * g + k] = m[:, k * span : (k + 1) * span]
        return carry

    lax.fori_loop(0, frames // group, middle, 0)
    side_ref[0] = mid_ref[1]
    side_ref[1] = mid_ref[frames - 2]

    channels = t3_ref.shape[0] // 2

    span = mid_ref.shape[-1]

    def run(t, pairs):
        stacks = [
            jnp.concatenate([mid_ref[u - 1], mid_ref[u], mid_ref[u + 1], mid_ref[u + 2]], axis=0)
            for u in [t + 2 * p for p in range(pairs)]
        ]
        stacked = stacks[0] if pairs == 1 else jnp.concatenate(stacks, axis=1)
        s = jnp.dot(t3_ref[...], stacked, preferred_element_type=jnp.float32)
        for p in range(pairs):
            u = t + 2 * p
            part = s[:, p * span : (p + 1) * span]
            _down(part[:channels], refs, u, wd_ref, keep_ref, out_ref, u - 1)
            _down(part[channels:], refs, u + 1, wd_ref, keep_ref, out_ref, u)

    def section(g, carry):
        run(4 * g + 1, 2)
        return carry

    lax.fori_loop(0, (frames - 2) // 4, section, 0)
    if (frames - 2) % 4:
        run(frames - 3, 1)


def _outer_one_kernel(
    keep_ref, above_ref, xp_ref, below_ref, t3_ref, wd_ref, before_ref, after_ref, edge_ref, side_ref, out_ref
):
    refs = (above_ref, xp_ref, below_ref)
    frames = xp_ref.shape[0]
    stacked = jnp.concatenate([before_ref[0], edge_ref[0], side_ref[0]], axis=0)
    _section_down(stacked, refs, 0, t3_ref, wd_ref, keep_ref, out_ref, 0)
    stacked = jnp.concatenate([side_ref[1], edge_ref[1], after_ref[0]], axis=0)
    _section_down(stacked, refs, frames - 1, t3_ref, wd_ref, keep_ref, out_ref, 1)


def block_one(above, rowed, below, keep_first, spatial_kernel, temporal_kernel, down_kernel):
    frames, rows, channels, width = rowed.shape
    rows = rows + 1
    mids = spatial_kernel.shape[2]
    outs = down_kernel.shape[2]
    w9 = jnp.transpose(spatial_kernel, (2, 0, 1, 3)).reshape(mids, 9 * channels)
    t3 = jnp.transpose(temporal_kernel, (1, 0, 2)).reshape(channels, 3 * mids)
    wd = jnp.transpose(down_kernel, (2, 0, 1, 3)).reshape(outs, 9 * channels)
    gap = jnp.zeros((channels, mids), t3.dtype)
    t4 = jnp.concatenate(
        [jnp.concatenate([t3, gap], axis=1), jnp.concatenate([gap, t3], axis=1)], axis=0
    )
    vmem = pltpu.MemorySpace.VMEM if hasattr(pltpu, "MemorySpace") else pltpu.VMEM
    smem = pltpu.MemorySpace.SMEM if hasattr(pltpu, "MemorySpace") else pltpu.SMEM
    params = pltpu.CompilerParams(vmem_limit_bytes=48 * 1024 * 1024)
    spec = pl.BlockSpec(memory_space=vmem)
    sspec = pl.BlockSpec(memory_space=smem)
    reduced_rows = (rows - 1) // 2
    plane = (mids, rows * width)
    out_plane = (reduced_rows, width // 2, outs)
    spatial_flops = 2 * rows * width * 9 * channels * mids
    section_flops = 2 * rows * width * 3 * mids * channels + 2 * reduced_rows * width * 9 * channels * outs
    edges = pl.pallas_call(
        _edges_one_kernel,
        out_shape=jax.ShapeDtypeStruct((2,) + plane, rowed.dtype),
        in_specs=[spec] * 4,
        out_specs=spec,
        compiler_params=params,
        cost_estimate=pl.CostEstimate(flops=2 * spatial_flops, bytes_accessed=2 * rowed.size, transcendentals=0),
    )(above, rowed, below, w9)
    before = from_behind(edges[1:], "tm", 1)
    after = from_behind(edges[:1], "tm", -1)
    inner, side = pl.pallas_call(
        _inner_one_kernel,
        out_shape=(
            jax.ShapeDtypeStruct((frames - 2,) + out_plane, rowed.dtype),
            jax.ShapeDtypeStruct((2,) + plane, rowed.dtype),
        ),
        in_specs=[sspec] + [spec] * 6,
        out_specs=(spec, spec),
        scratch_shapes=[pltpu.VMEM((frames,) + plane, jnp.bfloat16)],
        compiler_params=params,
        cost_estimate=pl.CostEstimate(
            flops=frames * (spatial_flops + section_flops), bytes_accessed=4 * rowed.size, transcendentals=0
        ),
    )(keep_first, above, rowed, below, w9, t4, wd)
    outer = pl.pallas_call(
        _outer_one_kernel,
        out_shape=jax.ShapeDtypeStruct((2,) + out_plane, rowed.dtype),
        in_specs=[sspec] + [spec] * 9,
        out_specs=spec,
        compiler_params=params,
    )(keep_first, above, rowed, below, t3, wd, before, after, edges, side)
    return jnp.concatenate([outer[:1], inner, outer[1:]], axis=0)


def _sublane_shift(x, by, axis):
    size = x.shape[axis]
    rolled = pltpu.roll(x, (-by) % size, axis)
    index = lax.broadcasted_iota(jnp.int32, x.shape, axis)
    inside = jnp.logical_and(index + by >= 0, index + by < size)
    return jnp.where(inside, rolled, jnp.zeros_like(rolled))


def _slab_two(above_ref, xp_ref, below_ref, f):
    return jnp.concatenate([above_ref[f], xp_ref[f], below_ref[f]], axis=0).astype(jnp.float32)


def _middle_two(slabs, w9_ref):
    rows = slabs[0].shape[0] - 2
    pieces = []
    for slab in slabs:
        shifted = [_sublane_shift(slab, b - 1, 1).astype(jnp.bfloat16) for b in range(3)]
        for i in range(rows):
            pieces.append(jnp.concatenate([shifted[b][i + a] for a in range(3) for b in range(3)], axis=1))
    stacked = jnp.concatenate(pieces, axis=0)
    m = jnp.dot(stacked, w9_ref[...], preferred_element_type=jnp.float32)
    return jnp.maximum(m, 0.0).astype(jnp.bfloat16)


def _edges_two_kernel(above_ref, xp_ref, below_ref, w9_ref, edge_ref):
    frames = xp_ref.shape[0]
    plane = edge_ref.shape[1]
    m = _middle_two(
        [_slab_two(above_ref, xp_ref, below_ref, 0), _slab_two(above_ref, xp_ref, below_ref, frames - 1)], w9_ref
    )
    edge_ref[0] = m[:plane]
    edge_ref[1] = m[plane:]


def _finish(s, xp_ref, t, out_ref, slot):
    rows, width = xp_ref.shape[1], xp_ref.shape[2]
    for i in range(rows):
        v = s[i * width : (i + 1) * width] + xp_ref[t, i].astype(jnp.float32)
        out_ref[slot, i] = jnp.maximum(v, 0.0).astype(out_ref.dtype)


def _inner_two_kernel(above_ref, xp_ref, below_ref, w9_ref, t3_ref, out_ref, side_ref, mid_ref):
    frames = xp_ref.shape[0]
    plane = mid_ref.shape[1]

    group = 8 if frames % 8 == 0 else 2

    def middle(g, carry):
        f = group * g
        m = _middle_two([_slab_two(above_ref, xp_ref, below_ref, f + k) for k in range(group)], w9_ref)
        for k in range(group):
            mid_ref[f + k] = m[k * plane : (k + 1) * plane]
        return carry

    lax.fori_loop(0, frames // group, middle, 0)
    side_ref[0] = mid_ref[1]
    side_ref[1] = mid_ref[frames - 2]

    def run(t, count):
        s = None
        for k in range(3):
            rows = jnp.concatenate([mid_ref[t - 1 + k + j] for j in range(count)], axis=0)
            d = jnp.dot(rows, t3_ref[k], preferred_element_type=jnp.float32)
            s = d if s is None else s + d
        for j in range(count):
            _finish(s[j * plane : (j + 1) * plane], xp_ref, t + j, out_ref, t + j - 1)

    def section(g, carry):
        run(4 * g + 1, 4)
        return carry

    lax.fori_loop(0, (frames - 2) // 4, section, 0)
    left = (frames - 2) % 4
    if left:
        run(frames - 1 - left, left)


def _outer_two_kernel(xp_ref, t3_ref, before_ref, after_ref, edge_ref, side_ref, out_ref):
    frames = xp_ref.shape[0]
    s = jnp.dot(before_ref[0], t3_ref[0], preferred_element_type=jnp.float32)
    s = s + jnp.dot(edge_ref[0], t3_ref[1], preferred_element_type=jnp.float32)
    s = s + jnp.dot(side_ref[0], t3_ref[2], preferred_element_type=jnp.float32)
    _finish(s, xp_ref, 0, out_ref, 0)
    s = jnp.dot(side_ref[1], t3_ref[0], preferred_element_type=jnp.float32)
    s = s + jnp.dot(edge_ref[1], t3_ref[1], preferred_element_type=jnp.float32)
    s = s + jnp.dot(after_ref[0], t3_ref[2], preferred_element_type=jnp.float32)
    _finish(s, xp_ref, frames - 1, out_ref, 1)


def block_two(above, rowed, below, spatial_kernel, temporal_kernel):
    frames, rows, width, channels = rowed.shape
    mids = spatial_kernel.shape[2]
    w9 = jnp.transpose(spatial_kernel, (0, 1, 3, 2)).reshape(9 * channels, mids)
    t3 = jnp.transpose(temporal_kernel, (0, 2, 1))
    vmem = pltpu.MemorySpace.VMEM if hasattr(pltpu, "MemorySpace") else pltpu.VMEM
    params = pltpu.CompilerParams(vmem_limit_bytes=48 * 1024 * 1024)
    spec = pl.BlockSpec(memory_space=vmem)
    plane = (rows * width, mids)
    edges = pl.pallas_call(
        _edges_two_kernel,
        out_shape=jax.ShapeDtypeStruct((2,) + plane, rowed.dtype),
        in_specs=[spec] * 4,
        out_specs=spec,
        compiler_params=params,
        cost_estimate=pl.CostEstimate(
            flops=2 * 2 * rows * width * 9 * channels * mids, bytes_accessed=2 * rowed.size, transcendentals=0
        ),
    )(above, rowed, below, w9)
    before = from_behind(edges[1:], "tm", 1)
    after = from_behind(edges[:1], "tm", -1)
    inner, side = pl.pallas_call(
        _inner_two_kernel,
        out_shape=(
            jax.ShapeDtypeStruct((frames - 2, rows, width, channels), rowed.dtype),
            jax.ShapeDtypeStruct((2,) + plane, rowed.dtype),
        ),
        in_specs=[spec] * 5,
        out_specs=(spec, spec),
        scratch_shapes=[pltpu.VMEM((frames,) + plane, jnp.bfloat16)],
        compiler_params=params,
        cost_estimate=pl.CostEstimate(
            flops=2 * frames * rows * width * (9 * channels * mids + 3 * mids * channels),
            bytes_accessed=4 * rowed.size,
            transcendentals=0,
        ),
    )(above, rowed, below, w9, t3)
    outer = pl.pallas_call(
        _outer_two_kernel,
        out_shape=jax.ShapeDtypeStruct((2, rows, width, channels), rowed.dtype),
        in_specs=[spec] * 6,
        out_specs=spec,
        compiler_params=params,
    )(rowed, t3, before, after, edges, side)
    return jnp.concatenate([outer[:1], inner, outer[1:]], axis=0)


def _copy_kernel(top_ref, bottom_ref, top_out, bottom_out):
    top_out[...] = top_ref[...]
    bottom_out[...] = bottom_ref[...]


def edge_rows(block, top, bottom):
    frames, rows, channels, width = block.shape
    top_spec = pl.BlockSpec((frames, top, channels, width), lambda i: (0, rows // top - 1, 0, 0))
    bottom_spec = pl.BlockSpec((frames, bottom, channels, width), lambda i: (0, 0, 0, 0))
    return pl.pallas_call(
        _copy_kernel,
        grid=(1,),
        out_shape=(
            jax.ShapeDtypeStruct((frames, top, channels, width), block.dtype),
            jax.ShapeDtypeStruct((frames, bottom, channels, width), block.dtype),
        ),
        in_specs=[top_spec, bottom_spec],
        out_specs=(pl.BlockSpec((frames, top, channels, width), lambda i: (0, 0, 0, 0)), bottom_spec),
    )(block, block)


def on_device(video_clip, spatial_one, temporal_one, down_weight, spatial_two, temporal_two):
    rows = video_clip.shape[1]
    top, bottom = edge_rows(video_clip, 2, 1)
    above = from_behind(top, "row", 1)
    below = from_behind(bottom, "row", -1)
    keep_first = (lax.axis_index("row") > 0).astype(jnp.int32).reshape(1)
    reduced = block_one(above, video_clip, below, keep_first, spatial_one, temporal_one, down_weight)
    rows = reduced.shape[1]
    above = from_behind(reduced[:, rows - 1 :], "row", 1)
    below = from_behind(reduced[:, :1], "row", -1)
    return block_two(above, reduced, below, spatial_two, temporal_two)


def solution(mesh):
    placed = (P("tm", "row", None, None), P(), P(), P(), P(), P())
    return jax.shard_map(
        on_device, mesh=mesh, in_specs=placed, out_specs=P("tm", "row", None, None), check_vma=False
    )
```

```python
import functools

import jax
import jax.numpy as jnp
from jax import lax
from jax.experimental import pallas as pl
from jax.experimental.pallas import tpu as pltpu
from jax.sharding import PartitionSpec as P


def padded_2(block, sides, width):
    for axis, dim in sides:
        count = lax.axis_size(axis)
        forward = [(i, i + 1) for i in range(count - 1)]
        backward = [(target, source) for source, target in forward]
        low = lax.ppermute(
            lax.slice_in_dim(block, block.shape[dim] - width, None, axis=dim), axis, forward
        )
        high = lax.ppermute(lax.slice_in_dim(block, 0, width, axis=dim), axis, backward)
        block = jnp.concatenate([low, block, high], axis=dim)
    return block


def from_behind(array, axis, by):
    devices = lax.axis_size(axis)
    pairs = [(i, i + by) for i in range(devices) if 0 <= i + by < devices]
    return lax.ppermute(array, axis, pairs)


def spatial(source, kernel, layout):
    return lax.conv_general_dilated(
        source,
        kernel,
        (1, 1),
        ((0, 0), (1, 1)),
        dimension_numbers=(layout, "HWOI", layout),
        preferred_element_type=jnp.float32,
    )


def temporal(source, kernel, layout):
    return lax.conv_general_dilated(
        source,
        kernel[:, None],
        (1, 1),
        ((0, 0), (0, 0)),
        dimension_numbers=(layout, "HWOI", layout),
        preferred_element_type=jnp.float32,
    )


def residual_block(source, spatial_kernel, temporal_kernel, space_layout, time_layout):
    padded = padded_2(source, (("tm", 0), ("row", 1)), 1)
    framed = jax.nn.relu(spatial(padded, spatial_kernel, space_layout)).astype(jnp.bfloat16)
    summed = source.astype(jnp.float32) + temporal(framed, temporal_kernel, time_layout)
    return jax.nn.relu(summed).astype(jnp.bfloat16)


def _lane_shift(x, by):
    width = x.shape[-1]
    rolled = pltpu.roll(x, (-by) % width, x.ndim - 1)
    lane = lax.broadcasted_iota(jnp.int32, x.shape, x.ndim - 1)
    inside = jnp.logical_and(lane + by >= 0, lane + by < width)
    return jnp.where(inside, rolled, jnp.zeros_like(rolled))


def _middle_one(refs, fs, w9_ref):
    above_ref, xp_ref, below_ref = refs
    rows = xp_ref.shape[1] + 1
    columns = []
    for f in fs:
        slab = jnp.concatenate([above_ref[f], xp_ref[f], below_ref[f]], axis=0).astype(jnp.float32)
        shifted = [_lane_shift(slab, b - 1).astype(jnp.bfloat16) for b in range(3)]
        parts = []
        for a in range(3):
            for b in range(3):
                parts.append(jnp.concatenate([shifted[b][h + a] for h in range(rows)], axis=1))
        columns.append(jnp.concatenate(parts, axis=0))
    stacked = columns[0] if len(columns) == 1 else jnp.concatenate(columns, axis=1)
    m = jnp.dot(w9_ref[...], stacked, preferred_element_type=jnp.float32)
    return jnp.maximum(m, 0.0).astype(jnp.bfloat16)


def _section_down(stacked, refs, t, t3_ref, wd_ref, keep_ref, out_ref, slot):
    s = jnp.dot(t3_ref[...], stacked, preferred_element_type=jnp.float32)
    _down(s, refs, t, wd_ref, keep_ref, out_ref, slot)


def _down(s, refs, t, wd_ref, keep_ref, out_ref, slot):
    _down_many([s], refs, [t], wd_ref, keep_ref, out_ref, [slot])


def _down_many(sums, refs, ts, wd_ref, keep_ref, out_ref, slots):
    above_ref, xp_ref, _ = refs
    rows = xp_ref.shape[1] + 1
    width = xp_ref.shape[-1]
    reduced_rows = (rows - 1) // 2
    lane = lax.broadcasted_iota(jnp.int32, (width // 2, width), 1)
    column = lax.broadcasted_iota(jnp.int32, (width // 2, width), 0)
    pick = (lane == 2 * column).astype(jnp.bfloat16)
    columns = []
    for s, t in zip(sums, ts):
        sec = []
        for h in range(rows):
            own = above_ref[t, 1] if h == 0 else xp_ref[t, h - 1]
            v = s[:, h * width : (h + 1) * width] + own.astype(jnp.float32)
            v = jnp.maximum(v, 0.0)
            if h == 0:
                v = v * keep_ref[0].astype(jnp.float32)
            sec.append(v.astype(jnp.bfloat16).astype(jnp.float32))
        shifted = [[_lane_shift(r, b - 1).astype(jnp.bfloat16) for b in range(3)] for r in sec]
        parts = []
        for a in range(3):
            for b in range(3):
                parts.append(jnp.concatenate([shifted[2 * i + a][b] for i in range(reduced_rows)], axis=1))
        columns.append(jnp.concatenate(parts, axis=0))
    stacked = columns[0] if len(columns) == 1 else jnp.concatenate(columns, axis=1)
    full = jnp.dot(wd_ref[...], stacked, preferred_element_type=jnp.float32)
    full = jnp.maximum(full, 0.0).astype(jnp.bfloat16)
    outs = full.shape[0]
    span = reduced_rows * width
    for n, slot in enumerate(slots):
        rows_by_d = jnp.concatenate(
            [full[:, n * span + i * width : n * span + (i + 1) * width] for i in range(reduced_rows)], axis=0
        )
        r = lax.dot_general(pick, rows_by_d, (((1,), (1,)), ((), ())), preferred_element_type=jnp.float32)
        for i in range(reduced_rows):
            out_ref[slot, i] = r[:, i * outs : (i + 1) * outs].astype(out_ref.dtype)


def _edges_one_kernel(above_ref, xp_ref, below_ref, w9_ref, edge_ref):
    refs = (above_ref, xp_ref, below_ref)
    frames = xp_ref.shape[0]
    span = edge_ref.shape[-1]
    m = _middle_one(refs, [0, frames - 1], w9_ref)
    edge_ref[0] = m[:, :span]
    edge_ref[1] = m[:, span:]


def _inner_one_kernel(keep_ref, above_ref, xp_ref, below_ref, w9_ref, t3_ref, wd_ref, out_ref, side_ref, mid_ref):
    refs = (above_ref, xp_ref, below_ref)
    frames = xp_ref.shape[0]

    span = mid_ref.shape[-1]
    group = 4 if frames % 4 == 0 else 2

    def middle(g, carry):
        m = _middle_one(refs, [group * g + k for k in range(group)], w9_ref)
        for k in range(group):
            mid_ref[group * g + k] = m[:, k * span : (k + 1) * span]
        return carry

    lax.fori_loop(0, frames // group, middle, 0)
    side_ref[0] = mid_ref[1]
    side_ref[1] = mid_ref[frames - 2]

    channels = t3_ref.shape[0] // 2

    span = mid_ref.shape[-1]

    def run(t, pairs):
        stacks = [
            jnp.concatenate([mid_ref[u - 1], mid_ref[u], mid_ref[u + 1], mid_ref[u + 2]], axis=0)
            for u in [t + 2 * p for p in range(pairs)]
        ]
        stacked = stacks[0] if pairs == 1 else jnp.concatenate(stacks, axis=1)
        s = jnp.dot(t3_ref[...], stacked, preferred_element_type=jnp.float32)
        sums, ts = [], []
        for p in range(pairs):
            u = t + 2 * p
            part = s[:, p * span : (p + 1) * span]
            sums += [part[:channels], part[channels:]]
            ts += [u, u + 1]
        _down_many(sums, refs, ts, wd_ref, keep_ref, out_ref, [u - 1 for u in ts])

    def section(g, carry):
        run(4 * g + 1, 2)
        return carry

    lax.fori_loop(0, (frames - 2) // 4, section, 0)
    if (frames - 2) % 4:
        run(frames - 3, 1)


def _outer_one_kernel(
    keep_ref, above_ref, xp_ref, below_ref, t3_ref, wd_ref, before_ref, after_ref, edge_ref, side_ref, out_ref
):
    refs = (above_ref, xp_ref, below_ref)
    frames = xp_ref.shape[0]
    stacked = jnp.concatenate([before_ref[0], edge_ref[0], side_ref[0]], axis=0)
    _section_down(stacked, refs, 0, t3_ref, wd_ref, keep_ref, out_ref, 0)
    stacked = jnp.concatenate([side_ref[1], edge_ref[1], after_ref[0]], axis=0)
    _section_down(stacked, refs, frames - 1, t3_ref, wd_ref, keep_ref, out_ref, 1)


def block_one(above, rowed, below, keep_first, spatial_kernel, temporal_kernel, down_kernel):
    frames, rows, channels, width = rowed.shape
    rows = rows + 1
    mids = spatial_kernel.shape[2]
    outs = down_kernel.shape[2]
    w9 = jnp.transpose(spatial_kernel, (2, 0, 1, 3)).reshape(mids, 9 * channels)
    t3 = jnp.transpose(temporal_kernel, (1, 0, 2)).reshape(channels, 3 * mids)
    wd = jnp.transpose(down_kernel, (2, 0, 1, 3)).reshape(outs, 9 * channels)
    gap = jnp.zeros((channels, mids), t3.dtype)
    t4 = jnp.concatenate(
        [jnp.concatenate([t3, gap], axis=1), jnp.concatenate([gap, t3], axis=1)], axis=0
    )
    vmem = pltpu.MemorySpace.VMEM if hasattr(pltpu, "MemorySpace") else pltpu.VMEM
    smem = pltpu.MemorySpace.SMEM if hasattr(pltpu, "MemorySpace") else pltpu.SMEM
    params = pltpu.CompilerParams(vmem_limit_bytes=48 * 1024 * 1024)
    spec = pl.BlockSpec(memory_space=vmem)
    sspec = pl.BlockSpec(memory_space=smem)
    reduced_rows = (rows - 1) // 2
    plane = (mids, rows * width)
    out_plane = (reduced_rows, width // 2, outs)
    spatial_flops = 2 * rows * width * 9 * channels * mids
    section_flops = 2 * rows * width * 3 * mids * channels + 2 * reduced_rows * width * 9 * channels * outs
    edges = pl.pallas_call(
        _edges_one_kernel,
        out_shape=jax.ShapeDtypeStruct((2,) + plane, rowed.dtype),
        in_specs=[spec] * 4,
        out_specs=spec,
        compiler_params=params,
        cost_estimate=pl.CostEstimate(flops=2 * spatial_flops, bytes_accessed=2 * rowed.size, transcendentals=0),
    )(above, rowed, below, w9)
    before = from_behind(edges[1:], "tm", 1)
    after = from_behind(edges[:1], "tm", -1)
    inner, side = pl.pallas_call(
        _inner_one_kernel,
        out_shape=(
            jax.ShapeDtypeStruct((frames - 2,) + out_plane, rowed.dtype),
            jax.ShapeDtypeStruct((2,) + plane, rowed.dtype),
        ),
        in_specs=[sspec] + [spec] * 6,
        out_specs=(spec, spec),
        scratch_shapes=[pltpu.VMEM((frames,) + plane, jnp.bfloat16)],
        compiler_params=params,
        cost_estimate=pl.CostEstimate(
            flops=frames * (spatial_flops + section_flops), bytes_accessed=4 * rowed.size, transcendentals=0
        ),
    )(keep_first, above, rowed, below, w9, t4, wd)
    outer = pl.pallas_call(
        _outer_one_kernel,
        out_shape=jax.ShapeDtypeStruct((2,) + out_plane, rowed.dtype),
        in_specs=[sspec] + [spec] * 9,
        out_specs=spec,
        compiler_params=params,
    )(keep_first, above, rowed, below, t3, wd, before, after, edges, side)
    return jnp.concatenate([outer[:1], inner, outer[1:]], axis=0)


def _sublane_shift(x, by, axis):
    size = x.shape[axis]
    rolled = pltpu.roll(x, (-by) % size, axis)
    index = lax.broadcasted_iota(jnp.int32, x.shape, axis)
    inside = jnp.logical_and(index + by >= 0, index + by < size)
    return jnp.where(inside, rolled, jnp.zeros_like(rolled))


def _slab_two(above_ref, xp_ref, below_ref, f):
    return jnp.concatenate([above_ref[f], xp_ref[f], below_ref[f]], axis=0).astype(jnp.float32)


def _middle_two(slabs, w9_ref):
    rows = slabs[0].shape[0] - 2
    pieces = []
    for slab in slabs:
        shifted = [_sublane_shift(slab, b - 1, 1).astype(jnp.bfloat16) for b in range(3)]
        for i in range(rows):
            pieces.append(jnp.concatenate([shifted[b][i + a] for a in range(3) for b in range(3)], axis=1))
    stacked = jnp.concatenate(pieces, axis=0)
    m = jnp.dot(stacked, w9_ref[...], preferred_element_type=jnp.float32)
    return jnp.maximum(m, 0.0).astype(jnp.bfloat16)


def _edges_two_kernel(above_ref, xp_ref, below_ref, w9_ref, edge_ref):
    frames = xp_ref.shape[0]
    plane = edge_ref.shape[1]
    m = _middle_two(
        [_slab_two(above_ref, xp_ref, below_ref, 0), _slab_two(above_ref, xp_ref, below_ref, frames - 1)], w9_ref
    )
    edge_ref[0] = m[:plane]
    edge_ref[1] = m[plane:]


def _finish(s, xp_ref, t, out_ref, slot):
    rows, width = xp_ref.shape[1], xp_ref.shape[2]
    for i in range(rows):
        v = s[i * width : (i + 1) * width] + xp_ref[t, i].astype(jnp.float32)
        out_ref[slot, i] = jnp.maximum(v, 0.0).astype(out_ref.dtype)


def _inner_two_kernel(above_ref, xp_ref, below_ref, w9_ref, t3_ref, out_ref, side_ref, mid_ref):
    frames = xp_ref.shape[0]
    plane = mid_ref.shape[1]

    group = 8 if frames % 8 == 0 else 2

    def middle(g, carry):
        f = group * g
        m = _middle_two([_slab_two(above_ref, xp_ref, below_ref, f + k) for k in range(group)], w9_ref)
        for k in range(group):
            mid_ref[f + k] = m[k * plane : (k + 1) * plane]
        return carry

    lax.fori_loop(0, frames // group, middle, 0)
    side_ref[0] = mid_ref[1]
    side_ref[1] = mid_ref[frames - 2]

    def run(t, count):
        s = None
        for k in range(3):
            rows = jnp.concatenate([mid_ref[t - 1 + k + j] for j in range(count)], axis=0)
            d = jnp.dot(rows, t3_ref[k], preferred_element_type=jnp.float32)
            s = d if s is None else s + d
        for j in range(count):
            _finish(s[j * plane : (j + 1) * plane], xp_ref, t + j, out_ref, t + j - 1)

    def section(g, carry):
        run(4 * g + 1, 4)
        return carry

    lax.fori_loop(0, (frames - 2) // 4, section, 0)
    left = (frames - 2) % 4
    if left:
        run(frames - 1 - left, left)


def _outer_two_kernel(xp_ref, t3_ref, before_ref, after_ref, edge_ref, side_ref, out_ref):
    frames = xp_ref.shape[0]
    s = jnp.dot(before_ref[0], t3_ref[0], preferred_element_type=jnp.float32)
    s = s + jnp.dot(edge_ref[0], t3_ref[1], preferred_element_type=jnp.float32)
    s = s + jnp.dot(side_ref[0], t3_ref[2], preferred_element_type=jnp.float32)
    _finish(s, xp_ref, 0, out_ref, 0)
    s = jnp.dot(side_ref[1], t3_ref[0], preferred_element_type=jnp.float32)
    s = s + jnp.dot(edge_ref[1], t3_ref[1], preferred_element_type=jnp.float32)
    s = s + jnp.dot(after_ref[0], t3_ref[2], preferred_element_type=jnp.float32)
    _finish(s, xp_ref, frames - 1, out_ref, 1)


def block_two(above, rowed, below, spatial_kernel, temporal_kernel):
    frames, rows, width, channels = rowed.shape
    mids = spatial_kernel.shape[2]
    w9 = jnp.transpose(spatial_kernel, (0, 1, 3, 2)).reshape(9 * channels, mids)
    t3 = jnp.transpose(temporal_kernel, (0, 2, 1))
    vmem = pltpu.MemorySpace.VMEM if hasattr(pltpu, "MemorySpace") else pltpu.VMEM
    params = pltpu.CompilerParams(vmem_limit_bytes=48 * 1024 * 1024)
    spec = pl.BlockSpec(memory_space=vmem)
    plane = (rows * width, mids)
    edges = pl.pallas_call(
        _edges_two_kernel,
        out_shape=jax.ShapeDtypeStruct((2,) + plane, rowed.dtype),
        in_specs=[spec] * 4,
        out_specs=spec,
        compiler_params=params,
        cost_estimate=pl.CostEstimate(
            flops=2 * 2 * rows * width * 9 * channels * mids, bytes_accessed=2 * rowed.size, transcendentals=0
        ),
    )(above, rowed, below, w9)
    before = from_behind(edges[1:], "tm", 1)
    after = from_behind(edges[:1], "tm", -1)
    inner, side = pl.pallas_call(
        _inner_two_kernel,
        out_shape=(
            jax.ShapeDtypeStruct((frames - 2, rows, width, channels), rowed.dtype),
            jax.ShapeDtypeStruct((2,) + plane, rowed.dtype),
        ),
        in_specs=[spec] * 5,
        out_specs=(spec, spec),
        scratch_shapes=[pltpu.VMEM((frames,) + plane, jnp.bfloat16)],
        compiler_params=params,
        cost_estimate=pl.CostEstimate(
            flops=2 * frames * rows * width * (9 * channels * mids + 3 * mids * channels),
            bytes_accessed=4 * rowed.size,
            transcendentals=0,
        ),
    )(above, rowed, below, w9, t3)
    outer = pl.pallas_call(
        _outer_two_kernel,
        out_shape=jax.ShapeDtypeStruct((2, rows, width, channels), rowed.dtype),
        in_specs=[spec] * 6,
        out_specs=spec,
        compiler_params=params,
    )(rowed, t3, before, after, edges, side)
    return jnp.concatenate([outer[:1], inner, outer[1:]], axis=0)


def _copy_kernel(top_ref, bottom_ref, top_out, bottom_out):
    top_out[...] = top_ref[...]
    bottom_out[...] = bottom_ref[...]


def edge_rows(block, top, bottom):
    frames, rows, channels, width = block.shape
    top_spec = pl.BlockSpec((frames, top, channels, width), lambda i: (0, rows // top - 1, 0, 0))
    bottom_spec = pl.BlockSpec((frames, bottom, channels, width), lambda i: (0, 0, 0, 0))
    return pl.pallas_call(
        _copy_kernel,
        grid=(1,),
        out_shape=(
            jax.ShapeDtypeStruct((frames, top, channels, width), block.dtype),
            jax.ShapeDtypeStruct((frames, bottom, channels, width), block.dtype),
        ),
        in_specs=[top_spec, bottom_spec],
        out_specs=(pl.BlockSpec((frames, top, channels, width), lambda i: (0, 0, 0, 0)), bottom_spec),
    )(block, block)


def on_device(video_clip, spatial_one, temporal_one, down_weight, spatial_two, temporal_two):
    rows = video_clip.shape[1]
    top, bottom = edge_rows(video_clip, 2, 1)
    above = from_behind(top, "row", 1)
    below = from_behind(bottom, "row", -1)
    keep_first = (lax.axis_index("row") > 0).astype(jnp.int32).reshape(1)
    reduced = block_one(above, video_clip, below, keep_first, spatial_one, temporal_one, down_weight)
    rows = reduced.shape[1]
    above = from_behind(reduced[:, rows - 1 :], "row", 1)
    below = from_behind(reduced[:, :1], "row", -1)
    return block_two(above, reduced, below, spatial_two, temporal_two)


def solution(mesh):
    placed = (P("tm", "row", None, None), P(), P(), P(), P(), P())
    return jax.shard_map(
        on_device, mesh=mesh, in_specs=placed, out_specs=P("tm", "row", None, None), check_vma=False
    )
```

```python
import functools

import jax
import jax.numpy as jnp
from jax import lax
from jax.experimental import pallas as pl
from jax.experimental.pallas import tpu as pltpu
from jax.sharding import PartitionSpec as P


def padded_2(block, sides, width):
    for axis, dim in sides:
        count = lax.axis_size(axis)
        forward = [(i, i + 1) for i in range(count - 1)]
        backward = [(target, source) for source, target in forward]
        low = lax.ppermute(
            lax.slice_in_dim(block, block.shape[dim] - width, None, axis=dim), axis, forward
        )
        high = lax.ppermute(lax.slice_in_dim(block, 0, width, axis=dim), axis, backward)
        block = jnp.concatenate([low, block, high], axis=dim)
    return block


def from_behind(array, axis, by):
    devices = lax.axis_size(axis)
    pairs = [(i, i + by) for i in range(devices) if 0 <= i + by < devices]
    return lax.ppermute(array, axis, pairs)


def spatial(source, kernel, layout):
    return lax.conv_general_dilated(
        source,
        kernel,
        (1, 1),
        ((0, 0), (1, 1)),
        dimension_numbers=(layout, "HWOI", layout),
        preferred_element_type=jnp.float32,
    )


def temporal(source, kernel, layout):
    return lax.conv_general_dilated(
        source,
        kernel[:, None],
        (1, 1),
        ((0, 0), (0, 0)),
        dimension_numbers=(layout, "HWOI", layout),
        preferred_element_type=jnp.float32,
    )


def residual_block(source, spatial_kernel, temporal_kernel, space_layout, time_layout):
    padded = padded_2(source, (("tm", 0), ("row", 1)), 1)
    framed = jax.nn.relu(spatial(padded, spatial_kernel, space_layout)).astype(jnp.bfloat16)
    summed = source.astype(jnp.float32) + temporal(framed, temporal_kernel, time_layout)
    return jax.nn.relu(summed).astype(jnp.bfloat16)


def _lane_shift(x, by):
    width = x.shape[-1]
    rolled = pltpu.roll(x, (-by) % width, x.ndim - 1)
    lane = lax.broadcasted_iota(jnp.int32, x.shape, x.ndim - 1)
    inside = jnp.logical_and(lane + by >= 0, lane + by < width)
    return jnp.where(inside, rolled, jnp.zeros_like(rolled))


def _middle_one(refs, fs, w9_ref):
    above_ref, xp_ref, below_ref = refs
    rows = xp_ref.shape[1] + 1
    columns = []
    for f in fs:
        slab = jnp.concatenate([above_ref[f], xp_ref[f], below_ref[f]], axis=0).astype(jnp.float32)
        shifted = [_lane_shift(slab, b - 1).astype(jnp.bfloat16) for b in range(3)]
        parts = []
        for a in range(3):
            for b in range(3):
                parts.append(jnp.concatenate([shifted[b][h + a] for h in range(rows)], axis=1))
        columns.append(jnp.concatenate(parts, axis=0))
    stacked = columns[0] if len(columns) == 1 else jnp.concatenate(columns, axis=1)
    m = jnp.dot(w9_ref[...], stacked, preferred_element_type=jnp.float32)
    return jnp.maximum(m, 0.0).astype(jnp.bfloat16)


def _section_down(stacked, refs, t, t3_ref, wd_ref, keep_ref, out_ref, slot):
    s = jnp.dot(t3_ref[...], stacked, preferred_element_type=jnp.float32)
    _down(s, refs, t, wd_ref, keep_ref, out_ref, slot)


def _down(s, refs, t, wd_ref, keep_ref, out_ref, slot):
    _down_many([s], refs, [t], wd_ref, keep_ref, out_ref, [slot])


def _down_many(sums, refs, ts, wd_ref, keep_ref, out_ref, slots):
    above_ref, xp_ref, _ = refs
    rows = xp_ref.shape[1] + 1
    width = xp_ref.shape[-1]
    reduced_rows = (rows - 1) // 2
    lane = lax.broadcasted_iota(jnp.int32, (width // 2, width), 1)
    column = lax.broadcasted_iota(jnp.int32, (width // 2, width), 0)
    pick = (lane == 2 * column).astype(jnp.bfloat16)
    columns = []
    for s, t in zip(sums, ts):
        sec = []
        for h in range(rows):
            own = above_ref[t, 1] if h == 0 else xp_ref[t, h - 1]
            v = s[:, h * width : (h + 1) * width] + own.astype(jnp.float32)
            v = jnp.maximum(v, 0.0)
            if h == 0:
                v = v * keep_ref[0].astype(jnp.float32)
            sec.append(v.astype(jnp.bfloat16).astype(jnp.float32))
        shifted = [[_lane_shift(r, b - 1).astype(jnp.bfloat16) for b in range(3)] for r in sec]
        parts = []
        for a in range(3):
            for b in range(3):
                parts.append(jnp.concatenate([shifted[2 * i + a][b] for i in range(reduced_rows)], axis=1))
        columns.append(jnp.concatenate(parts, axis=0))
    stacked = columns[0] if len(columns) == 1 else jnp.concatenate(columns, axis=1)
    full = jnp.dot(wd_ref[...], stacked, preferred_element_type=jnp.float32)
    full = jnp.maximum(full, 0.0).astype(jnp.bfloat16)
    outs = full.shape[0]
    span = reduced_rows * width
    for n, slot in enumerate(slots):
        rows_by_d = jnp.concatenate(
            [full[:, n * span + i * width : n * span + (i + 1) * width] for i in range(reduced_rows)], axis=0
        )
        r = lax.dot_general(pick, rows_by_d, (((1,), (1,)), ((), ())), preferred_element_type=jnp.float32)
        for i in range(reduced_rows):
            out_ref[slot, i] = r[:, i * outs : (i + 1) * outs].astype(out_ref.dtype)


def _edges_one_kernel(above_ref, xp_ref, below_ref, w9_ref, edge_ref):
    refs = (above_ref, xp_ref, below_ref)
    frames = xp_ref.shape[0]
    span = edge_ref.shape[-1]
    m = _middle_one(refs, [0, frames - 1], w9_ref)
    edge_ref[0] = m[:, :span]
    edge_ref[1] = m[:, span:]


def _inner_one_kernel(keep_ref, above_ref, xp_ref, below_ref, w9_ref, t3_ref, wd_ref, out_ref, side_ref, mid_ref):
    refs = (above_ref, xp_ref, below_ref)
    frames = xp_ref.shape[0]

    span = mid_ref.shape[-1]
    group = 4 if frames % 4 == 0 else 2

    def middle(g, carry):
        m = _middle_one(refs, [group * g + k for k in range(group)], w9_ref)
        for k in range(group):
            mid_ref[group * g + k] = m[:, k * span : (k + 1) * span]
        return carry

    lax.fori_loop(0, frames // group, middle, 0)
    side_ref[0] = mid_ref[1]
    side_ref[1] = mid_ref[frames - 2]

    channels = t3_ref.shape[0] // 2

    span = mid_ref.shape[-1]

    def run(t, pairs):
        stacks = [
            jnp.concatenate([mid_ref[u - 1], mid_ref[u], mid_ref[u + 1], mid_ref[u + 2]], axis=0)
            for u in [t + 2 * p for p in range(pairs)]
        ]
        stacked = stacks[0] if pairs == 1 else jnp.concatenate(stacks, axis=1)
        s = jnp.dot(t3_ref[...], stacked, preferred_element_type=jnp.float32)
        sums, ts = [], []
        for p in range(pairs):
            u = t + 2 * p
            part = s[:, p * span : (p + 1) * span]
            sums += [part[:channels], part[channels:]]
            ts += [u, u + 1]
        _down_many(sums, refs, ts, wd_ref, keep_ref, out_ref, [u - 1 for u in ts])

    def section(g, carry):
        run(4 * g + 1, 2)
        return carry

    lax.fori_loop(0, (frames - 2) // 4, section, 0)
    if (frames - 2) % 4:
        run(frames - 3, 1)


def _outer_one_kernel(
    keep_ref, above_ref, xp_ref, below_ref, t3_ref, wd_ref, before_ref, after_ref, edge_ref, side_ref, out_ref
):
    refs = (above_ref, xp_ref, below_ref)
    frames = xp_ref.shape[0]
    first = jnp.concatenate([before_ref[0], edge_ref[0], side_ref[0]], axis=0)
    last = jnp.concatenate([side_ref[1], edge_ref[1], after_ref[0]], axis=0)
    sums = jnp.dot(t3_ref[...], jnp.concatenate([first, last], axis=1), preferred_element_type=jnp.float32)
    span = first.shape[-1]
    _down_many(
        [sums[:, :span], sums[:, span:]], refs, [0, frames - 1], wd_ref, keep_ref, out_ref, [0, 1]
    )


def block_one(above, rowed, below, keep_first, spatial_kernel, temporal_kernel, down_kernel):
    frames, rows, channels, width = rowed.shape
    rows = rows + 1
    mids = spatial_kernel.shape[2]
    outs = down_kernel.shape[2]
    w9 = jnp.transpose(spatial_kernel, (2, 0, 1, 3)).reshape(mids, 9 * channels)
    t3 = jnp.transpose(temporal_kernel, (1, 0, 2)).reshape(channels, 3 * mids)
    wd = jnp.transpose(down_kernel, (2, 0, 1, 3)).reshape(outs, 9 * channels)
    gap = jnp.zeros((channels, mids), t3.dtype)
    t4 = jnp.concatenate(
        [jnp.concatenate([t3, gap], axis=1), jnp.concatenate([gap, t3], axis=1)], axis=0
    )
    vmem = pltpu.MemorySpace.VMEM if hasattr(pltpu, "MemorySpace") else pltpu.VMEM
    smem = pltpu.MemorySpace.SMEM if hasattr(pltpu, "MemorySpace") else pltpu.SMEM
    params = pltpu.CompilerParams(vmem_limit_bytes=48 * 1024 * 1024)
    spec = pl.BlockSpec(memory_space=vmem)
    sspec = pl.BlockSpec(memory_space=smem)
    reduced_rows = (rows - 1) // 2
    plane = (mids, rows * width)
    out_plane = (reduced_rows, width // 2, outs)
    spatial_flops = 2 * rows * width * 9 * channels * mids
    section_flops = 2 * rows * width * 3 * mids * channels + 2 * reduced_rows * width * 9 * channels * outs
    edges = pl.pallas_call(
        _edges_one_kernel,
        out_shape=jax.ShapeDtypeStruct((2,) + plane, rowed.dtype),
        in_specs=[spec] * 4,
        out_specs=spec,
        compiler_params=params,
        cost_estimate=pl.CostEstimate(flops=2 * spatial_flops, bytes_accessed=2 * rowed.size, transcendentals=0),
    )(above, rowed, below, w9)
    before = from_behind(edges[1:], "tm", 1)
    after = from_behind(edges[:1], "tm", -1)
    inner, side = pl.pallas_call(
        _inner_one_kernel,
        out_shape=(
            jax.ShapeDtypeStruct((frames - 2,) + out_plane, rowed.dtype),
            jax.ShapeDtypeStruct((2,) + plane, rowed.dtype),
        ),
        in_specs=[sspec] + [spec] * 6,
        out_specs=(spec, spec),
        scratch_shapes=[pltpu.VMEM((frames,) + plane, jnp.bfloat16)],
        compiler_params=params,
        cost_estimate=pl.CostEstimate(
            flops=frames * (spatial_flops + section_flops), bytes_accessed=4 * rowed.size, transcendentals=0
        ),
    )(keep_first, above, rowed, below, w9, t4, wd)
    outer = pl.pallas_call(
        _outer_one_kernel,
        out_shape=jax.ShapeDtypeStruct((2,) + out_plane, rowed.dtype),
        in_specs=[sspec] + [spec] * 9,
        out_specs=spec,
        compiler_params=params,
    )(keep_first, above, rowed, below, t3, wd, before, after, edges, side)
    return jnp.concatenate([outer[:1], inner, outer[1:]], axis=0)


def _sublane_shift(x, by, axis):
    size = x.shape[axis]
    rolled = pltpu.roll(x, (-by) % size, axis)
    index = lax.broadcasted_iota(jnp.int32, x.shape, axis)
    inside = jnp.logical_and(index + by >= 0, index + by < size)
    return jnp.where(inside, rolled, jnp.zeros_like(rolled))


def _slab_two(above_ref, xp_ref, below_ref, f):
    return jnp.concatenate([above_ref[f], xp_ref[f], below_ref[f]], axis=0).astype(jnp.float32)


def _middle_two(slabs, w9_ref):
    rows = slabs[0].shape[0] - 2
    pieces = []
    for slab in slabs:
        shifted = [_sublane_shift(slab, b - 1, 1).astype(jnp.bfloat16) for b in range(3)]
        for i in range(rows):
            pieces.append(jnp.concatenate([shifted[b][i + a] for a in range(3) for b in range(3)], axis=1))
    stacked = jnp.concatenate(pieces, axis=0)
    m = jnp.dot(stacked, w9_ref[...], preferred_element_type=jnp.float32)
    return jnp.maximum(m, 0.0).astype(jnp.bfloat16)


def _edges_two_kernel(above_ref, xp_ref, below_ref, w9_ref, edge_ref):
    frames = xp_ref.shape[0]
    plane = edge_ref.shape[1]
    m = _middle_two(
        [_slab_two(above_ref, xp_ref, below_ref, 0), _slab_two(above_ref, xp_ref, below_ref, frames - 1)], w9_ref
    )
    edge_ref[0] = m[:plane]
    edge_ref[1] = m[plane:]


def _finish(s, xp_ref, t, out_ref, slot):
    rows, width = xp_ref.shape[1], xp_ref.shape[2]
    for i in range(rows):
        v = s[i * width : (i + 1) * width] + xp_ref[t, i].astype(jnp.float32)
        out_ref[slot, i] = jnp.maximum(v, 0.0).astype(out_ref.dtype)


def _inner_two_kernel(above_ref, xp_ref, below_ref, w9_ref, t3_ref, out_ref, side_ref, mid_ref):
    frames = xp_ref.shape[0]
    plane = mid_ref.shape[1]

    group = 8 if frames % 8 == 0 else 2

    def middle(g, carry):
        f = group * g
        m = _middle_two([_slab_two(above_ref, xp_ref, below_ref, f + k) for k in range(group)], w9_ref)
        for k in range(group):
            mid_ref[f + k] = m[k * plane : (k + 1) * plane]
        return carry

    lax.fori_loop(0, frames // group, middle, 0)
    side_ref[0] = mid_ref[1]
    side_ref[1] = mid_ref[frames - 2]

    def run(t, count):
        s = None
        for k in range(3):
            rows = jnp.concatenate([mid_ref[t - 1 + k + j] for j in range(count)], axis=0)
            d = jnp.dot(rows, t3_ref[k], preferred_element_type=jnp.float32)
            s = d if s is None else s + d
        for j in range(count):
            _finish(s[j * plane : (j + 1) * plane], xp_ref, t + j, out_ref, t + j - 1)

    def section(g, carry):
        run(4 * g + 1, 4)
        return carry

    lax.fori_loop(0, (frames - 2) // 4, section, 0)
    left = (frames - 2) % 4
    if left:
        run(frames - 1 - left, left)


def _outer_two_kernel(xp_ref, t3_ref, before_ref, after_ref, edge_ref, side_ref, out_ref):
    frames = xp_ref.shape[0]
    s = jnp.dot(before_ref[0], t3_ref[0], preferred_element_type=jnp.float32)
    s = s + jnp.dot(edge_ref[0], t3_ref[1], preferred_element_type=jnp.float32)
    s = s + jnp.dot(side_ref[0], t3_ref[2], preferred_element_type=jnp.float32)
    _finish(s, xp_ref, 0, out_ref, 0)
    s = jnp.dot(side_ref[1], t3_ref[0], preferred_element_type=jnp.float32)
    s = s + jnp.dot(edge_ref[1], t3_ref[1], preferred_element_type=jnp.float32)
    s = s + jnp.dot(after_ref[0], t3_ref[2], preferred_element_type=jnp.float32)
    _finish(s, xp_ref, frames - 1, out_ref, 1)


def block_two(above, rowed, below, spatial_kernel, temporal_kernel):
    frames, rows, width, channels = rowed.shape
    mids = spatial_kernel.shape[2]
    w9 = jnp.transpose(spatial_kernel, (0, 1, 3, 2)).reshape(9 * channels, mids)
    t3 = jnp.transpose(temporal_kernel, (0, 2, 1))
    vmem = pltpu.MemorySpace.VMEM if hasattr(pltpu, "MemorySpace") else pltpu.VMEM
    params = pltpu.CompilerParams(vmem_limit_bytes=48 * 1024 * 1024)
    spec = pl.BlockSpec(memory_space=vmem)
    plane = (rows * width, mids)
    edges = pl.pallas_call(
        _edges_two_kernel,
        out_shape=jax.ShapeDtypeStruct((2,) + plane, rowed.dtype),
        in_specs=[spec] * 4,
        out_specs=spec,
        compiler_params=params,
        cost_estimate=pl.CostEstimate(
            flops=2 * 2 * rows * width * 9 * channels * mids, bytes_accessed=2 * rowed.size, transcendentals=0
        ),
    )(above, rowed, below, w9)
    before = from_behind(edges[1:], "tm", 1)
    after = from_behind(edges[:1], "tm", -1)
    inner, side = pl.pallas_call(
        _inner_two_kernel,
        out_shape=(
            jax.ShapeDtypeStruct((frames - 2, rows, width, channels), rowed.dtype),
            jax.ShapeDtypeStruct((2,) + plane, rowed.dtype),
        ),
        in_specs=[spec] * 5,
        out_specs=(spec, spec),
        scratch_shapes=[pltpu.VMEM((frames,) + plane, jnp.bfloat16)],
        compiler_params=params,
        cost_estimate=pl.CostEstimate(
            flops=2 * frames * rows * width * (9 * channels * mids + 3 * mids * channels),
            bytes_accessed=4 * rowed.size,
            transcendentals=0,
        ),
    )(above, rowed, below, w9, t3)
    outer = pl.pallas_call(
        _outer_two_kernel,
        out_shape=jax.ShapeDtypeStruct((2, rows, width, channels), rowed.dtype),
        in_specs=[spec] * 6,
        out_specs=spec,
        compiler_params=params,
    )(rowed, t3, before, after, edges, side)
    return jnp.concatenate([outer[:1], inner, outer[1:]], axis=0)


def _copy_kernel(top_ref, bottom_ref, top_out, bottom_out):
    top_out[...] = top_ref[...]
    bottom_out[...] = bottom_ref[...]


def edge_rows(block, top, bottom):
    frames, rows, channels, width = block.shape
    top_spec = pl.BlockSpec((frames, top, channels, width), lambda i: (0, rows // top - 1, 0, 0))
    bottom_spec = pl.BlockSpec((frames, bottom, channels, width), lambda i: (0, 0, 0, 0))
    return pl.pallas_call(
        _copy_kernel,
        grid=(1,),
        out_shape=(
            jax.ShapeDtypeStruct((frames, top, channels, width), block.dtype),
            jax.ShapeDtypeStruct((frames, bottom, channels, width), block.dtype),
        ),
        in_specs=[top_spec, bottom_spec],
        out_specs=(pl.BlockSpec((frames, top, channels, width), lambda i: (0, 0, 0, 0)), bottom_spec),
    )(block, block)


def on_device(video_clip, spatial_one, temporal_one, down_weight, spatial_two, temporal_two):
    rows = video_clip.shape[1]
    top, bottom = edge_rows(video_clip, 2, 1)
    above = from_behind(top, "row", 1)
    below = from_behind(bottom, "row", -1)
    keep_first = (lax.axis_index("row") > 0).astype(jnp.int32).reshape(1)
    reduced = block_one(above, video_clip, below, keep_first, spatial_one, temporal_one, down_weight)
    rows = reduced.shape[1]
    above = from_behind(reduced[:, rows - 1 :], "row", 1)
    below = from_behind(reduced[:, :1], "row", -1)
    return block_two(above, reduced, below, spatial_two, temporal_two)


def solution(mesh):
    placed = (P("tm", "row", None, None), P(), P(), P(), P(), P())
    return jax.shard_map(
        on_device, mesh=mesh, in_specs=placed, out_specs=P("tm", "row", None, None), check_vma=False
    )
```

```python
import functools

import jax
import jax.numpy as jnp
from jax import lax
from jax.experimental import pallas as pl
from jax.experimental.pallas import tpu as pltpu
from jax.sharding import PartitionSpec as P


def padded_2(block, sides, width):
    for axis, dim in sides:
        count = lax.axis_size(axis)
        forward = [(i, i + 1) for i in range(count - 1)]
        backward = [(target, source) for source, target in forward]
        low = lax.ppermute(
            lax.slice_in_dim(block, block.shape[dim] - width, None, axis=dim), axis, forward
        )
        high = lax.ppermute(lax.slice_in_dim(block, 0, width, axis=dim), axis, backward)
        block = jnp.concatenate([low, block, high], axis=dim)
    return block


def from_behind(array, axis, by):
    devices = lax.axis_size(axis)
    pairs = [(i, i + by) for i in range(devices) if 0 <= i + by < devices]
    return lax.ppermute(array, axis, pairs)


def spatial(source, kernel, layout):
    return lax.conv_general_dilated(
        source,
        kernel,
        (1, 1),
        ((0, 0), (1, 1)),
        dimension_numbers=(layout, "HWOI", layout),
        preferred_element_type=jnp.float32,
    )


def temporal(source, kernel, layout):
    return lax.conv_general_dilated(
        source,
        kernel[:, None],
        (1, 1),
        ((0, 0), (0, 0)),
        dimension_numbers=(layout, "HWOI", layout),
        preferred_element_type=jnp.float32,
    )


def residual_block(source, spatial_kernel, temporal_kernel, space_layout, time_layout):
    padded = padded_2(source, (("tm", 0), ("row", 1)), 1)
    framed = jax.nn.relu(spatial(padded, spatial_kernel, space_layout)).astype(jnp.bfloat16)
    summed = source.astype(jnp.float32) + temporal(framed, temporal_kernel, time_layout)
    return jax.nn.relu(summed).astype(jnp.bfloat16)


def _lane_shift(x, by):
    width = x.shape[-1]
    rolled = pltpu.roll(x, (-by) % width, x.ndim - 1)
    lane = lax.broadcasted_iota(jnp.int32, x.shape, x.ndim - 1)
    inside = jnp.logical_and(lane + by >= 0, lane + by < width)
    return jnp.where(inside, rolled, jnp.zeros_like(rolled))


def _middle_one(refs, fs, w9_ref):
    above_ref, xp_ref, below_ref = refs
    rows = xp_ref.shape[1] + 1
    columns = []
    for f in fs:
        slab = jnp.concatenate([above_ref[f], xp_ref[f], below_ref[f]], axis=0).astype(jnp.float32)
        shifted = [_lane_shift(slab, b - 1).astype(jnp.bfloat16) for b in range(3)]
        parts = []
        for a in range(3):
            for b in range(3):
                parts.append(jnp.concatenate([shifted[b][h + a] for h in range(rows)], axis=1))
        columns.append(jnp.concatenate(parts, axis=0))
    stacked = columns[0] if len(columns) == 1 else jnp.concatenate(columns, axis=1)
    m = jnp.dot(w9_ref[...], stacked, preferred_element_type=jnp.float32)
    return jnp.maximum(m, 0.0).astype(jnp.bfloat16)


def _section_down(stacked, refs, t, t3_ref, wd_ref, keep_ref, out_ref, slot):
    s = jnp.dot(t3_ref[...], stacked, preferred_element_type=jnp.float32)
    _down(s, refs, t, wd_ref, keep_ref, out_ref, slot)


def _down(s, refs, t, wd_ref, keep_ref, out_ref, slot):
    _down_many([s], refs, [t], wd_ref, keep_ref, out_ref, [slot])


def _down_many(sums, refs, ts, wd_ref, keep_ref, out_ref, slots):
    above_ref, xp_ref, _ = refs
    rows = xp_ref.shape[1] + 1
    width = xp_ref.shape[-1]
    reduced_rows = (rows - 1) // 2
    lane = lax.broadcasted_iota(jnp.int32, (width // 2, width), 1)
    column = lax.broadcasted_iota(jnp.int32, (width // 2, width), 0)
    pick = (lane == 2 * column).astype(jnp.bfloat16)
    columns = []
    for s, t in zip(sums, ts):
        sec = []
        for h in range(rows):
            own = above_ref[t, 1] if h == 0 else xp_ref[t, h - 1]
            v = s[:, h * width : (h + 1) * width] + own.astype(jnp.float32)
            v = jnp.maximum(v, 0.0)
            if h == 0:
                v = v * keep_ref[0].astype(jnp.float32)
            sec.append(v.astype(jnp.bfloat16).astype(jnp.float32))
        shifted = [[_lane_shift(r, b - 1).astype(jnp.bfloat16) for b in range(3)] for r in sec]
        parts = []
        for a in range(3):
            for b in range(3):
                parts.append(jnp.concatenate([shifted[2 * i + a][b] for i in range(reduced_rows)], axis=1))
        columns.append(jnp.concatenate(parts, axis=0))
    stacked = columns[0] if len(columns) == 1 else jnp.concatenate(columns, axis=1)
    full = jnp.dot(wd_ref[...], stacked, preferred_element_type=jnp.float32)
    full = jnp.maximum(full, 0.0).astype(jnp.bfloat16)
    outs = full.shape[0]
    span = reduced_rows * width
    for n, slot in enumerate(slots):
        rows_by_d = jnp.concatenate(
            [full[:, n * span + i * width : n * span + (i + 1) * width] for i in range(reduced_rows)], axis=0
        )
        r = lax.dot_general(pick, rows_by_d, (((1,), (1,)), ((), ())), preferred_element_type=jnp.float32)
        for i in range(reduced_rows):
            out_ref[slot, i] = r[:, i * outs : (i + 1) * outs].astype(out_ref.dtype)


def _edges_one_kernel(above_ref, xp_ref, below_ref, w9_ref, edge_ref):
    refs = (above_ref, xp_ref, below_ref)
    frames = xp_ref.shape[0]
    span = edge_ref.shape[-1]
    m = _middle_one(refs, [0, frames - 1], w9_ref)
    edge_ref[0] = m[:, :span]
    edge_ref[1] = m[:, span:]


def _inner_one_kernel(keep_ref, above_ref, xp_ref, below_ref, w9_ref, t3_ref, wd_ref, out_ref, side_ref, mid_ref):
    refs = (above_ref, xp_ref, below_ref)
    frames = xp_ref.shape[0]

    span = mid_ref.shape[-1]
    group = 4 if frames % 4 == 0 else 2

    def middle(g, carry):
        m = _middle_one(refs, [group * g + k for k in range(group)], w9_ref)
        for k in range(group):
            mid_ref[group * g + k] = m[:, k * span : (k + 1) * span]
        return carry

    lax.fori_loop(0, frames // group, middle, 0)
    side_ref[0] = mid_ref[1]
    side_ref[1] = mid_ref[frames - 2]

    channels = t3_ref.shape[0] // 2

    span = mid_ref.shape[-1]

    def run(t, pairs):
        stacks = [
            jnp.concatenate([mid_ref[u - 1], mid_ref[u], mid_ref[u + 1], mid_ref[u + 2]], axis=0)
            for u in [t + 2 * p for p in range(pairs)]
        ]
        stacked = stacks[0] if pairs == 1 else jnp.concatenate(stacks, axis=1)
        s = jnp.dot(t3_ref[...], stacked, preferred_element_type=jnp.float32)
        sums, ts = [], []
        for p in range(pairs):
            u = t + 2 * p
            part = s[:, p * span : (p + 1) * span]
            sums += [part[:channels], part[channels:]]
            ts += [u, u + 1]
        _down_many(sums, refs, ts, wd_ref, keep_ref, out_ref, [u - 1 for u in ts])

    def section(g, carry):
        run(6 * g + 1, 3)
        return carry

    lax.fori_loop(0, (frames - 2) // 6, section, 0)
    left = ((frames - 2) % 6) // 2
    if left:
        run(frames - 1 - 2 * left, left)


def _outer_one_kernel(
    keep_ref, above_ref, xp_ref, below_ref, t3_ref, wd_ref, before_ref, after_ref, edge_ref, side_ref, out_ref
):
    refs = (above_ref, xp_ref, below_ref)
    frames = xp_ref.shape[0]
    first = jnp.concatenate([before_ref[0], edge_ref[0], side_ref[0]], axis=0)
    last = jnp.concatenate([side_ref[1], edge_ref[1], after_ref[0]], axis=0)
    sums = jnp.dot(t3_ref[...], jnp.concatenate([first, last], axis=1), preferred_element_type=jnp.float32)
    span = first.shape[-1]
    _down_many(
        [sums[:, :span], sums[:, span:]], refs, [0, frames - 1], wd_ref, keep_ref, out_ref, [0, 1]
    )


def block_one(above, rowed, below, keep_first, spatial_kernel, temporal_kernel, down_kernel):
    frames, rows, channels, width = rowed.shape
    rows = rows + 1
    mids = spatial_kernel.shape[2]
    outs = down_kernel.shape[2]
    w9 = jnp.transpose(spatial_kernel, (2, 0, 1, 3)).reshape(mids, 9 * channels)
    t3 = jnp.transpose(temporal_kernel, (1, 0, 2)).reshape(channels, 3 * mids)
    wd = jnp.transpose(down_kernel, (2, 0, 1, 3)).reshape(outs, 9 * channels)
    gap = jnp.zeros((channels, mids), t3.dtype)
    t4 = jnp.concatenate(
        [jnp.concatenate([t3, gap], axis=1), jnp.concatenate([gap, t3], axis=1)], axis=0
    )
    vmem = pltpu.MemorySpace.VMEM if hasattr(pltpu, "MemorySpace") else pltpu.VMEM
    smem = pltpu.MemorySpace.SMEM if hasattr(pltpu, "MemorySpace") else pltpu.SMEM
    params = pltpu.CompilerParams(vmem_limit_bytes=48 * 1024 * 1024)
    spec = pl.BlockSpec(memory_space=vmem)
    sspec = pl.BlockSpec(memory_space=smem)
    reduced_rows = (rows - 1) // 2
    plane = (mids, rows * width)
    out_plane = (reduced_rows, width // 2, outs)
    spatial_flops = 2 * rows * width * 9 * channels * mids
    section_flops = 2 * rows * width * 3 * mids * channels + 2 * reduced_rows * width * 9 * channels * outs
    edges = pl.pallas_call(
        _edges_one_kernel,
        out_shape=jax.ShapeDtypeStruct((2,) + plane, rowed.dtype),
        in_specs=[spec] * 4,
        out_specs=spec,
        compiler_params=params,
        cost_estimate=pl.CostEstimate(flops=2 * spatial_flops, bytes_accessed=2 * rowed.size, transcendentals=0),
    )(above, rowed, below, w9)
    before = from_behind(edges[1:], "tm", 1)
    after = from_behind(edges[:1], "tm", -1)
    inner, side = pl.pallas_call(
        _inner_one_kernel,
        out_shape=(
            jax.ShapeDtypeStruct((frames - 2,) + out_plane, rowed.dtype),
            jax.ShapeDtypeStruct((2,) + plane, rowed.dtype),
        ),
        in_specs=[sspec] + [spec] * 6,
        out_specs=(spec, spec),
        scratch_shapes=[pltpu.VMEM((frames,) + plane, jnp.bfloat16)],
        compiler_params=params,
        cost_estimate=pl.CostEstimate(
            flops=frames * (spatial_flops + section_flops), bytes_accessed=4 * rowed.size, transcendentals=0
        ),
    )(keep_first, above, rowed, below, w9, t4, wd)
    outer = pl.pallas_call(
        _outer_one_kernel,
        out_shape=jax.ShapeDtypeStruct((2,) + out_plane, rowed.dtype),
        in_specs=[sspec] + [spec] * 9,
        out_specs=spec,
        compiler_params=params,
    )(keep_first, above, rowed, below, t3, wd, before, after, edges, side)
    return jnp.concatenate([outer[:1], inner, outer[1:]], axis=0)


def _sublane_shift(x, by, axis):
    size = x.shape[axis]
    rolled = pltpu.roll(x, (-by) % size, axis)
    index = lax.broadcasted_iota(jnp.int32, x.shape, axis)
    inside = jnp.logical_and(index + by >= 0, index + by < size)
    return jnp.where(inside, rolled, jnp.zeros_like(rolled))


def _slab_two(above_ref, xp_ref, below_ref, f):
    return jnp.concatenate([above_ref[f], xp_ref[f], below_ref[f]], axis=0).astype(jnp.float32)


def _middle_two(slabs, w9_ref):
    rows = slabs[0].shape[0] - 2
    pieces = []
    for slab in slabs:
        shifted = [_sublane_shift(slab, b - 1, 1).astype(jnp.bfloat16) for b in range(3)]
        for i in range(rows):
            pieces.append(jnp.concatenate([shifted[b][i + a] for a in range(3) for b in range(3)], axis=1))
    stacked = jnp.concatenate(pieces, axis=0)
    m = jnp.dot(stacked, w9_ref[...], preferred_element_type=jnp.float32)
    return jnp.maximum(m, 0.0).astype(jnp.bfloat16)


def _edges_two_kernel(above_ref, xp_ref, below_ref, w9_ref, edge_ref):
    frames = xp_ref.shape[0]
    plane = edge_ref.shape[1]
    m = _middle_two(
        [_slab_two(above_ref, xp_ref, below_ref, 0), _slab_two(above_ref, xp_ref, below_ref, frames - 1)], w9_ref
    )
    edge_ref[0] = m[:plane]
    edge_ref[1] = m[plane:]


def _finish(s, xp_ref, t, out_ref, slot):
    rows, width = xp_ref.shape[1], xp_ref.shape[2]
    for i in range(rows):
        v = s[i * width : (i + 1) * width] + xp_ref[t, i].astype(jnp.float32)
        out_ref[slot, i] = jnp.maximum(v, 0.0).astype(out_ref.dtype)


def _inner_two_kernel(above_ref, xp_ref, below_ref, w9_ref, t3_ref, out_ref, side_ref, mid_ref):
    frames = xp_ref.shape[0]
    plane = mid_ref.shape[1]

    group = 8 if frames % 8 == 0 else 2

    def middle(g, carry):
        f = group * g
        m = _middle_two([_slab_two(above_ref, xp_ref, below_ref, f + k) for k in range(group)], w9_ref)
        for k in range(group):
            mid_ref[f + k] = m[k * plane : (k + 1) * plane]
        return carry

    lax.fori_loop(0, frames // group, middle, 0)
    side_ref[0] = mid_ref[1]
    side_ref[1] = mid_ref[frames - 2]

    def run(t, count):
        s = None
        for k in range(3):
            rows = jnp.concatenate([mid_ref[t - 1 + k + j] for j in range(count)], axis=0)
            d = jnp.dot(rows, t3_ref[k], preferred_element_type=jnp.float32)
            s = d if s is None else s + d
        for j in range(count):
            _finish(s[j * plane : (j + 1) * plane], xp_ref, t + j, out_ref, t + j - 1)

    def section(g, carry):
        run(4 * g + 1, 4)
        return carry

    lax.fori_loop(0, (frames - 2) // 4, section, 0)
    left = (frames - 2) % 4
    if left:
        run(frames - 1 - left, left)


def _outer_two_kernel(xp_ref, t3_ref, before_ref, after_ref, edge_ref, side_ref, out_ref):
    frames = xp_ref.shape[0]
    s = jnp.dot(before_ref[0], t3_ref[0], preferred_element_type=jnp.float32)
    s = s + jnp.dot(edge_ref[0], t3_ref[1], preferred_element_type=jnp.float32)
    s = s + jnp.dot(side_ref[0], t3_ref[2], preferred_element_type=jnp.float32)
    _finish(s, xp_ref, 0, out_ref, 0)
    s = jnp.dot(side_ref[1], t3_ref[0], preferred_element_type=jnp.float32)
    s = s + jnp.dot(edge_ref[1], t3_ref[1], preferred_element_type=jnp.float32)
    s = s + jnp.dot(after_ref[0], t3_ref[2], preferred_element_type=jnp.float32)
    _finish(s, xp_ref, frames - 1, out_ref, 1)


def block_two(above, rowed, below, spatial_kernel, temporal_kernel):
    frames, rows, width, channels = rowed.shape
    mids = spatial_kernel.shape[2]
    w9 = jnp.transpose(spatial_kernel, (0, 1, 3, 2)).reshape(9 * channels, mids)
    t3 = jnp.transpose(temporal_kernel, (0, 2, 1))
    vmem = pltpu.MemorySpace.VMEM if hasattr(pltpu, "MemorySpace") else pltpu.VMEM
    params = pltpu.CompilerParams(vmem_limit_bytes=48 * 1024 * 1024)
    spec = pl.BlockSpec(memory_space=vmem)
    plane = (rows * width, mids)
    edges = pl.pallas_call(
        _edges_two_kernel,
        out_shape=jax.ShapeDtypeStruct((2,) + plane, rowed.dtype),
        in_specs=[spec] * 4,
        out_specs=spec,
        compiler_params=params,
        cost_estimate=pl.CostEstimate(
            flops=2 * 2 * rows * width * 9 * channels * mids, bytes_accessed=2 * rowed.size, transcendentals=0
        ),
    )(above, rowed, below, w9)
    before = from_behind(edges[1:], "tm", 1)
    after = from_behind(edges[:1], "tm", -1)
    inner, side = pl.pallas_call(
        _inner_two_kernel,
        out_shape=(
            jax.ShapeDtypeStruct((frames - 2, rows, width, channels), rowed.dtype),
            jax.ShapeDtypeStruct((2,) + plane, rowed.dtype),
        ),
        in_specs=[spec] * 5,
        out_specs=(spec, spec),
        scratch_shapes=[pltpu.VMEM((frames,) + plane, jnp.bfloat16)],
        compiler_params=params,
        cost_estimate=pl.CostEstimate(
            flops=2 * frames * rows * width * (9 * channels * mids + 3 * mids * channels),
            bytes_accessed=4 * rowed.size,
            transcendentals=0,
        ),
    )(above, rowed, below, w9, t3)
    outer = pl.pallas_call(
        _outer_two_kernel,
        out_shape=jax.ShapeDtypeStruct((2, rows, width, channels), rowed.dtype),
        in_specs=[spec] * 6,
        out_specs=spec,
        compiler_params=params,
    )(rowed, t3, before, after, edges, side)
    return jnp.concatenate([outer[:1], inner, outer[1:]], axis=0)


def _copy_kernel(top_ref, bottom_ref, top_out, bottom_out):
    top_out[...] = top_ref[...]
    bottom_out[...] = bottom_ref[...]


def edge_rows(block, top, bottom):
    frames, rows, channels, width = block.shape
    top_spec = pl.BlockSpec((frames, top, channels, width), lambda i: (0, rows // top - 1, 0, 0))
    bottom_spec = pl.BlockSpec((frames, bottom, channels, width), lambda i: (0, 0, 0, 0))
    return pl.pallas_call(
        _copy_kernel,
        grid=(1,),
        out_shape=(
            jax.ShapeDtypeStruct((frames, top, channels, width), block.dtype),
            jax.ShapeDtypeStruct((frames, bottom, channels, width), block.dtype),
        ),
        in_specs=[top_spec, bottom_spec],
        out_specs=(pl.BlockSpec((frames, top, channels, width), lambda i: (0, 0, 0, 0)), bottom_spec),
    )(block, block)


def on_device(video_clip, spatial_one, temporal_one, down_weight, spatial_two, temporal_two):
    rows = video_clip.shape[1]
    top, bottom = edge_rows(video_clip, 2, 1)
    above = from_behind(top, "row", 1)
    below = from_behind(bottom, "row", -1)
    keep_first = (lax.axis_index("row") > 0).astype(jnp.int32).reshape(1)
    reduced = block_one(above, video_clip, below, keep_first, spatial_one, temporal_one, down_weight)
    rows = reduced.shape[1]
    above = from_behind(reduced[:, rows - 1 :], "row", 1)
    below = from_behind(reduced[:, :1], "row", -1)
    return block_two(above, reduced, below, spatial_two, temporal_two)


def solution(mesh):
    placed = (P("tm", "row", None, None), P(), P(), P(), P(), P())
    return jax.shard_map(
        on_device, mesh=mesh, in_specs=placed, out_specs=P("tm", "row", None, None), check_vma=False
    )
```
